32 devices in a mesh: groups: 2 (over x), frame: 16 (over z, y, core).
Axes of the slice: x: 2, y: 2, z: 4, core: 2. Of those that a mesh axis runs over, the one named last changes fastest.
Arguments:
- latents: bfloat16 [32, 72, 32, 320], P(('groups', 'frame')), parts along dimension 0, may hold values from -30 to 30
- conv1_weight: bfloat16 [3, 3, 320, 320], replicated, may hold values from -0.109375 to 0.109375
- qkv_weight: bfloat16 [320, 960], replicated, may hold values from -0.3125 to 0.3125
- out_weight: bfloat16 [320, 320], replicated, may hold values from -0.3125 to 0.3125
- pos_bias: float32 [5, 4, 4], replicated, may hold values from -4 to 305
- conv2_weight: bfloat16 [3, 3, 320, 320], replicated, may hold values from -0.109375 to 0.109375
Outputs:
- denoised: bfloat16 [32, 72, 32, 320], P(('groups', 'frame')), parts along dimension 0
The draws below stay inside these ranges and needn't reach their ends.
There are 2 independent parts, one for each index of `groups`. The reference program is written for one: setup_inputs(seed, part) draws one part's arguments, and reference() takes and returns one part's arrays. A program takes and returns all parts, laid end to end along the dimension named above; an argument that names none is the same for every part. Nothing has to cross between parts.
All inputs are finite; a program needn't handle non-finite values.
Results may differ from the reference program's by a relative error of at most 0.01.
Values may be sent and summed in bfloat16 or wider, within the bound.
No kernel may reach another device: no remote copies, remote signals or barrier semaphores. Data moves between devices by JAX's collectives and lax.ppermute only.
A program may use at most 128 MiB of HBM per device.

```python
import math
import jax
import jax.numpy as jnp
from jax import lax

C = 320
HEADS = 5
ROWS = 72
COLS = 128
QCOLS = 32
FRAMES = 4
TILES = 16


def draw_latents(key, part):
    key_base, key_chan, key_pix = jax.random.split(key, 3)
    dims_out = (TILES, ROWS, QCOLS, C)
    chan_scale = jnp.exp(jax.random.uniform(key_chan, (C,), jnp.float32, 0.0, math.log(10.0)))
    pix_scale = jnp.exp(jax.random.uniform(key_pix, (TILES, ROWS, QCOLS, 1), jnp.float32, 0.0, math.log(10.0)))
    base_draw = jax.random.truncated_normal(key_base, -3.0, 3.0, dims_out, jnp.float32)
    return (0.1 * base_draw * chan_scale * pix_scale).astype(jnp.bfloat16)


def draw_pos_bias(key, part):
    key_base = jax.random.fold_in(key, 0)
    dims_out = (HEADS, FRAMES, FRAMES)
    return jax.random.truncated_normal(key_base, -4.0, 4.0, dims_out, jnp.float32)


def scatter_about(own_key, extent, scale, limit, kind=jnp.bfloat16):
    entries = scale * jax.random.normal(own_key, extent, jnp.float32)
    return jnp.clip(entries, min=-limit, max=limit).astype(kind)


def setup_inputs(seed: int = 0, part: int = 0) -> dict:
    streams_of = jax.random.split(jax.random.key(seed), 7)
    part_keys = jax.random.split(jax.random.fold_in(streams_of[6], part), 7)
    return {
        "latents": draw_latents(jax.random.fold_in(jax.random.fold_in(streams_of[6], part), 71), part),
        "conv1_weight": scatter_about(streams_of[1], (3, 3, C, C), (9 * C) ** -0.5, 0.109375),
        "qkv_weight": scatter_about(streams_of[2], (C, 3 * C), C ** -0.5, 0.3125),
        "out_weight": scatter_about(streams_of[3], (C, C), C ** -0.5, 0.3125),
        "pos_bias": draw_pos_bias(jax.random.fold_in(streams_of[6], 71), part),
        "conv2_weight": scatter_about(streams_of[5], (3, 3, C, C), (9 * C) ** -0.5, 0.109375),
    }


def to_video(tiles):
    shaped = tiles.reshape(4, FRAMES, ROWS, QCOLS, C)
    return shaped.transpose(1, 2, 0, 3, 4).reshape(FRAMES, ROWS, COLS, C)

def to_tiles(video):
    shaped = video.reshape(FRAMES, ROWS, 4, QCOLS, C)
    return shaped.transpose(2, 0, 1, 3, 4).reshape(TILES, ROWS, QCOLS, C)

def convolve(field_in, weight):
    return lax.conv_general_dilated(field_in.astype(jnp.float32), weight.astype(jnp.float32), (1, 1), ((1, 1), (1, 1)), dimension_numbers=('NHWC', 'HWIO', 'NHWC'), precision=lax.Precision.HIGHEST)

def reference(latents, conv1_weight, qkv_weight, out_weight, pos_bias, conv2_weight):
    video = to_video(latents)
    first = convolve(video, conv1_weight)
    normed = first * lax.rsqrt(lax.optimization_barrier(jnp.mean(first * first, axis=-1, keepdims=True)) + 1e-06)
    hidden = jax.nn.gelu(normed, approximate=True).astype(jnp.bfloat16)
    qkv_all = jnp.dot(hidden, qkv_weight, preferred_element_type=jnp.float32).astype(jnp.bfloat16)
    head_dim = C // HEADS
    split = qkv_all.reshape(FRAMES, ROWS * COLS, 3, HEADS, head_dim).astype(jnp.float32)
    queries = split[:, :, 0]
    key_part = split[:, :, 1]
    value_part = split[:, :, 2]
    scores = jnp.einsum('fphd,gphd->phfg', queries, key_part) * head_dim ** (-0.5) + pos_bias[None]
    scores = scores - lax.optimization_barrier(jnp.max(scores, axis=-1, keepdims=True))
    attn_p = jnp.exp(scores)
    attn_p = (attn_p / lax.optimization_barrier(jnp.sum(attn_p, axis=-1, keepdims=True))).astype(jnp.bfloat16)
    blended = jnp.einsum('phfg,gphd->fphd', attn_p.astype(jnp.float32), value_part)
    blended = blended.astype(jnp.bfloat16).reshape(FRAMES, ROWS, COLS, C)
    projected = jnp.dot(blended, out_weight, preferred_element_type=jnp.float32).astype(jnp.bfloat16)
    joined = (hidden.astype(jnp.float32) + projected.astype(jnp.float32)).astype(jnp.bfloat16)
    second = convolve(joined, conv2_weight).astype(jnp.bfloat16)
    return to_tiles(second)
```

```python
import jax
import jax.numpy as jnp
from jax import lax
from jax.sharding import Mesh, PartitionSpec as P

HEADS = 5


def shifted(block, axis, distance):
    devices = range(lax.axis_size(axis))
    route = [(i - distance, i) for i in devices if i - distance in devices]
    return lax.ppermute(block, axis, route)


def convolve(field_in, weight):
    left_rim = shifted(field_in[:, :, -1:, :], "quarter", 1)
    right_rim = shifted(field_in[:, :, :1, :], "quarter", -1)
    widened = jnp.concatenate([left_rim, field_in, right_rim], axis=2)
    return lax.conv_general_dilated(
        widened,
        weight,
        (1, 1),
        ((1, 1), (0, 0)),
        dimension_numbers=("NHWC", "HWIO", "NHWC"),
        preferred_element_type=jnp.float32,
    )


def attend(grid, qkv_weight, pos_bias, out_weight):
    frames_all, count, channels = grid.shape
    head_dim = channels // HEADS
    qkv = jnp.dot(
        grid.reshape(frames_all * count, channels), qkv_weight, preferred_element_type=jnp.float32
    ).astype(jnp.bfloat16)
    split = qkv.reshape(frames_all, count, 3, HEADS, head_dim)
    queries = split[:, :, 0]
    key_part = split[:, :, 1]
    value_part = split[:, :, 2]
    scores = jnp.einsum("fnhd,gnhd->nhfg", queries, key_part, preferred_element_type=jnp.float32)
    scores = scores * head_dim ** (-0.5) + pos_bias[None]
    scores = scores - jnp.max(scores, axis=-1, keepdims=True)
    attn_p = jnp.exp(scores)
    attn_p = (attn_p / jnp.sum(attn_p, axis=-1, keepdims=True)).astype(jnp.bfloat16)
    blended = jnp.einsum("nhfg,gnhd->fnhd", attn_p, value_part, preferred_element_type=jnp.float32)
    blended = blended.astype(jnp.bfloat16).reshape(frames_all * count, channels)
    projected = jnp.dot(blended, out_weight, preferred_element_type=jnp.float32).astype(jnp.bfloat16)
    return projected.reshape(frames_all, count, channels)


def body(latents, conv1_weight, qkv_weight, out_weight, pos_bias, conv2_weight):
    frames_dev, row_count, col_count, channels = latents.shape
    frames_all = lax.axis_size("frame")
    pix_piece = row_count * col_count // frames_all
    first = convolve(latents, conv1_weight)
    normed = first * lax.rsqrt(jnp.mean(first * first, axis=-1, keepdims=True) + 1e-06)
    hidden = jax.nn.gelu(normed, approximate=True).astype(jnp.bfloat16)
    pieces = lax.all_to_all(
        hidden.reshape(frames_all, pix_piece, channels), "frame", split_axis=0, concat_axis=0, tiled=True
    )
    attended = attend(pieces, qkv_weight, pos_bias, out_weight)
    returned = lax.all_to_all(attended, "frame", split_axis=0, concat_axis=0, tiled=True)
    returned = returned.reshape(frames_dev, row_count, col_count, channels)
    joined = (hidden.astype(jnp.float32) + returned.astype(jnp.float32)).astype(jnp.bfloat16)
    return convolve(joined, conv2_weight).astype(jnp.bfloat16)


def solution(mesh):
    groups = mesh.shape["groups"]
    frames_all = mesh.shape["frame"] // 4
    split_mesh = Mesh(
        mesh.devices.reshape(groups, 4, frames_all), ("groups", "quarter", "frame")
    )
    tiles = P(("groups", "quarter", "frame"), None, None, None)
    placed = (tiles, P(), P(), P(), P(), P())
    return jax.shard_map(
        body,
        mesh=split_mesh,
        in_specs=placed,
        out_specs=tiles,
        check_vma=False,
    )
```

```python
import jax
import jax.numpy as jnp
from jax import lax
from jax.experimental import pallas as pl
from jax.experimental.pallas import tpu as pltpu
from jax.sharding import Mesh, PartitionSpec as P

HEADS = 5


def shifted(block, axis, distance):
    devices = range(lax.axis_size(axis))
    route = [(i - distance, i) for i in devices if i - distance in devices]
    return lax.ppermute(block, axis, route)


def convolve(field_in, weight):
    left_rim = shifted(field_in[:, :, -1:, :], "quarter", 1)
    right_rim = shifted(field_in[:, :, :1, :], "quarter", -1)
    widened = jnp.concatenate([left_rim, field_in, right_rim], axis=2)
    return lax.conv_general_dilated(
        widened,
        weight,
        (1, 1),
        ((1, 1), (0, 0)),
        dimension_numbers=("NHWC", "HWIO", "NHWC"),
        preferred_element_type=jnp.float32,
    )


def attend_kernel(x_ref, wqkv_ref, bias_ref, wout_ref, o_ref, qkv_s, blend_s):
    frames_all, count, channels = x_ref.shape
    head_dim = channels // HEADS
    scale = head_dim ** (-0.5)
    block = min(frames_all, 4)

    def project(f, carry):
        qkv_s[f] = lax.dot_general(
            wqkv_ref[...], x_ref[f], (((1,), (1,)), ((), ())), preferred_element_type=jnp.float32
        ).astype(jnp.bfloat16)
        return carry

    lax.fori_loop(0, frames_all, project, 0, unroll=frames_all <= 4)

    def head_block(h, first):
        frames = pl.ds(first, block)
        queries = qkv_s[frames, pl.ds(h * head_dim, head_dim), :].astype(jnp.float32)
        scores = []
        for g in range(frames_all):
            key_part = qkv_s[g, pl.ds(channels + h * head_dim, head_dim), :].astype(jnp.float32)
            bias = bias_ref[h, g, frames]
            scores.append(jnp.sum(queries * key_part[None], axis=1) * scale + bias)
        top = scores[0]
        for g in range(1, frames_all):
            top = jnp.maximum(top, scores[g])
        weights = [jnp.exp(s - top) for s in scores]
        total = weights[0]
        for g in range(1, frames_all):
            total = total + weights[g]
        blended = None
        for g in range(frames_all):
            value_part = qkv_s[g, pl.ds(2 * channels + h * head_dim, head_dim), :].astype(jnp.float32)
            prob = (weights[g] / total).astype(jnp.bfloat16).astype(jnp.float32)
            term = prob[:, None, :] * value_part[None]
            blended = term if blended is None else blended + term
        blend_s[frames, pl.ds(h * head_dim, head_dim), :] = blended.astype(jnp.bfloat16)

    def frame_block(i, carry):
        for h in range(HEADS):
            head_block(h, i * block)
        return carry

    lax.fori_loop(0, frames_all // block, frame_block, 0, unroll=frames_all <= 4)

    def out_project(f, carry):
        o_ref[f] = jnp.dot(wout_ref[...], blend_s[f], preferred_element_type=jnp.float32).astype(
            jnp.bfloat16
        )
        return carry

    lax.fori_loop(0, frames_all, out_project, 0, unroll=frames_all <= 4)


def attend(grid, qkv_weight, pos_bias, out_weight):
    frames_all, count, channels = grid.shape
    vmem = pl.BlockSpec(memory_space=pltpu.VMEM)
    return pl.pallas_call(
        attend_kernel,
        out_shape=jax.ShapeDtypeStruct((frames_all, channels, count), jnp.bfloat16),
        in_specs=[vmem] * 4,
        out_specs=vmem,
        scratch_shapes=[
            pltpu.VMEM((frames_all, 3 * channels, count), jnp.bfloat16),
            pltpu.VMEM((frames_all, channels, count), jnp.bfloat16),
        ],
    )(grid, qkv_weight.T, pos_bias.transpose(0, 2, 1)[..., None], out_weight.T)


def body(latents, conv1_weight, qkv_weight, out_weight, pos_bias, conv2_weight):
    frames_dev, row_count, col_count, channels = latents.shape
    frames_all = lax.axis_size("frame")
    pix_piece = row_count * col_count // frames_all
    first = convolve(latents, conv1_weight)
    normed = first * lax.rsqrt(jnp.mean(first * first, axis=-1, keepdims=True) + 1e-06)
    hidden = jax.nn.gelu(normed, approximate=True).astype(jnp.bfloat16)
    pieces = lax.all_to_all(
        hidden.reshape(frames_all, pix_piece, channels), "frame", split_axis=0, concat_axis=0, tiled=True
    )
    attended = attend(pieces, qkv_weight, pos_bias, out_weight)
    returned = lax.all_to_all(attended, "frame", split_axis=0, concat_axis=0, tiled=True)
    returned = returned.transpose(0, 2, 1).reshape(frames_dev, row_count, col_count, channels)
    joined = (hidden.astype(jnp.float32) + returned.astype(jnp.float32)).astype(jnp.bfloat16)
    return convolve(joined, conv2_weight).astype(jnp.bfloat16)


def solution(mesh):
    groups = mesh.shape["groups"]
    frames_all = mesh.shape["frame"] // 4
    split_mesh = Mesh(
        mesh.devices.reshape(groups, 4, frames_all), ("groups", "quarter", "frame")
    )
    tiles = P(("groups", "quarter", "frame"), None, None, None)
    placed = (tiles, P(), P(), P(), P(), P())
    return jax.shard_map(
        body,
        mesh=split_mesh,
        in_specs=placed,
        out_specs=tiles,
        check_vma=False,
    )
```

```python
import functools

import jax
import jax.numpy as jnp
from jax import lax
from jax.experimental import pallas as pl
from jax.experimental.pallas import tpu as pltpu
from jax.sharding import Mesh, PartitionSpec as P

HEADS = 5


def shifted(block, axis, distance):
    devices = range(lax.axis_size(axis))
    route = [(i - distance, i) for i in devices if i - distance in devices]
    return lax.ppermute(block, axis, route)


def conv_kernel(*refs, parts, finish):
    sources = refs[:parts]
    left_ref, right_ref, w_ref, o_ref, side_l, side_c, side_r, shift_s = refs[parts:]
    row_count, col_count, channels = o_ref.shape
    band = 8
    span = band * col_count
    zeros = jnp.zeros((col_count, channels), jnp.bfloat16)
    for side in (side_l, side_c, side_r):
        side[pl.ds(0, col_count)] = zeros
        side[pl.ds((row_count + 1) * col_count, col_count)] = zeros
    column = lax.broadcasted_iota(jnp.int32, (band, col_count, channels), 1)

    def build(i, carry):
        r0 = i * band
        block = sources[0][pl.ds(r0, band)].astype(jnp.float32)
        for extra in sources[1:]:
            block = block + extra[pl.ds(r0, band)].astype(jnp.float32)
        block = block.astype(jnp.bfloat16)
        flat = block.astype(jnp.float32).reshape(span, channels)
        shift_s[pl.ds(8, span)] = flat
        before = shift_s[pl.ds(7, span)].reshape(band, col_count, channels)
        after = shift_s[pl.ds(9, span)].reshape(band, col_count, channels)
        rim_l = left_ref[pl.ds(r0, band)].astype(jnp.float32)[:, None, :]
        rim_r = right_ref[pl.ds(r0, band)].astype(jnp.float32)[:, None, :]
        before = jnp.where(column == 0, rim_l, before)
        after = jnp.where(column == col_count - 1, rim_r, after)
        at = pl.ds(pl.multiple_of((r0 + 1) * col_count, col_count), span)
        side_c[at] = block.reshape(span, channels)
        side_l[at] = before.reshape(span, channels).astype(jnp.bfloat16)
        side_r[at] = after.reshape(span, channels).astype(jnp.bfloat16)
        return carry

    lax.fori_loop(0, row_count // band, build, 0)

    def compute(i, carry):
        r0 = i * band
        acc = None
        for a in range(3):
            at = pl.ds(pl.multiple_of((r0 + a) * col_count, col_count), span)
            for b, side in enumerate((side_l, side_c, side_r)):
                term = jnp.dot(side[at], w_ref[a, b], preferred_element_type=jnp.float32)
                acc = term if acc is None else acc + term
        o_ref[pl.ds(r0, band)] = finish(acc).reshape(band, col_count, channels)
        return carry

    lax.fori_loop(0, row_count // band, compute, 0)


def norm_gelu(first):
    normed = first * lax.rsqrt(jnp.mean(first * first, axis=-1, keepdims=True) + 1e-06)
    return jax.nn.gelu(normed, approximate=True).astype(jnp.bfloat16)


def to_bf16(acc):
    return acc.astype(jnp.bfloat16)


def convolve(sources, edge_of, weight, finish):
    row_count, col_count, channels = sources[0].shape
    left_rim = shifted(edge_of(-1), "quarter", 1)
    right_rim = shifted(edge_of(0), "quarter", -1)
    vmem = pl.BlockSpec(memory_space=pltpu.VMEM)
    padded = (row_count + 2) * col_count
    return pl.pallas_call(
        functools.partial(conv_kernel, parts=len(sources), finish=finish),
        out_shape=jax.ShapeDtypeStruct((row_count, col_count, channels), jnp.bfloat16),
        in_specs=[vmem] * (len(sources) + 3),
        out_specs=vmem,
        scratch_shapes=[pltpu.VMEM((padded, channels), jnp.bfloat16)] * 3
        + [pltpu.VMEM((8 * col_count + 16, channels), jnp.float32)],
    )(*sources, left_rim, right_rim, weight)


def attend_kernel(x_ref, wqkv_ref, bias_ref, wout_ref, o_ref, qkv_s, blend_s):
    frames_all, count, channels = x_ref.shape
    head_dim = channels // HEADS
    scale = head_dim ** (-0.5)
    block = min(frames_all, 4)

    def project(f, carry):
        qkv_s[f] = lax.dot_general(
            wqkv_ref[...], x_ref[f], (((1,), (1,)), ((), ())), preferred_element_type=jnp.float32
        ).astype(jnp.bfloat16)
        return carry

    lax.fori_loop(0, frames_all, project, 0, unroll=frames_all <= 4)

    def head_block(h, first):
        frames = pl.ds(first, block)
        queries = qkv_s[frames, pl.ds(h * head_dim, head_dim), :].astype(jnp.float32)
        scores = []
        for g in range(frames_all):
            key_part = qkv_s[g, pl.ds(channels + h * head_dim, head_dim), :].astype(jnp.float32)
            bias = bias_ref[h, g, frames]
            scores.append(jnp.sum(queries * key_part[None], axis=1) * scale + bias)
        top = scores[0]
        for g in range(1, frames_all):
            top = jnp.maximum(top, scores[g])
        weights = [jnp.exp(s - top) for s in scores]
        total = weights[0]
        for g in range(1, frames_all):
            total = total + weights[g]
        blended = None
        for g in range(frames_all):
            value_part = qkv_s[g, pl.ds(2 * channels + h * head_dim, head_dim), :].astype(jnp.float32)
            prob = (weights[g] / total).astype(jnp.bfloat16).astype(jnp.float32)
            term = prob[:, None, :] * value_part[None]
            blended = term if blended is None else blended + term
        blend_s[frames, pl.ds(h * head_dim, head_dim), :] = blended.astype(jnp.bfloat16)

    def frame_block(i, carry):
        for h in range(HEADS):
            head_block(h, i * block)
        return carry

    lax.fori_loop(0, frames_all // block, frame_block, 0, unroll=frames_all <= 4)

    def out_project(f, carry):
        o_ref[f] = lax.dot_general(
            blend_s[f], wout_ref[...], (((0,), (0,)), ((), ())), preferred_element_type=jnp.float32
        ).astype(jnp.bfloat16)
        return carry

    lax.fori_loop(0, frames_all, out_project, 0, unroll=frames_all <= 4)


def attend(grid, qkv_weight, pos_bias, out_weight):
    frames_all, count, channels = grid.shape
    vmem = pl.BlockSpec(memory_space=pltpu.VMEM)
    return pl.pallas_call(
        attend_kernel,
        out_shape=jax.ShapeDtypeStruct((frames_all, count, channels), jnp.bfloat16),
        in_specs=[vmem] * 4,
        out_specs=vmem,
        scratch_shapes=[
            pltpu.VMEM((frames_all, 3 * channels, count), jnp.bfloat16),
            pltpu.VMEM((frames_all, channels, count), jnp.bfloat16),
        ],
    )(grid, qkv_weight.T, pos_bias.transpose(0, 2, 1)[..., None], out_weight)


def body(latents, conv1_weight, qkv_weight, out_weight, pos_bias, conv2_weight):
    frames_dev, row_count, col_count, channels = latents.shape
    frames_all = lax.axis_size("frame")
    pix_piece = row_count * col_count // frames_all
    tile = latents.reshape(row_count, col_count, channels)
    hidden = convolve([tile], lambda c: tile[:, c, :], conv1_weight, norm_gelu)
    pieces = lax.all_to_all(
        hidden.reshape(frames_all, pix_piece, channels), "frame", split_axis=0, concat_axis=0, tiled=True
    )
    attended = attend(pieces, qkv_weight, pos_bias, out_weight)
    returned = lax.all_to_all(attended, "frame", split_axis=0, concat_axis=0, tiled=True)
    returned = returned.reshape(row_count, col_count, channels)

    def joined_edge(c):
        summed = hidden[:, c, :].astype(jnp.float32) + returned[:, c, :].astype(jnp.float32)
        return summed.astype(jnp.bfloat16)

    second = convolve([hidden, returned], joined_edge, conv2_weight, to_bf16)
    return second.reshape(frames_dev, row_count, col_count, channels)


def solution(mesh):
    groups = mesh.shape["groups"]
    frames_all = mesh.shape["frame"] // 4
    split_mesh = Mesh(
        mesh.devices.reshape(groups, 4, frames_all), ("groups", "quarter", "frame")
    )
    tiles = P(("groups", "quarter", "frame"), None, None, None)
    placed = (tiles, P(), P(), P(), P(), P())
    return jax.shard_map(
        body,
        mesh=split_mesh,
        in_specs=placed,
        out_specs=tiles,
        check_vma=False,
    )
```

```python
import functools

import jax
import jax.numpy as jnp
from jax import lax
from jax.experimental import pallas as pl
from jax.experimental.pallas import tpu as pltpu
from jax.sharding import Mesh, PartitionSpec as P

HEADS = 5


def shifted(block, axis, distance):
    devices = range(lax.axis_size(axis))
    route = [(i - distance, i) for i in devices if i - distance in devices]
    return lax.ppermute(block, axis, route)


def conv_kernel(*refs, parts, finish):
    sources = refs[:parts]
    left_ref, right_ref, w_ref, o_ref, slab, shift_s = refs[parts:]
    row_count, col_count, channels = o_ref.shape
    lanes = slab.shape[1] // 3
    band = 24
    span = band * col_count
    padded_rows = slab.shape[0]
    slab[pl.ds(0, col_count)] = jnp.zeros((col_count, slab.shape[1]), jnp.bfloat16)
    slab[pl.ds(padded_rows - col_count, col_count)] = jnp.zeros((col_count, slab.shape[1]), jnp.bfloat16)
    if lanes > channels:
        pad = jnp.zeros((padded_rows, lanes - channels), jnp.bfloat16)
        for b in range(3):
            slab[:, pl.ds(b * lanes + channels, lanes - channels)] = pad
    column = lax.broadcasted_iota(jnp.int32, (band, col_count, channels), 1)

    def build(i, carry):
        r0 = i * band
        block = sources[0][pl.ds(r0, band)].astype(jnp.float32)
        for extra in sources[1:]:
            block = block + extra[pl.ds(r0, band)].astype(jnp.float32)
        block = block.astype(jnp.bfloat16)
        shift_s[pl.ds(8, span)] = block.astype(jnp.float32).reshape(span, channels)
        before = shift_s[pl.ds(7, span)].reshape(band, col_count, channels)
        after = shift_s[pl.ds(9, span)].reshape(band, col_count, channels)
        rim_l = left_ref[pl.ds(r0, band)].astype(jnp.float32)[:, None, :]
        rim_r = right_ref[pl.ds(r0, band)].astype(jnp.float32)[:, None, :]
        before = jnp.where(column == 0, rim_l, before)
        after = jnp.where(column == col_count - 1, rim_r, after)
        rows = pl.ds(pl.multiple_of((r0 + 1) * col_count, col_count), span)
        slab[rows, pl.ds(0, channels)] = before.reshape(span, channels).astype(jnp.bfloat16)
        slab[rows, pl.ds(lanes, channels)] = block.reshape(span, channels)
        slab[rows, pl.ds(2 * lanes, channels)] = after.reshape(span, channels).astype(jnp.bfloat16)
        return carry

    lax.fori_loop(0, row_count // band, build, 0)

    def compute(i, carry):
        r0 = i * band
        acc = None
        for a in range(3):
            rows = pl.ds(pl.multiple_of((r0 + a) * col_count, col_count), span)
            term = jnp.dot(slab[rows, :], w_ref[a], preferred_element_type=jnp.float32)
            acc = term if acc is None else acc + term
        o_ref[pl.ds(r0, band)] = finish(acc).reshape(band, col_count, channels)
        return carry

    lax.fori_loop(0, row_count // band, compute, 0)


def norm_gelu(first):
    normed = first * lax.rsqrt(jnp.mean(first * first, axis=-1, keepdims=True) + 1e-06)
    return jax.nn.gelu(normed, approximate=True).astype(jnp.bfloat16)


def to_bf16(acc):
    return acc.astype(jnp.bfloat16)


def convolve(sources, edge_of, weight, finish):
    row_count, col_count, channels = sources[0].shape
    left_rim = shifted(edge_of(-1), "quarter", 1)
    right_rim = shifted(edge_of(0), "quarter", -1)
    vmem = pl.BlockSpec(memory_space=pltpu.VMEM)
    padded = (row_count + 2) * col_count
    lanes = -(-channels // 128) * 128
    stacked = jnp.pad(weight, ((0, 0), (0, 0), (0, lanes - channels), (0, 0)))
    stacked = stacked.reshape(3, 3 * lanes, channels)
    return pl.pallas_call(
        functools.partial(conv_kernel, parts=len(sources), finish=finish),
        out_shape=jax.ShapeDtypeStruct((row_count, col_count, channels), jnp.bfloat16),
        in_specs=[vmem] * (len(sources) + 3),
        out_specs=vmem,
        scratch_shapes=[
            pltpu.VMEM((padded, 3 * lanes), jnp.bfloat16),
            pltpu.VMEM((24 * col_count + 16, channels), jnp.float32),
        ],
    )(*sources, left_rim, right_rim, stacked)


def attend_kernel(x_ref, wqkv_ref, bias_ref, wout_ref, o_ref, qkv_s, blend_s):
    frames_all, count, channels = x_ref.shape
    head_dim = channels // HEADS
    scale = head_dim ** (-0.5)
    block = min(frames_all, 4)

    def project(f, carry):
        qkv_s[f] = lax.dot_general(
            wqkv_ref[...], x_ref[f], (((1,), (1,)), ((), ())), preferred_element_type=jnp.float32
        ).astype(jnp.bfloat16)
        return carry

    lax.fori_loop(0, frames_all, project, 0, unroll=frames_all <= 4)

    def head_block(h, first):
        frames = pl.ds(first, block)
        queries = qkv_s[frames, pl.ds(h * head_dim, head_dim), :].astype(jnp.float32)
        scores = []
        for g in range(frames_all):
            key_part = qkv_s[g, pl.ds(channels + h * head_dim, head_dim), :].astype(jnp.float32)
            bias = bias_ref[h, g, frames]
            scores.append(jnp.sum(queries * key_part[None], axis=1) * scale + bias)
        top = scores[0]
        for g in range(1, frames_all):
            top = jnp.maximum(top, scores[g])
        weights = [jnp.exp(s - top) for s in scores]
        total = weights[0]
        for g in range(1, frames_all):
            total = total + weights[g]
        blended = None
        for g in range(frames_all):
            value_part = qkv_s[g, pl.ds(2 * channels + h * head_dim, head_dim), :].astype(jnp.float32)
            prob = (weights[g] / total).astype(jnp.bfloat16).astype(jnp.float32)
            term = prob[:, None, :] * value_part[None]
            blended = term if blended is None else blended + term
        blend_s[frames, pl.ds(h * head_dim, head_dim), :] = blended.astype(jnp.bfloat16)

    def frame_block(i, carry):
        for h in range(HEADS):
            head_block(h, i * block)
        return carry

    lax.fori_loop(0, frames_all // block, frame_block, 0, unroll=frames_all <= 4)

    def out_project(f, carry):
        o_ref[f] = lax.dot_general(
            blend_s[f], wout_ref[...], (((0,), (0,)), ((), ())), preferred_element_type=jnp.float32
        ).astype(jnp.bfloat16)
        return carry

    lax.fori_loop(0, frames_all, out_project, 0, unroll=frames_all <= 4)


def attend(grid, qkv_weight, pos_bias, out_weight):
    frames_all, count, channels = grid.shape
    vmem = pl.BlockSpec(memory_space=pltpu.VMEM)
    return pl.pallas_call(
        attend_kernel,
        out_shape=jax.ShapeDtypeStruct((frames_all, count, channels), jnp.bfloat16),
        in_specs=[vmem] * 4,
        out_specs=vmem,
        scratch_shapes=[
            pltpu.VMEM((frames_all, 3 * channels, count), jnp.bfloat16),
            pltpu.VMEM((frames_all, channels, count), jnp.bfloat16),
        ],
    )(grid, qkv_weight.T, pos_bias.transpose(0, 2, 1)[..., None], out_weight)


def body(latents, conv1_weight, qkv_weight, out_weight, pos_bias, conv2_weight):
    frames_dev, row_count, col_count, channels = latents.shape
    frames_all = lax.axis_size("frame")
    pix_piece = row_count * col_count // frames_all
    tile = latents.reshape(row_count, col_count, channels)
    hidden = convolve([tile], lambda c: tile[:, c, :], conv1_weight, norm_gelu)
    pieces = lax.all_to_all(
        hidden.reshape(frames_all, pix_piece, channels), "frame", split_axis=0, concat_axis=0, tiled=True
    )
    attended = attend(pieces, qkv_weight, pos_bias, out_weight)
    returned = lax.all_to_all(attended, "frame", split_axis=0, concat_axis=0, tiled=True)
    returned = returned.reshape(row_count, col_count, channels)

    def joined_edge(c):
        summed = hidden[:, c, :].astype(jnp.float32) + returned[:, c, :].astype(jnp.float32)
        return summed.astype(jnp.bfloat16)

    second = convolve([hidden, returned], joined_edge, conv2_weight, to_bf16)
    return second.reshape(frames_dev, row_count, col_count, channels)


def solution(mesh):
    groups = mesh.shape["groups"]
    frames_all = mesh.shape["frame"] // 4
    split_mesh = Mesh(
        mesh.devices.reshape(groups, 4, frames_all), ("groups", "quarter", "frame")
    )
    tiles = P(("groups", "quarter", "frame"), None, None, None)
    placed = (tiles, P(), P(), P(), P(), P())
    return jax.shard_map(
        body,
        mesh=split_mesh,
        in_specs=placed,
        out_specs=tiles,
        check_vma=False,
    )
```

```python
import functools

import jax
import jax.numpy as jnp
from jax import lax
from jax.experimental import pallas as pl
from jax.experimental.pallas import tpu as pltpu
from jax.sharding import Mesh, PartitionSpec as P

HEADS = 5


def shifted(block, axis, distance):
    devices = range(lax.axis_size(axis))
    route = [(i - distance, i) for i in devices if i - distance in devices]
    return lax.ppermute(block, axis, route)


def conv_kernel(*refs, parts, finish):
    sources = refs[:parts]
    left_ref, right_ref, w_ref, o_ref, slab, shift_s = refs[parts:]
    row_count, col_count, channels = o_ref.shape
    lanes = slab.shape[1] // 3
    band = 24
    span = band * col_count
    padded_rows = slab.shape[0]
    slab[pl.ds(0, col_count)] = jnp.zeros((col_count, slab.shape[1]), jnp.bfloat16)
    slab[pl.ds(padded_rows - col_count, col_count)] = jnp.zeros((col_count, slab.shape[1]), jnp.bfloat16)
    if lanes > channels:
        pad = jnp.zeros((padded_rows, lanes - channels), jnp.bfloat16)
        for b in range(3):
            slab[:, pl.ds(b * lanes + channels, lanes - channels)] = pad
    column = lax.broadcasted_iota(jnp.int32, (band, col_count, channels), 1)

    def build(i, carry):
        r0 = i * band
        block = sources[0][pl.ds(r0, band)].astype(jnp.float32)
        for extra in sources[1:]:
            block = block + extra[pl.ds(r0, band)].astype(jnp.float32)
        block = block.astype(jnp.bfloat16)
        shift_s[pl.ds(8, span)] = block.astype(jnp.float32).reshape(span, channels)
        before = shift_s[pl.ds(7, span)].reshape(band, col_count, channels)
        after = shift_s[pl.ds(9, span)].reshape(band, col_count, channels)
        rim_l = left_ref[pl.ds(r0, band)].astype(jnp.float32)[:, None, :]
        rim_r = right_ref[pl.ds(r0, band)].astype(jnp.float32)[:, None, :]
        before = jnp.where(column == 0, rim_l, before)
        after = jnp.where(column == col_count - 1, rim_r, after)
        rows = pl.ds(pl.multiple_of((r0 + 1) * col_count, col_count), span)
        slab[rows, pl.ds(0, channels)] = before.reshape(span, channels).astype(jnp.bfloat16)
        slab[rows, pl.ds(lanes, channels)] = block.reshape(span, channels)
        slab[rows, pl.ds(2 * lanes, channels)] = after.reshape(span, channels).astype(jnp.bfloat16)
        return carry

    lax.fori_loop(0, row_count // band, build, 0)

    def compute(i, carry):
        r0 = i * band
        acc = None
        for a in range(3):
            rows = pl.ds(pl.multiple_of((r0 + a) * col_count, col_count), span)
            term = jnp.dot(slab[rows, :], w_ref[a], preferred_element_type=jnp.float32)
            acc = term if acc is None else acc + term
        o_ref[pl.ds(r0, band)] = finish(acc).reshape(band, col_count, channels)
        return carry

    lax.fori_loop(0, row_count // band, compute, 0)


def norm_gelu(first):
    normed = first * lax.rsqrt(jnp.mean(first * first, axis=-1, keepdims=True) + 1e-06)
    return jax.nn.gelu(normed, approximate=True).astype(jnp.bfloat16)


def to_bf16(acc):
    return acc.astype(jnp.bfloat16)


def convolve(sources, edge_of, weight, finish):
    row_count, col_count, channels = sources[0].shape
    left_rim = shifted(edge_of(-1), "quarter", 1)
    right_rim = shifted(edge_of(0), "quarter", -1)
    vmem = pl.BlockSpec(memory_space=pltpu.VMEM)
    padded = (row_count + 2) * col_count
    lanes = channels
    stacked = weight.reshape(3, 3 * lanes, channels)
    return pl.pallas_call(
        functools.partial(conv_kernel, parts=len(sources), finish=finish),
        out_shape=jax.ShapeDtypeStruct((row_count, col_count, channels), jnp.bfloat16),
        in_specs=[vmem] * (len(sources) + 3),
        out_specs=vmem,
        scratch_shapes=[
            pltpu.VMEM((padded, 3 * lanes), jnp.bfloat16),
            pltpu.VMEM((24 * col_count + 16, channels), jnp.float32),
        ],
    )(*sources, left_rim, right_rim, stacked)


def attend_kernel(x_ref, wqkv_ref, bias_ref, wout_ref, o_ref, qkv_s, blend_s):
    frames_all, count, channels = x_ref.shape
    head_dim = channels // HEADS
    scale = head_dim ** (-0.5)
    block = min(frames_all, 4)

    def project(f, carry):
        qkv_s[f] = lax.dot_general(
            wqkv_ref[...], x_ref[f], (((1,), (1,)), ((), ())), preferred_element_type=jnp.float32
        ).astype(jnp.bfloat16)
        return carry

    lax.fori_loop(0, frames_all, project, 0, unroll=frames_all <= 4)

    def head_block(h, first):
        frames = pl.ds(first, block)
        queries = qkv_s[frames, pl.ds(h * head_dim, head_dim), :].astype(jnp.float32)
        scores = []
        for g in range(frames_all):
            key_part = qkv_s[g, pl.ds(channels + h * head_dim, head_dim), :].astype(jnp.float32)
            bias = bias_ref[h, g, frames]
            scores.append(jnp.sum(queries * key_part[None], axis=1) * scale + bias)
        top = scores[0]
        for g in range(1, frames_all):
            top = jnp.maximum(top, scores[g])
        weights = [jnp.exp(s - top) for s in scores]
        total = weights[0]
        for g in range(1, frames_all):
            total = total + weights[g]
        blended = None
        for g in range(frames_all):
            value_part = qkv_s[g, pl.ds(2 * channels + h * head_dim, head_dim), :].astype(jnp.float32)
            prob = (weights[g] / total).astype(jnp.bfloat16).astype(jnp.float32)
            term = prob[:, None, :] * value_part[None]
            blended = term if blended is None else blended + term
        blend_s[frames, pl.ds(h * head_dim, head_dim), :] = blended.astype(jnp.bfloat16)

    def frame_block(i, carry):
        for h in range(HEADS):
            head_block(h, i * block)
        return carry

    lax.fori_loop(0, frames_all // block, frame_block, 0, unroll=frames_all <= 4)

    def out_project(f, carry):
        o_ref[f] = lax.dot_general(
            blend_s[f], wout_ref[...], (((0,), (0,)), ((), ())), preferred_element_type=jnp.float32
        ).astype(jnp.bfloat16)
        return carry

    lax.fori_loop(0, frames_all, out_project, 0, unroll=frames_all <= 4)


def attend(grid, qkv_weight, pos_bias, out_weight):
    frames_all, count, channels = grid.shape
    vmem = pl.BlockSpec(memory_space=pltpu.VMEM)
    return pl.pallas_call(
        attend_kernel,
        out_shape=jax.ShapeDtypeStruct((frames_all, count, channels), jnp.bfloat16),
        in_specs=[vmem] * 4,
        out_specs=vmem,
        scratch_shapes=[
            pltpu.VMEM((frames_all, 3 * channels, count), jnp.bfloat16),
            pltpu.VMEM((frames_all, channels, count), jnp.bfloat16),
        ],
    )(grid, qkv_weight.T, pos_bias.transpose(0, 2, 1)[..., None], out_weight)


def body(latents, conv1_weight, qkv_weight, out_weight, pos_bias, conv2_weight):
    frames_dev, row_count, col_count, channels = latents.shape
    frames_all = lax.axis_size("frame")
    pix_piece = row_count * col_count // frames_all
    tile = latents.reshape(row_count, col_count, channels)
    hidden = convolve([tile], lambda c: tile[:, c, :], conv1_weight, norm_gelu)
    pieces = lax.all_to_all(
        hidden.reshape(frames_all, pix_piece * channels), "frame", split_axis=0, concat_axis=0, tiled=True
    )
    attended = attend(pieces.reshape(frames_all, pix_piece, channels), qkv_weight, pos_bias, out_weight)
    returned = lax.all_to_all(
        attended.reshape(frames_all, pix_piece * channels), "frame", split_axis=0, concat_axis=0, tiled=True
    )
    returned = returned.reshape(row_count, col_count, channels)

    def joined_edge(c):
        summed = hidden[:, c, :].astype(jnp.float32) + returned[:, c, :].astype(jnp.float32)
        return summed.astype(jnp.bfloat16)

    second = convolve([hidden, returned], joined_edge, conv2_weight, to_bf16)
    return second.reshape(frames_dev, row_count, col_count, channels)


def solution(mesh):
    groups = mesh.shape["groups"]
    frames_all = mesh.shape["frame"] // 4
    split_mesh = Mesh(
        mesh.devices.reshape(groups, 4, frames_all), ("groups", "quarter", "frame")
    )
    tiles = P(("groups", "quarter", "frame"), None, None, None)
    placed = (tiles, P(), P(), P(), P(), P())
    return jax.shard_map(
        body,
        mesh=split_mesh,
        in_specs=placed,
        out_specs=tiles,
        check_vma=False,
    )
```

```python
import functools

import jax
import jax.numpy as jnp
from jax import lax
from jax.experimental import pallas as pl
from jax.experimental.pallas import tpu as pltpu
from jax.sharding import Mesh, PartitionSpec as P

HEADS = 5


def shifted(block, axis, distance):
    devices = range(lax.axis_size(axis))
    route = [(i - distance, i) for i in devices if i - distance in devices]
    return lax.ppermute(block, axis, route)


def conv_kernel(*refs, parts, finish):
    sources = refs[:parts]
    left_ref, right_ref, w_ref, o_ref, slab, shift_s = refs[parts:]
    row_count, col_count, channels = o_ref.shape
    lanes = slab.shape[1] // 3
    band = 24
    span = band * col_count
    padded_rows = slab.shape[0]
    slab[pl.ds(0, col_count)] = jnp.zeros((col_count, slab.shape[1]), jnp.bfloat16)
    slab[pl.ds(padded_rows - col_count, col_count)] = jnp.zeros((col_count, slab.shape[1]), jnp.bfloat16)
    if lanes > channels:
        pad = jnp.zeros((padded_rows, lanes - channels), jnp.bfloat16)
        for b in range(3):
            slab[:, pl.ds(b * lanes + channels, lanes - channels)] = pad
    column = lax.broadcasted_iota(jnp.int32, (band, col_count, channels), 1)

    def build(i, carry):
        r0 = i * band
        block = sources[0][pl.ds(r0, band)].astype(jnp.float32)
        for extra in sources[1:]:
            block = block + extra[pl.ds(r0, band)].astype(jnp.float32)
        block = block.astype(jnp.bfloat16)
        shift_s[pl.ds(8, span)] = block.astype(jnp.float32).reshape(span, channels)
        before = shift_s[pl.ds(7, span)].reshape(band, col_count, channels)
        after = shift_s[pl.ds(9, span)].reshape(band, col_count, channels)
        rim_l = left_ref[pl.ds(r0, band)].astype(jnp.float32)[:, None, :]
        rim_r = right_ref[pl.ds(r0, band)].astype(jnp.float32)[:, None, :]
        before = jnp.where(column == 0, rim_l, before)
        after = jnp.where(column == col_count - 1, rim_r, after)
        rows = pl.ds(pl.multiple_of((r0 + 1) * col_count, col_count), span)
        slab[rows, pl.ds(0, channels)] = before.reshape(span, channels).astype(jnp.bfloat16)
        slab[rows, pl.ds(lanes, channels)] = block.reshape(span, channels)
        slab[rows, pl.ds(2 * lanes, channels)] = after.reshape(span, channels).astype(jnp.bfloat16)
        return carry

    lax.fori_loop(0, row_count // band, build, 0)

    def compute(i, carry):
        r0 = i * band
        acc = None
        for a in range(3):
            rows = pl.ds(pl.multiple_of((r0 + a) * col_count, col_count), span)
            term = jnp.dot(slab[rows, :], w_ref[a], preferred_element_type=jnp.float32)
            acc = term if acc is None else acc + term
        o_ref[pl.ds(r0, band)] = finish(acc).reshape(band, col_count, channels)
        return carry

    lax.fori_loop(0, row_count // band, compute, 0)


def norm_gelu(first):
    normed = first * lax.rsqrt(jnp.mean(first * first, axis=-1, keepdims=True) + 1e-06)
    return jax.nn.gelu(normed, approximate=True).astype(jnp.bfloat16)


def to_bf16(acc):
    return acc.astype(jnp.bfloat16)


def convolve(sources, edge_of, weight, finish):
    row_count, col_count, channels = sources[0].shape
    left_rim = shifted(edge_of(-1), "quarter", 1)
    right_rim = shifted(edge_of(0), "quarter", -1)
    vmem = pl.BlockSpec(memory_space=pltpu.VMEM)
    padded = (row_count + 2) * col_count
    lanes = channels
    stacked = weight.reshape(3, 3 * lanes, channels)
    return pl.pallas_call(
        functools.partial(conv_kernel, parts=len(sources), finish=finish),
        out_shape=jax.ShapeDtypeStruct((row_count, col_count, channels), jnp.bfloat16),
        in_specs=[vmem] * (len(sources) + 3),
        out_specs=vmem,
        scratch_shapes=[
            pltpu.VMEM((padded, 3 * lanes), jnp.bfloat16),
            pltpu.VMEM((24 * col_count + 16, channels), jnp.float32),
        ],
    )(*sources, left_rim, right_rim, stacked)


def attend_kernel(x_ref, wqkv_ref, bias_ref, wout_ref, o_ref, qkv_s, blend_s):
    frames_all, count, channels = x_ref.shape
    head_dim = channels // HEADS
    scale = head_dim ** (-0.5)
    block = min(frames_all, 4)

    def project(f, carry):
        qkv_s[f] = lax.dot_general(
            wqkv_ref[...], x_ref[f], (((1,), (1,)), ((), ())), preferred_element_type=jnp.float32
        ).astype(jnp.bfloat16)
        return carry

    lax.fori_loop(0, frames_all, project, 0, unroll=frames_all <= 4)

    def head_block(h, first):
        frames = pl.ds(first, block)
        queries = qkv_s[frames, pl.ds(h * head_dim, head_dim), :].astype(jnp.float32)
        scores = []
        for g in range(frames_all):
            key_part = qkv_s[g, pl.ds(channels + h * head_dim, head_dim), :].astype(jnp.float32)
            bias = bias_ref[h, g, frames]
            scores.append(jnp.sum(queries * key_part[None], axis=1) * scale + bias)
        top = scores[0]
        for g in range(1, frames_all):
            top = jnp.maximum(top, scores[g])
        weights = [jnp.exp(s - top) for s in scores]
        total = weights[0]
        for g in range(1, frames_all):
            total = total + weights[g]
        blended = None
        for g in range(frames_all):
            value_part = qkv_s[g, pl.ds(2 * channels + h * head_dim, head_dim), :].astype(jnp.float32)
            prob = (weights[g] / total).astype(jnp.bfloat16).astype(jnp.float32)
            term = prob[:, None, :] * value_part[None]
            blended = term if blended is None else blended + term
        blend_s[frames, pl.ds(h * head_dim, head_dim), :] = blended.astype(jnp.bfloat16)

    def frame_block(i, carry):
        for h in range(HEADS):
            head_block(h, i * block)
        return carry

    lax.fori_loop(0, frames_all // block, frame_block, 0, unroll=frames_all <= 4)

    def out_project(f, carry):
        o_ref[f] = lax.dot_general(
            blend_s[f], wout_ref[...], (((0,), (0,)), ((), ())), preferred_element_type=jnp.float32
        ).astype(jnp.bfloat16)
        return carry

    lax.fori_loop(0, frames_all, out_project, 0, unroll=frames_all <= 4)


def attend(grid, qkv_weight, pos_bias, out_weight):
    frames_all, count, channels = grid.shape
    vmem = pl.BlockSpec(memory_space=pltpu.VMEM)
    return pl.pallas_call(
        attend_kernel,
        out_shape=jax.ShapeDtypeStruct((frames_all, count, channels), jnp.bfloat16),
        in_specs=[vmem] * 4,
        out_specs=vmem,
        scratch_shapes=[
            pltpu.VMEM((frames_all, 3 * channels, count), jnp.bfloat16),
            pltpu.VMEM((frames_all, channels, count), jnp.bfloat16),
        ],
    )(grid, qkv_weight.T, pos_bias.transpose(0, 2, 1)[..., None], out_weight)


def body(latents, conv1_weight, qkv_weight, out_weight, pos_bias, conv2_weight):
    frames_dev, row_count, col_count, channels = latents.shape
    frames_all = lax.axis_size("frame")
    pix_piece = row_count * col_count // frames_all
    tile = latents.reshape(row_count, col_count, channels)
    hidden = convolve([tile], lambda c: tile[:, c, :], conv1_weight, norm_gelu)
    if row_count % frames_all == 0:
        piece_shape = (frames_all, row_count // frames_all, col_count, channels)
    else:
        piece_shape = (frames_all, pix_piece, channels)
    pieces = lax.all_to_all(hidden.reshape(piece_shape), "frame", split_axis=0, concat_axis=0, tiled=True)
    attended = attend(pieces.reshape(frames_all, pix_piece, channels), qkv_weight, pos_bias, out_weight)
    returned = lax.all_to_all(attended.reshape(piece_shape), "frame", split_axis=0, concat_axis=0, tiled=True)
    returned = returned.reshape(row_count, col_count, channels)

    def joined_edge(c):
        summed = hidden[:, c, :].astype(jnp.float32) + returned[:, c, :].astype(jnp.float32)
        return summed.astype(jnp.bfloat16)

    second = convolve([hidden, returned], joined_edge, conv2_weight, to_bf16)
    return second.reshape(frames_dev, row_count, col_count, channels)


def solution(mesh):
    groups = mesh.shape["groups"]
    frames_all = mesh.shape["frame"] // 4
    split_mesh = Mesh(
        mesh.devices.reshape(groups, 4, frames_all), ("groups", "quarter", "frame")
    )
    tiles = P(("groups", "quarter", "frame"), None, None, None)
    placed = (tiles, P(), P(), P(), P(), P())
    return jax.shard_map(
        body,
        mesh=split_mesh,
        in_specs=placed,
        out_specs=tiles,
        check_vma=False,
    )
```

```python
import functools

import jax
import jax.numpy as jnp
from jax import lax
from jax.experimental import pallas as pl
from jax.experimental.pallas import tpu as pltpu
from jax.sharding import Mesh, PartitionSpec as P

HEADS = 5


def shifted(block, axis, distance):
    devices = range(lax.axis_size(axis))
    route = [(i - distance, i) for i in devices if i - distance in devices]
    return lax.ppermute(block, axis, route)


def conv_kernel(*refs, parts, finish):
    sources = refs[:parts]
    w_ref, o_ref, edge_ref, slab, shift_s = refs[parts:]
    row_count, col_count, channels = o_ref.shape
    lanes = slab.shape[1] // 3
    band = 24
    span = band * col_count
    padded_rows = slab.shape[0]
    slab[pl.ds(0, col_count)] = jnp.zeros((col_count, slab.shape[1]), jnp.bfloat16)
    slab[pl.ds(padded_rows - col_count, col_count)] = jnp.zeros((col_count, slab.shape[1]), jnp.bfloat16)
    column = lax.broadcasted_iota(jnp.int32, (band, col_count, channels), 1)

    def build(i, carry):
        r0 = i * band
        block = sources[0][pl.ds(r0, band)].astype(jnp.float32)
        for extra in sources[1:]:
            block = block + extra[pl.ds(r0, band)].astype(jnp.float32)
        block = block.astype(jnp.bfloat16)
        shift_s[pl.ds(8, span)] = block.astype(jnp.float32).reshape(span, channels)
        before = shift_s[pl.ds(7, span)].reshape(band, col_count, channels)
        after = shift_s[pl.ds(9, span)].reshape(band, col_count, channels)
        before = jnp.where(column == 0, 0.0, before)
        after = jnp.where(column == col_count - 1, 0.0, after)
        rows = pl.ds(pl.multiple_of((r0 + 1) * col_count, col_count), span)
        slab[rows, pl.ds(0, channels)] = before.reshape(span, channels).astype(jnp.bfloat16)
        slab[rows, pl.ds(lanes, channels)] = block.reshape(span, channels)
        slab[rows, pl.ds(2 * lanes, channels)] = after.reshape(span, channels).astype(jnp.bfloat16)
        return carry

    lax.fori_loop(0, row_count // band, build, 0)

    def compute(i, carry):
        r0 = i * band
        acc = None
        for a in range(3):
            rows = pl.ds(pl.multiple_of((r0 + a) * col_count, col_count), span)
            term = jnp.dot(slab[rows, :], w_ref[a], preferred_element_type=jnp.float32)
            acc = term if acc is None else acc + term
        grid = acc.reshape(band, col_count, channels)
        o_ref[pl.ds(r0, band)] = finish(acc).reshape(band, col_count, channels)
        edge_ref[0, pl.ds(r0, band)] = grid[:, 0, :]
        edge_ref[1, pl.ds(r0, band)] = grid[:, col_count - 1, :]
        return carry

    lax.fori_loop(0, row_count // band, compute, 0)


def edge_kernel(x_ref, o_ref):
    block = x_ref[...]
    last = block.shape[1] - 1
    o_ref[0] = jnp.where(pl.program_id(0) == 0, block[:, 0, :], block[:, last, :])


def tile_edges(tile):
    row_count, col_count, channels = tile.shape
    width = 16
    blocks = col_count // width
    return pl.pallas_call(
        edge_kernel,
        out_shape=jax.ShapeDtypeStruct((2, row_count, channels), tile.dtype),
        grid=(2,),
        in_specs=[pl.BlockSpec((row_count, width, channels), lambda i: (0, i * (blocks - 1), 0))],
        out_specs=pl.BlockSpec((1, row_count, channels), lambda i: (i, 0, 0)),
    )(tile)


def norm_gelu(first):
    normed = first * lax.rsqrt(jnp.mean(first * first, axis=-1, keepdims=True) + 1e-06)
    return jax.nn.gelu(normed, approximate=True).astype(jnp.bfloat16)


def to_bf16(acc):
    return acc.astype(jnp.bfloat16)


def rim_term(rim, taps):
    padded = jnp.pad(rim, ((1, 1), (0, 0)))
    row_count = rim.shape[0]
    stacked = jnp.concatenate([padded[a : a + row_count] for a in range(3)], axis=1)
    return jnp.dot(stacked, taps.reshape(-1, taps.shape[-1]), preferred_element_type=jnp.float32)


def convolve(sources, edges, weight, finish):
    row_count, col_count, channels = sources[0].shape
    left_rim = shifted(edges[1], "quarter", 1)
    right_rim = shifted(edges[0], "quarter", -1)
    vmem = pl.BlockSpec(memory_space=pltpu.VMEM)
    padded = (row_count + 2) * col_count
    main, raw = pl.pallas_call(
        functools.partial(conv_kernel, parts=len(sources), finish=finish),
        out_shape=(
            jax.ShapeDtypeStruct((row_count, col_count, channels), jnp.bfloat16),
            jax.ShapeDtypeStruct((2, row_count, channels), jnp.float32),
        ),
        in_specs=[vmem] * (len(sources) + 1),
        out_specs=(vmem, vmem),
        scratch_shapes=[
            pltpu.VMEM((padded, 3 * channels), jnp.bfloat16),
            pltpu.VMEM((24 * col_count + 16, channels), jnp.float32),
        ],
    )(*sources, weight.reshape(3, 3 * channels, channels))
    first_col = finish(raw[0] + rim_term(left_rim, weight[:, 0]))
    last_col = finish(raw[1] + rim_term(right_rim, weight[:, 2]))
    main = main.at[:, 0, :].set(first_col)
    return main.at[:, col_count - 1, :].set(last_col)


def attend_kernel(x_ref, wqkv_ref, bias_ref, wout_ref, o_ref, qkv_s, blend_s):
    frames_all, count, channels = x_ref.shape
    head_dim = channels // HEADS
    scale = head_dim ** (-0.5)
    block = min(frames_all, 4)

    def project(f, carry):
        qkv_s[f] = lax.dot_general(
            wqkv_ref[...], x_ref[f], (((1,), (1,)), ((), ())), preferred_element_type=jnp.float32
        ).astype(jnp.bfloat16)
        return carry

    lax.fori_loop(0, frames_all, project, 0, unroll=frames_all <= 4)

    def head_block(h, first):
        frames = pl.ds(first, block)
        queries = qkv_s[frames, pl.ds(h * head_dim, head_dim), :].astype(jnp.float32)
        scores = []
        for g in range(frames_all):
            key_part = qkv_s[g, pl.ds(channels + h * head_dim, head_dim), :].astype(jnp.float32)
            bias = bias_ref[h, g, frames]
            scores.append(jnp.sum(queries * key_part[None], axis=1) * scale + bias)
        top = scores[0]
        for g in range(1, frames_all):
            top = jnp.maximum(top, scores[g])
        weights = [jnp.exp(s - top) for s in scores]
        total = weights[0]
        for g in range(1, frames_all):
            total = total + weights[g]
        blended = None
        for g in range(frames_all):
            value_part = qkv_s[g, pl.ds(2 * channels + h * head_dim, head_dim), :].astype(jnp.float32)
            prob = (weights[g] / total).astype(jnp.bfloat16).astype(jnp.float32)
            term = prob[:, None, :] * value_part[None]
            blended = term if blended is None else blended + term
        blend_s[frames, pl.ds(h * head_dim, head_dim), :] = blended.astype(jnp.bfloat16)

    def frame_block(i, carry):
        for h in range(HEADS):
            head_block(h, i * block)
        return carry

    lax.fori_loop(0, frames_all // block, frame_block, 0, unroll=frames_all <= 4)

    def out_project(f, carry):
        o_ref[f] = lax.dot_general(
            blend_s[f], wout_ref[...], (((0,), (0,)), ((), ())), preferred_element_type=jnp.float32
        ).astype(jnp.bfloat16)
        return carry

    lax.fori_loop(0, frames_all, out_project, 0, unroll=frames_all <= 4)


def attend(grid, qkv_weight, pos_bias, out_weight):
    frames_all, count, channels = grid.shape
    vmem = pl.BlockSpec(memory_space=pltpu.VMEM)
    return pl.pallas_call(
        attend_kernel,
        out_shape=jax.ShapeDtypeStruct((frames_all, count, channels), jnp.bfloat16),
        in_specs=[vmem] * 4,
        out_specs=vmem,
        scratch_shapes=[
            pltpu.VMEM((frames_all, 3 * channels, count), jnp.bfloat16),
            pltpu.VMEM((frames_all, channels, count), jnp.bfloat16),
        ],
    )(grid, qkv_weight.T, pos_bias.transpose(0, 2, 1)[..., None], out_weight)


def body(latents, conv1_weight, qkv_weight, out_weight, pos_bias, conv2_weight):
    frames_dev, row_count, col_count, channels = latents.shape
    frames_all = lax.axis_size("frame")
    pix_piece = row_count * col_count // frames_all
    tile = latents.reshape(row_count, col_count, channels)
    hidden = convolve([tile], tile_edges(tile), conv1_weight, norm_gelu)
    if row_count % frames_all == 0:
        piece_shape = (frames_all, row_count // frames_all, col_count, channels)
    else:
        piece_shape = (frames_all, pix_piece, channels)
    pieces = lax.all_to_all(hidden.reshape(piece_shape), "frame", split_axis=0, concat_axis=0, tiled=True)
    attended = attend(pieces.reshape(frames_all, pix_piece, channels), qkv_weight, pos_bias, out_weight)
    returned = lax.all_to_all(attended.reshape(piece_shape), "frame", split_axis=0, concat_axis=0, tiled=True)
    returned = returned.reshape(row_count, col_count, channels)

    joined_edges = (
        tile_edges(hidden).astype(jnp.float32) + tile_edges(returned).astype(jnp.float32)
    ).astype(jnp.bfloat16)
    second = convolve([hidden, returned], joined_edges, conv2_weight, to_bf16)
    return second.reshape(frames_dev, row_count, col_count, channels)


def solution(mesh):
    groups = mesh.shape["groups"]
    frames_all = mesh.shape["frame"] // 4
    split_mesh = Mesh(
        mesh.devices.reshape(groups, 4, frames_all), ("groups", "quarter", "frame")
    )
    tiles = P(("groups", "quarter", "frame"), None, None, None)
    placed = (tiles, P(), P(), P(), P(), P())
    return jax.shard_map(
        body,
        mesh=split_mesh,
        in_specs=placed,
        out_specs=tiles,
        check_vma=False,
    )
```

```python
import functools

import jax
import jax.numpy as jnp
from jax import lax
from jax.experimental import pallas as pl
from jax.experimental.pallas import tpu as pltpu
from jax.sharding import Mesh, PartitionSpec as P

HEADS = 5


def shifted(block, axis, distance):
    devices = range(lax.axis_size(axis))
    route = [(i - distance, i) for i in devices if i - distance in devices]
    return lax.ppermute(block, axis, route)


def conv_kernel(*refs, layout, lo, hi, finish):
    count = sum(len(segments) for segments in layout)
    flat = refs[:count]
    left_ref, right_ref, w_ref, o_ref, slab, shift_s = refs[count:]
    row_count = left_ref.shape[0]
    _, col_count, channels = o_ref.shape
    lanes = slab.shape[1] // 3
    band = 12
    span = band * col_count
    padded_rows = slab.shape[0]
    slab[pl.ds(0, col_count)] = jnp.zeros((col_count, slab.shape[1]), jnp.bfloat16)
    slab[pl.ds(padded_rows - col_count, col_count)] = jnp.zeros((col_count, slab.shape[1]), jnp.bfloat16)
    column = lax.broadcasted_iota(jnp.int32, (band, col_count, channels), 1)
    addends = []
    at = 0
    for segments in layout:
        addends.append(list(zip(flat[at : at + len(segments)], segments)))
        at += len(segments)

    def rows_of(ref_list, r0):
        for ref, (first, last) in ref_list:
            if first <= r0 < last:
                return ref[pl.ds(r0 - first, band)]

    for r0 in range(max(lo - band, 0), min(hi + band, row_count), band):
        block = rows_of(addends[0], r0).astype(jnp.float32)
        for extra in addends[1:]:
            block = block + rows_of(extra, r0).astype(jnp.float32)
        block = block.astype(jnp.bfloat16)
        shift_s[pl.ds(8, span)] = block.astype(jnp.float32).reshape(span, channels)
        before = shift_s[pl.ds(7, span)].reshape(band, col_count, channels)
        after = shift_s[pl.ds(9, span)].reshape(band, col_count, channels)
        rim_l = left_ref[pl.ds(r0, band)].astype(jnp.float32)[:, None, :]
        rim_r = right_ref[pl.ds(r0, band)].astype(jnp.float32)[:, None, :]
        before = jnp.where(column == 0, rim_l, before)
        after = jnp.where(column == col_count - 1, rim_r, after)
        rows = pl.ds((r0 + 1) * col_count, span)
        slab[rows, pl.ds(0, channels)] = before.reshape(span, channels).astype(jnp.bfloat16)
        slab[rows, pl.ds(lanes, channels)] = block.reshape(span, channels)
        slab[rows, pl.ds(2 * lanes, channels)] = after.reshape(span, channels).astype(jnp.bfloat16)

    for r0 in range(lo, hi, band):
        acc = None
        for a in range(3):
            rows = pl.ds((r0 + a) * col_count, span)
            term = jnp.dot(slab[rows, :], w_ref[a], preferred_element_type=jnp.float32)
            acc = term if acc is None else acc + term
        o_ref[pl.ds(r0 - lo, band)] = finish(acc).reshape(band, col_count, channels)


def norm_gelu(first):
    normed = first * lax.rsqrt(jnp.mean(first * first, axis=-1, keepdims=True) + 1e-06)
    return jax.nn.gelu(normed, approximate=True).astype(jnp.bfloat16)


def to_bf16(acc):
    return acc.astype(jnp.bfloat16)


def halo(edge_of):
    return shifted(edge_of(-1), "quarter", 1), shifted(edge_of(0), "quarter", -1)


def convolve(groups, rims, weight, finish, lo, hi):
    row_count, channels = rims[0].shape
    col_count = groups[0][0].shape[1]
    layout = []
    for segments in groups:
        spans = []
        first = 0
        for piece in segments:
            spans.append((first, first + piece.shape[0]))
            first += piece.shape[0]
        layout.append(tuple(spans))
    flat = [piece for segments in groups for piece in segments]
    vmem = pl.BlockSpec(memory_space=pltpu.VMEM)
    padded = (row_count + 2) * col_count
    stacked = weight.reshape(3, 3 * channels, channels)
    return pl.pallas_call(
        functools.partial(conv_kernel, layout=tuple(layout), lo=lo, hi=hi, finish=finish),
        out_shape=jax.ShapeDtypeStruct((hi - lo, col_count, channels), jnp.bfloat16),
        in_specs=[vmem] * (len(flat) + 3),
        out_specs=vmem,
        scratch_shapes=[
            pltpu.VMEM((padded, 3 * channels), jnp.bfloat16),
            pltpu.VMEM((12 * col_count + 16, channels), jnp.float32),
        ],
    )(*flat, *rims, stacked)


def attend_kernel(x_ref, wqkv_ref, bias_ref, wout_ref, o_ref, qkv_s, blend_s):
    frames_all, count, channels = x_ref.shape
    head_dim = channels // HEADS
    scale = head_dim ** (-0.5)
    block = min(frames_all, 4)

    def project(f, carry):
        qkv_s[f] = lax.dot_general(
            wqkv_ref[...], x_ref[f], (((1,), (1,)), ((), ())), preferred_element_type=jnp.float32
        ).astype(jnp.bfloat16)
        return carry

    lax.fori_loop(0, frames_all, project, 0, unroll=frames_all <= 4)

    def head_block(h, first):
        frames = pl.ds(first, block)
        queries = qkv_s[frames, pl.ds(h * head_dim, head_dim), :].astype(jnp.float32)
        scores = []
        for g in range(frames_all):
            key_part = qkv_s[g, pl.ds(channels + h * head_dim, head_dim), :].astype(jnp.float32)
            bias = bias_ref[h, g, frames]
            scores.append(jnp.sum(queries * key_part[None], axis=1) * scale + bias)
        top = scores[0]
        for g in range(1, frames_all):
            top = jnp.maximum(top, scores[g])
        weights = [jnp.exp(s - top) for s in scores]
        total = weights[0]
        for g in range(1, frames_all):
            total = total + weights[g]
        blended = None
        for g in range(frames_all):
            value_part = qkv_s[g, pl.ds(2 * channels + h * head_dim, head_dim), :].astype(jnp.float32)
            prob = (weights[g] / total).astype(jnp.bfloat16).astype(jnp.float32)
            term = prob[:, None, :] * value_part[None]
            blended = term if blended is None else blended + term
        blend_s[frames, pl.ds(h * head_dim, head_dim), :] = blended.astype(jnp.bfloat16)

    def frame_block(i, carry):
        for h in range(HEADS):
            head_block(h, i * block)
        return carry

    lax.fori_loop(0, frames_all // block, frame_block, 0, unroll=frames_all <= 4)

    def out_project(f, carry):
        o_ref[f] = lax.dot_general(
            blend_s[f], wout_ref[...], (((0,), (0,)), ((), ())), preferred_element_type=jnp.float32
        ).astype(jnp.bfloat16)
        return carry

    lax.fori_loop(0, frames_all, out_project, 0, unroll=frames_all <= 4)


def attend(grid, qkv_weight, pos_bias, out_weight):
    frames_all, count, channels = grid.shape
    vmem = pl.BlockSpec(memory_space=pltpu.VMEM)
    return pl.pallas_call(
        attend_kernel,
        out_shape=jax.ShapeDtypeStruct((frames_all, count, channels), jnp.bfloat16),
        in_specs=[vmem] * 4,
        out_specs=vmem,
        scratch_shapes=[
            pltpu.VMEM((frames_all, 3 * channels, count), jnp.bfloat16),
            pltpu.VMEM((frames_all, channels, count), jnp.bfloat16),
        ],
    )(grid, qkv_weight.T, pos_bias.transpose(0, 2, 1)[..., None], out_weight)


def body(latents, conv1_weight, qkv_weight, out_weight, pos_bias, conv2_weight):
    frames_dev, row_count, col_count, channels = latents.shape
    frames_all = lax.axis_size("frame")
    tile = latents.reshape(row_count, col_count, channels)
    rims = halo(lambda c: tile[:, c, :])
    half = row_count // 2
    hidden = []
    returned = []
    for lo in (0, half):
        hidden.append(convolve([[tile]], rims, conv1_weight, norm_gelu, lo, lo + half))
    pix_piece = half * col_count // frames_all
    if half % frames_all == 0:
        piece_shape = (frames_all, half // frames_all, col_count, channels)
    else:
        piece_shape = (frames_all, pix_piece, channels)
    for part in hidden:
        pieces = lax.all_to_all(part.reshape(piece_shape), "frame", split_axis=0, concat_axis=0, tiled=True)
        attended = attend(pieces.reshape(frames_all, pix_piece, channels), qkv_weight, pos_bias, out_weight)
        back = lax.all_to_all(attended.reshape(piece_shape), "frame", split_axis=0, concat_axis=0, tiled=True)
        returned.append(back.reshape(half, col_count, channels))

    def joined_edge(c):
        summed = [h[:, c, :].astype(jnp.float32) + r[:, c, :].astype(jnp.float32) for h, r in zip(hidden, returned)]
        return jnp.concatenate(summed, axis=0).astype(jnp.bfloat16)

    second = convolve([hidden, returned], halo(joined_edge), conv2_weight, to_bf16, 0, row_count)
    return second.reshape(frames_dev, row_count, col_count, channels)


def solution(mesh):
    groups = mesh.shape["groups"]
    frames_all = mesh.shape["frame"] // 4
    split_mesh = Mesh(
        mesh.devices.reshape(groups, 4, frames_all), ("groups", "quarter", "frame")
    )
    tiles = P(("groups", "quarter", "frame"), None, None, None)
    placed = (tiles, P(), P(), P(), P(), P())
    return jax.shard_map(
        body,
        mesh=split_mesh,
        in_specs=placed,
        out_specs=tiles,
        check_vma=False,
    )
```

```python
import functools

import jax
import jax.numpy as jnp
from jax import lax
from jax.experimental import pallas as pl
from jax.experimental.pallas import tpu as pltpu
from jax.sharding import Mesh, PartitionSpec as P

HEADS = 5


def shifted(block, axis, distance):
    devices = range(lax.axis_size(axis))
    route = [(i - distance, i) for i in devices if i - distance in devices]
    return lax.ppermute(block, axis, route)


def conv_kernel(*refs, layout, lo, hi, finish):
    count = sum(len(segments) for segments in layout)
    flat = refs[:count]
    left_ref, right_ref, w_ref, o_ref, slab, shift_s = refs[count:]
    row_count = left_ref.shape[0]
    _, col_count, channels = o_ref.shape
    lanes = slab.shape[1] // 3
    band = 12
    span = band * col_count
    padded_rows = slab.shape[0]
    slab[pl.ds(0, col_count)] = jnp.zeros((col_count, slab.shape[1]), jnp.bfloat16)
    slab[pl.ds(padded_rows - col_count, col_count)] = jnp.zeros((col_count, slab.shape[1]), jnp.bfloat16)
    column = lax.broadcasted_iota(jnp.int32, (band, col_count, channels), 1)
    addends = []
    at = 0
    for segments in layout:
        addends.append(list(zip(flat[at : at + len(segments)], segments)))
        at += len(segments)

    def rows_of(ref_list, r0):
        for ref, (first, last) in ref_list:
            if first <= r0 < last:
                return ref[pl.ds(r0 - first, band)]

    for r0 in range(max(lo - band, 0), min(hi + band, row_count), band):
        block = rows_of(addends[0], r0).astype(jnp.float32)
        for extra in addends[1:]:
            block = block + rows_of(extra, r0).astype(jnp.float32)
        block = block.astype(jnp.bfloat16)
        shift_s[pl.ds(8, span)] = block.astype(jnp.float32).reshape(span, channels)
        before = shift_s[pl.ds(7, span)].reshape(band, col_count, channels)
        after = shift_s[pl.ds(9, span)].reshape(band, col_count, channels)
        rim_l = left_ref[pl.ds(r0, band)].astype(jnp.float32)[:, None, :]
        rim_r = right_ref[pl.ds(r0, band)].astype(jnp.float32)[:, None, :]
        before = jnp.where(column == 0, rim_l, before)
        after = jnp.where(column == col_count - 1, rim_r, after)
        rows = pl.ds((r0 + 1) * col_count, span)
        slab[rows, pl.ds(0, channels)] = before.reshape(span, channels).astype(jnp.bfloat16)
        slab[rows, pl.ds(lanes, channels)] = block.reshape(span, channels)
        slab[rows, pl.ds(2 * lanes, channels)] = after.reshape(span, channels).astype(jnp.bfloat16)

    for r0 in range(lo, hi, band):
        acc = None
        for a in range(3):
            rows = pl.ds((r0 + a) * col_count, span)
            term = jnp.dot(slab[rows, :], w_ref[a], preferred_element_type=jnp.float32)
            acc = term if acc is None else acc + term
        o_ref[pl.ds(r0 - lo, band)] = finish(acc).reshape(band, col_count, channels)


def norm_gelu(first):
    normed = first * lax.rsqrt(jnp.mean(first * first, axis=-1, keepdims=True) + 1e-06)
    return jax.nn.gelu(normed, approximate=True).astype(jnp.bfloat16)


def to_bf16(acc):
    return acc.astype(jnp.bfloat16)


def halo(edge_of):
    quarter = lax.axis_index("quarter")
    quarters = lax.axis_size("quarter")
    first = edge_of(0)[None]
    last = edge_of(-1)[None]
    slot = lax.broadcasted_iota(jnp.int32, (quarters, 1, 1), 0)
    zero = jnp.zeros_like(first)
    send = jnp.where(slot == quarter + 1, last, jnp.where(slot == quarter - 1, first, zero))
    got = lax.all_to_all(send, "quarter", split_axis=0, concat_axis=0, tiled=True)
    left = lax.dynamic_index_in_dim(got, jnp.maximum(quarter - 1, 0), keepdims=False)
    right = lax.dynamic_index_in_dim(got, jnp.minimum(quarter + 1, quarters - 1), keepdims=False)
    left = jnp.where(quarter > 0, left, jnp.zeros_like(left))
    right = jnp.where(quarter < quarters - 1, right, jnp.zeros_like(right))
    return left, right


def convolve(groups, rims, weight, finish, lo, hi):
    row_count, channels = rims[0].shape
    col_count = groups[0][0].shape[1]
    layout = []
    for segments in groups:
        spans = []
        first = 0
        for piece in segments:
            spans.append((first, first + piece.shape[0]))
            first += piece.shape[0]
        layout.append(tuple(spans))
    flat = [piece for segments in groups for piece in segments]
    vmem = pl.BlockSpec(memory_space=pltpu.VMEM)
    padded = (row_count + 2) * col_count
    stacked = weight.reshape(3, 3 * channels, channels)
    return pl.pallas_call(
        functools.partial(conv_kernel, layout=tuple(layout), lo=lo, hi=hi, finish=finish),
        out_shape=jax.ShapeDtypeStruct((hi - lo, col_count, channels), jnp.bfloat16),
        in_specs=[vmem] * (len(flat) + 3),
        out_specs=vmem,
        scratch_shapes=[
            pltpu.VMEM((padded, 3 * channels), jnp.bfloat16),
            pltpu.VMEM((12 * col_count + 16, channels), jnp.float32),
        ],
    )(*flat, *rims, stacked)


def attend_kernel(x_ref, wqkv_ref, bias_ref, wout_ref, o_ref, qkv_s, blend_s):
    frames_all, count, channels = x_ref.shape
    head_dim = channels // HEADS
    scale = head_dim ** (-0.5)
    block = min(frames_all, 4)

    def project(f, carry):
        qkv_s[f] = lax.dot_general(
            wqkv_ref[...], x_ref[f], (((1,), (1,)), ((), ())), preferred_element_type=jnp.float32
        ).astype(jnp.bfloat16)
        return carry

    lax.fori_loop(0, frames_all, project, 0, unroll=frames_all <= 4)

    def head_block(h, first):
        frames = pl.ds(first, block)
        queries = qkv_s[frames, pl.ds(h * head_dim, head_dim), :].astype(jnp.float32)
        scores = []
        for g in range(frames_all):
            key_part = qkv_s[g, pl.ds(channels + h * head_dim, head_dim), :].astype(jnp.float32)
            bias = bias_ref[h, g, frames]
            scores.append(jnp.sum(queries * key_part[None], axis=1) * scale + bias)
        top = scores[0]
        for g in range(1, frames_all):
            top = jnp.maximum(top, scores[g])
        weights = [jnp.exp(s - top) for s in scores]
        total = weights[0]
        for g in range(1, frames_all):
            total = total + weights[g]
        blended = None
        for g in range(frames_all):
            value_part = qkv_s[g, pl.ds(2 * channels + h * head_dim, head_dim), :].astype(jnp.float32)
            prob = (weights[g] / total).astype(jnp.bfloat16).astype(jnp.float32)
            term = prob[:, None, :] * value_part[None]
            blended = term if blended is None else blended + term
        blend_s[frames, pl.ds(h * head_dim, head_dim), :] = blended.astype(jnp.bfloat16)

    def frame_block(i, carry):
        for h in range(HEADS):
            head_block(h, i * block)
        return carry

    lax.fori_loop(0, frames_all // block, frame_block, 0, unroll=frames_all <= 4)

    def out_project(f, carry):
        o_ref[f] = lax.dot_general(
            blend_s[f], wout_ref[...], (((0,), (0,)), ((), ())), preferred_element_type=jnp.float32
        ).astype(jnp.bfloat16)
        return carry

    lax.fori_loop(0, frames_all, out_project, 0, unroll=frames_all <= 4)


def attend(grid, qkv_weight, pos_bias, out_weight):
    frames_all, count, channels = grid.shape
    vmem = pl.BlockSpec(memory_space=pltpu.VMEM)
    return pl.pallas_call(
        attend_kernel,
        out_shape=jax.ShapeDtypeStruct((frames_all, count, channels), jnp.bfloat16),
        in_specs=[vmem] * 4,
        out_specs=vmem,
        scratch_shapes=[
            pltpu.VMEM((frames_all, 3 * channels, count), jnp.bfloat16),
            pltpu.VMEM((frames_all, channels, count), jnp.bfloat16),
        ],
    )(grid, qkv_weight.T, pos_bias.transpose(0, 2, 1)[..., None], out_weight)


def body(latents, conv1_weight, qkv_weight, out_weight, pos_bias, conv2_weight):
    frames_dev, row_count, col_count, channels = latents.shape
    frames_all = lax.axis_size("frame")
    tile = latents.reshape(row_count, col_count, channels)
    rims = halo(lambda c: tile[:, c, :])
    half = row_count // 2
    hidden = []
    returned = []
    for lo in (0, half):
        hidden.append(convolve([[tile]], rims, conv1_weight, norm_gelu, lo, lo + half))
    pix_piece = half * col_count // frames_all
    if half % frames_all == 0:
        piece_shape = (frames_all, half // frames_all, col_count, channels)
    else:
        piece_shape = (frames_all, pix_piece, channels)
    for part in hidden:
        pieces = lax.all_to_all(part.reshape(piece_shape), "frame", split_axis=0, concat_axis=0, tiled=True)
        attended = attend(pieces.reshape(frames_all, pix_piece, channels), qkv_weight, pos_bias, out_weight)
        back = lax.all_to_all(attended.reshape(piece_shape), "frame", split_axis=0, concat_axis=0, tiled=True)
        returned.append(back.reshape(half, col_count, channels))

    def joined_edge(c):
        summed = [h[:, c, :].astype(jnp.float32) + r[:, c, :].astype(jnp.float32) for h, r in zip(hidden, returned)]
        return jnp.concatenate(summed, axis=0).astype(jnp.bfloat16)

    second = convolve([hidden, returned], halo(joined_edge), conv2_weight, to_bf16, 0, row_count)
    return second.reshape(frames_dev, row_count, col_count, channels)


def solution(mesh):
    groups = mesh.shape["groups"]
    frames_all = mesh.shape["frame"] // 4
    split_mesh = Mesh(
        mesh.devices.reshape(groups, 4, frames_all), ("groups", "quarter", "frame")
    )
    tiles = P(("groups", "quarter", "frame"), None, None, None)
    placed = (tiles, P(), P(), P(), P(), P())
    return jax.shard_map(
        body,
        mesh=split_mesh,
        in_specs=placed,
        out_specs=tiles,
        check_vma=False,
    )
```

```python
import functools

import jax
import jax.numpy as jnp
from jax import lax
from jax.experimental import pallas as pl
from jax.experimental.pallas import tpu as pltpu
from jax.sharding import Mesh, PartitionSpec as P

HEADS = 5


def shifted(block, axis, distance):
    size = lax.axis_size(axis)
    route = [((i - distance) % size, i) for i in range(size)]
    moved = lax.ppermute(block, axis, route)
    source = lax.axis_index(axis) - distance
    inside = (source >= 0) & (source < size)
    return jnp.where(inside, moved, jnp.zeros_like(moved))


def conv_kernel(*refs, layout, lo, hi, finish):
    count = sum(len(segments) for segments in layout)
    flat = refs[:count]
    left_ref, right_ref, w_ref, o_ref, slab, shift_s = refs[count:]
    row_count = left_ref.shape[0]
    _, col_count, channels = o_ref.shape
    lanes = slab.shape[1] // 3
    band = 12
    span = band * col_count
    padded_rows = slab.shape[0]
    slab[pl.ds(0, col_count)] = jnp.zeros((col_count, slab.shape[1]), jnp.bfloat16)
    slab[pl.ds(padded_rows - col_count, col_count)] = jnp.zeros((col_count, slab.shape[1]), jnp.bfloat16)
    column = lax.broadcasted_iota(jnp.int32, (band, col_count, channels), 1)
    addends = []
    at = 0
    for segments in layout:
        addends.append(list(zip(flat[at : at + len(segments)], segments)))
        at += len(segments)

    def rows_of(ref_list, r0):
        for ref, (first, last) in ref_list:
            if first <= r0 < last:
                return ref[pl.ds(r0 - first, band)]

    for r0 in range(max(lo - band, 0), min(hi + band, row_count), band):
        block = rows_of(addends[0], r0).astype(jnp.float32)
        for extra in addends[1:]:
            block = block + rows_of(extra, r0).astype(jnp.float32)
        block = block.astype(jnp.bfloat16)
        shift_s[pl.ds(8, span)] = block.astype(jnp.float32).reshape(span, channels)
        before = shift_s[pl.ds(7, span)].reshape(band, col_count, channels)
        after = shift_s[pl.ds(9, span)].reshape(band, col_count, channels)
        rim_l = left_ref[pl.ds(r0, band)].astype(jnp.float32)[:, None, :]
        rim_r = right_ref[pl.ds(r0, band)].astype(jnp.float32)[:, None, :]
        before = jnp.where(column == 0, rim_l, before)
        after = jnp.where(column == col_count - 1, rim_r, after)
        rows = pl.ds((r0 + 1) * col_count, span)
        slab[rows, pl.ds(0, channels)] = before.reshape(span, channels).astype(jnp.bfloat16)
        slab[rows, pl.ds(lanes, channels)] = block.reshape(span, channels)
        slab[rows, pl.ds(2 * lanes, channels)] = after.reshape(span, channels).astype(jnp.bfloat16)

    for r0 in range(lo, hi, band):
        acc = None
        for a in range(3):
            rows = pl.ds((r0 + a) * col_count, span)
            term = jnp.dot(slab[rows, :], w_ref[a], preferred_element_type=jnp.float32)
            acc = term if acc is None else acc + term
        o_ref[pl.ds(r0 - lo, band)] = finish(acc).reshape(band, col_count, channels)


def norm_gelu(first):
    normed = first * lax.rsqrt(jnp.mean(first * first, axis=-1, keepdims=True) + 1e-06)
    return jax.nn.gelu(normed, approximate=True).astype(jnp.bfloat16)


def to_bf16(acc):
    return acc.astype(jnp.bfloat16)


def halo(edge_of):
    return shifted(edge_of(-1), "quarter", 1), shifted(edge_of(0), "quarter", -1)


def convolve(groups, rims, weight, finish, lo, hi):
    row_count, channels = rims[0].shape
    col_count = groups[0][0].shape[1]
    layout = []
    for segments in groups:
        spans = []
        first = 0
        for piece in segments:
            spans.append((first, first + piece.shape[0]))
            first += piece.shape[0]
        layout.append(tuple(spans))
    flat = [piece for segments in groups for piece in segments]
    vmem = pl.BlockSpec(memory_space=pltpu.VMEM)
    padded = (row_count + 2) * col_count
    stacked = weight.reshape(3, 3 * channels, channels)
    return pl.pallas_call(
        functools.partial(conv_kernel, layout=tuple(layout), lo=lo, hi=hi, finish=finish),
        out_shape=jax.ShapeDtypeStruct((hi - lo, col_count, channels), jnp.bfloat16),
        in_specs=[vmem] * (len(flat) + 3),
        out_specs=vmem,
        scratch_shapes=[
            pltpu.VMEM((padded, 3 * channels), jnp.bfloat16),
            pltpu.VMEM((12 * col_count + 16, channels), jnp.float32),
        ],
    )(*flat, *rims, stacked)


def attend_kernel(x_ref, wqkv_ref, bias_ref, wout_ref, o_ref, qkv_s, blend_s):
    frames_all, count, channels = x_ref.shape
    head_dim = channels // HEADS
    scale = head_dim ** (-0.5)
    block = min(frames_all, 4)

    def project(f, carry):
        qkv_s[f] = lax.dot_general(
            wqkv_ref[...], x_ref[f], (((1,), (1,)), ((), ())), preferred_element_type=jnp.float32
        ).astype(jnp.bfloat16)
        return carry

    lax.fori_loop(0, frames_all, project, 0, unroll=frames_all <= 4)

    def head_block(h, first):
        frames = pl.ds(first, block)
        queries = qkv_s[frames, pl.ds(h * head_dim, head_dim), :].astype(jnp.float32)
        scores = []
        for g in range(frames_all):
            key_part = qkv_s[g, pl.ds(channels + h * head_dim, head_dim), :].astype(jnp.float32)
            bias = bias_ref[h, g, frames]
            scores.append(jnp.sum(queries * key_part[None], axis=1) * scale + bias)
        top = scores[0]
        for g in range(1, frames_all):
            top = jnp.maximum(top, scores[g])
        weights = [jnp.exp(s - top) for s in scores]
        total = weights[0]
        for g in range(1, frames_all):
            total = total + weights[g]
        blended = None
        for g in range(frames_all):
            value_part = qkv_s[g, pl.ds(2 * channels + h * head_dim, head_dim), :].astype(jnp.float32)
            prob = (weights[g] / total).astype(jnp.bfloat16).astype(jnp.float32)
            term = prob[:, None, :] * value_part[None]
            blended = term if blended is None else blended + term
        blend_s[frames, pl.ds(h * head_dim, head_dim), :] = blended.astype(jnp.bfloat16)

    def frame_block(i, carry):
        for h in range(HEADS):
            head_block(h, i * block)
        return carry

    lax.fori_loop(0, frames_all // block, frame_block, 0, unroll=frames_all <= 4)

    def out_project(f, carry):
        o_ref[f] = lax.dot_general(
            blend_s[f], wout_ref[...], (((0,), (0,)), ((), ())), preferred_element_type=jnp.float32
        ).astype(jnp.bfloat16)
        return carry

    lax.fori_loop(0, frames_all, out_project, 0, unroll=frames_all <= 4)


def attend(grid, qkv_weight, pos_bias, out_weight):
    frames_all, count, channels = grid.shape
    vmem = pl.BlockSpec(memory_space=pltpu.VMEM)
    return pl.pallas_call(
        attend_kernel,
        out_shape=jax.ShapeDtypeStruct((frames_all, count, channels), jnp.bfloat16),
        in_specs=[vmem] * 4,
        out_specs=vmem,
        scratch_shapes=[
            pltpu.VMEM((frames_all, 3 * channels, count), jnp.bfloat16),
            pltpu.VMEM((frames_all, channels, count), jnp.bfloat16),
        ],
    )(grid, qkv_weight.T, pos_bias.transpose(0, 2, 1)[..., None], out_weight)


def body(latents, conv1_weight, qkv_weight, out_weight, pos_bias, conv2_weight):
    frames_dev, row_count, col_count, channels = latents.shape
    frames_all = lax.axis_size("frame")
    tile = latents.reshape(row_count, col_count, channels)
    rims = halo(lambda c: tile[:, c, :])
    half = row_count // 2
    hidden = []
    returned = []
    for lo in (0, half):
        hidden.append(convolve([[tile]], rims, conv1_weight, norm_gelu, lo, lo + half))
    pix_piece = half * col_count // frames_all
    if half % frames_all == 0:
        piece_shape = (frames_all, half // frames_all, col_count, channels)
    else:
        piece_shape = (frames_all, pix_piece, channels)
    for part in hidden:
        pieces = lax.all_to_all(part.reshape(piece_shape), "frame", split_axis=0, concat_axis=0, tiled=True)
        attended = attend(pieces.reshape(frames_all, pix_piece, channels), qkv_weight, pos_bias, out_weight)
        back = lax.all_to_all(attended.reshape(piece_shape), "frame", split_axis=0, concat_axis=0, tiled=True)
        returned.append(back.reshape(half, col_count, channels))

    def joined_edge(c):
        summed = [h[:, c, :].astype(jnp.float32) + r[:, c, :].astype(jnp.float32) for h, r in zip(hidden, returned)]
        return jnp.concatenate(summed, axis=0).astype(jnp.bfloat16)

    second = convolve([hidden, returned], halo(joined_edge), conv2_weight, to_bf16, 0, row_count)
    return second.reshape(frames_dev, row_count, col_count, channels)


def solution(mesh):
    groups = mesh.shape["groups"]
    frames_all = mesh.shape["frame"] // 4
    split_mesh = Mesh(
        mesh.devices.reshape(groups, 4, frames_all), ("groups", "quarter", "frame")
    )
    tiles = P(("groups", "quarter", "frame"), None, None, None)
    placed = (tiles, P(), P(), P(), P(), P())
    return jax.shard_map(
        body,
        mesh=split_mesh,
        in_specs=placed,
        out_specs=tiles,
        check_vma=False,
    )
```

```python
import functools

import jax
import jax.numpy as jnp
from jax import lax
from jax.experimental import pallas as pl
from jax.experimental.pallas import tpu as pltpu
from jax.sharding import Mesh, PartitionSpec as P

HEADS = 5


def shifted(block, axis, distance):
    size = lax.axis_size(axis)
    route = [((i - distance) % size, i) for i in range(size)]
    moved = lax.ppermute(block, axis, route)
    source = lax.axis_index(axis) - distance
    inside = (source >= 0) & (source < size)
    return jnp.where(inside, moved, jnp.zeros_like(moved))


def conv_kernel(*refs, segments, parts, lo, band, first_build, lag, finish):
    count = len(segments) * parts
    blocks = refs[:count]
    left_ref, right_ref, w_hbm, o_ref, slab, shift_s, w_vmem, sem = refs[count:]
    _, col_count, channels = o_ref.shape
    lanes = slab.shape[1] // 3
    span = band * col_count
    padded_rows = slab.shape[0]
    step = pl.program_id(0)
    weight_copy = pltpu.make_async_copy(w_hbm, w_vmem, sem.at[0])

    @pl.when(step == 0)
    def _():
        weight_copy.start()
        slab[pl.ds(0, col_count)] = jnp.zeros((col_count, slab.shape[1]), jnp.bfloat16)
        slab[pl.ds(padded_rows - col_count, col_count)] = jnp.zeros((col_count, slab.shape[1]), jnp.bfloat16)

    r0 = first_build + step * band
    column = lax.broadcasted_iota(jnp.int32, (band, col_count, channels), 1)
    for t, (first, last) in enumerate(segments):

        @pl.when((r0 >= first) & (r0 < last))
        def _():
            block = blocks[t][...].astype(jnp.float32)
            for k in range(1, parts):
                block = block + blocks[k * len(segments) + t][...].astype(jnp.float32)
            block = block.astype(jnp.bfloat16)
            shift_s[pl.ds(8, span)] = block.astype(jnp.float32).reshape(span, channels)
            before = shift_s[pl.ds(7, span)].reshape(band, col_count, channels)
            after = shift_s[pl.ds(9, span)].reshape(band, col_count, channels)
            rim_l = left_ref[0].astype(jnp.float32)[:, None, :]
            rim_r = right_ref[0].astype(jnp.float32)[:, None, :]
            before = jnp.where(column == 0, rim_l, before)
            after = jnp.where(column == col_count - 1, rim_r, after)
            rows = pl.ds(pl.multiple_of((r0 + 1) * col_count, col_count), span)
            slab[rows, pl.ds(0, channels)] = before.reshape(span, channels).astype(jnp.bfloat16)
            slab[rows, pl.ds(lanes, channels)] = block.reshape(span, channels)
            slab[rows, pl.ds(2 * lanes, channels)] = after.reshape(span, channels).astype(jnp.bfloat16)

    @pl.when(step == lag)
    def _():
        weight_copy.wait()

    @pl.when(step >= lag)
    def _():
        out0 = lo + (step - lag) * band
        acc = None
        for a in range(3):
            rows = pl.ds(pl.multiple_of((out0 + a) * col_count, col_count), span)
            term = jnp.dot(slab[rows, :], w_vmem[a], preferred_element_type=jnp.float32)
            acc = term if acc is None else acc + term
        o_ref[...] = finish(acc).reshape(band, col_count, channels)


def norm_gelu(first):
    normed = first * lax.rsqrt(jnp.mean(first * first, axis=-1, keepdims=True) + 1e-06)
    return jax.nn.gelu(normed, approximate=True).astype(jnp.bfloat16)


def to_bf16(acc):
    return acc.astype(jnp.bfloat16)


def halo(edge_of):
    return shifted(edge_of(-1), "quarter", 1), shifted(edge_of(0), "quarter", -1)


def convolve(groups, rims, weight, finish, lo, hi, band):
    row_count, channels = rims[0].shape
    col_count = groups[0][0].shape[1]
    segments = []
    first = 0
    for piece in groups[0]:
        segments.append((first, first + piece.shape[0]))
        first += piece.shape[0]
    first_build = max(lo - band, 0)
    builds = len(range(first_build, min(hi + band, row_count), band))
    lag = (lo + band - first_build) // band
    steps = (hi - lo) // band + lag

    def source_map(first, last):
        offset = (first_build - first) // band
        top = (last - first) // band - 1
        return lambda s: (jnp.clip(s + offset, 0, top), 0, 0)

    flat = [piece for segs in groups for piece in segs]
    source_specs = [
        pl.BlockSpec((band, col_count, channels), source_map(*segments[t % len(segments)]))
        for t in range(len(flat))
    ]
    bands = row_count // band
    rim_spec = pl.BlockSpec((1, band, channels), lambda s: (jnp.clip(s + first_build // band, 0, bands - 1), 0, 0))
    padded = (row_count + 2) * col_count
    stacked = weight.reshape(3, 3 * channels, channels)
    kernel = functools.partial(
        conv_kernel,
        segments=tuple(segments),
        parts=len(groups),
        lo=lo,
        band=band,
        first_build=first_build,
        lag=lag,
        finish=finish,
    )
    del builds
    return pl.pallas_call(
        kernel,
        out_shape=jax.ShapeDtypeStruct((hi - lo, col_count, channels), jnp.bfloat16),
        grid=(steps,),
        in_specs=source_specs + [rim_spec, rim_spec, pl.BlockSpec(memory_space=pl.ANY)],
        out_specs=pl.BlockSpec((band, col_count, channels), lambda s: (jnp.maximum(s - lag, 0), 0, 0)),
        scratch_shapes=[
            pltpu.VMEM((padded, 3 * channels), jnp.bfloat16),
            pltpu.VMEM((band * col_count + 16, channels), jnp.float32),
            pltpu.VMEM((3, 3 * channels, channels), weight.dtype),
            pltpu.SemaphoreType.DMA((1,)),
        ],
    )(*flat, *(rim.reshape(bands, band, channels) for rim in rims), stacked)


def attend_kernel(x_ref, wqkv_ref, bias_ref, wout_ref, o_ref, qkv_s, blend_s):
    frames_all, count, channels = x_ref.shape
    head_dim = channels // HEADS
    scale = head_dim ** (-0.5)
    block = min(frames_all, 4)

    def project(f, carry):
        qkv_s[f] = lax.dot_general(
            wqkv_ref[...], x_ref[f], (((1,), (1,)), ((), ())), preferred_element_type=jnp.float32
        ).astype(jnp.bfloat16)
        return carry

    lax.fori_loop(0, frames_all, project, 0, unroll=frames_all <= 4)

    def head_block(h, first):
        frames = pl.ds(first, block)
        queries = qkv_s[frames, pl.ds(h * head_dim, head_dim), :].astype(jnp.float32)
        scores = []
        for g in range(frames_all):
            key_part = qkv_s[g, pl.ds(channels + h * head_dim, head_dim), :].astype(jnp.float32)
            bias = bias_ref[h, g, frames]
            scores.append(jnp.sum(queries * key_part[None], axis=1) * scale + bias)
        top = scores[0]
        for g in range(1, frames_all):
            top = jnp.maximum(top, scores[g])
        weights = [jnp.exp(s - top) for s in scores]
        total = weights[0]
        for g in range(1, frames_all):
            total = total + weights[g]
        blended = None
        for g in range(frames_all):
            value_part = qkv_s[g, pl.ds(2 * channels + h * head_dim, head_dim), :].astype(jnp.float32)
            prob = (weights[g] / total).astype(jnp.bfloat16).astype(jnp.float32)
            term = prob[:, None, :] * value_part[None]
            blended = term if blended is None else blended + term
        blend_s[frames, pl.ds(h * head_dim, head_dim), :] = blended.astype(jnp.bfloat16)

    def frame_block(i, carry):
        for h in range(HEADS):
            head_block(h, i * block)
        return carry

    lax.fori_loop(0, frames_all // block, frame_block, 0, unroll=frames_all <= 4)

    def out_project(f, carry):
        o_ref[f] = lax.dot_general(
            blend_s[f], wout_ref[...], (((0,), (0,)), ((), ())), preferred_element_type=jnp.float32
        ).astype(jnp.bfloat16)
        return carry

    lax.fori_loop(0, frames_all, out_project, 0, unroll=frames_all <= 4)


def attend(grid, qkv_weight, pos_bias, out_weight):
    frames_all, count, channels = grid.shape
    vmem = pl.BlockSpec(memory_space=pltpu.VMEM)
    return pl.pallas_call(
        attend_kernel,
        out_shape=jax.ShapeDtypeStruct((frames_all, count, channels), jnp.bfloat16),
        in_specs=[vmem] * 4,
        out_specs=vmem,
        scratch_shapes=[
            pltpu.VMEM((frames_all, 3 * channels, count), jnp.bfloat16),
            pltpu.VMEM((frames_all, channels, count), jnp.bfloat16),
        ],
    )(grid, qkv_weight.T, pos_bias.transpose(0, 2, 1)[..., None], out_weight)


def body(latents, conv1_weight, qkv_weight, out_weight, pos_bias, conv2_weight):
    frames_dev, row_count, col_count, channels = latents.shape
    frames_all = lax.axis_size("frame")
    tile = latents.reshape(row_count, col_count, channels)
    rims = halo(lambda c: tile[:, c, :])
    half = row_count // 2
    hidden = []
    returned = []
    for lo in (0, half):
        hidden.append(convolve([[tile]], rims, conv1_weight, norm_gelu, lo, lo + half, 12))
    pix_piece = half * col_count // frames_all
    if half % frames_all == 0:
        piece_shape = (frames_all, half // frames_all, col_count, channels)
    else:
        piece_shape = (frames_all, pix_piece, channels)
    for part in hidden:
        pieces = lax.all_to_all(part.reshape(piece_shape), "frame", split_axis=0, concat_axis=0, tiled=True)
        attended = attend(pieces.reshape(frames_all, pix_piece, channels), qkv_weight, pos_bias, out_weight)
        back = lax.all_to_all(attended.reshape(piece_shape), "frame", split_axis=0, concat_axis=0, tiled=True)
        returned.append(back.reshape(half, col_count, channels))

    def joined_edge(c):
        summed = [h[:, c, :].astype(jnp.float32) + r[:, c, :].astype(jnp.float32) for h, r in zip(hidden, returned)]
        return jnp.concatenate(summed, axis=0).astype(jnp.bfloat16)

    second = convolve([hidden, returned], halo(joined_edge), conv2_weight, to_bf16, 0, row_count, 12)
    return second.reshape(frames_dev, row_count, col_count, channels)


def solution(mesh):
    groups = mesh.shape["groups"]
    frames_all = mesh.shape["frame"] // 4
    split_mesh = Mesh(
        mesh.devices.reshape(groups, 4, frames_all), ("groups", "quarter", "frame")
    )
    tiles = P(("groups", "quarter", "frame"), None, None, None)
    placed = (tiles, P(), P(), P(), P(), P())
    return jax.shard_map(
        body,
        mesh=split_mesh,
        in_specs=placed,
        out_specs=tiles,
        check_vma=False,
    )
```

```python
import functools

import jax
import jax.numpy as jnp
from jax import lax
from jax.experimental import pallas as pl
from jax.experimental.pallas import tpu as pltpu
from jax.sharding import Mesh, PartitionSpec as P

HEADS = 5


def shifted(block, axis, distance):
    size = lax.axis_size(axis)
    route = [((i - distance) % size, i) for i in range(size)]
    moved = lax.ppermute(block, axis, route)
    source = lax.axis_index(axis) - distance
    inside = (source >= 0) & (source < size)
    return jnp.where(inside, moved, jnp.zeros_like(moved))


def conv_kernel(*refs, layout, lo, hi, band, finish):
    count = sum(len(segments) for segments in layout)
    flat = refs[:count]
    left_ref, right_ref, w_ref, o_ref, slab, shift_s = refs[count:]
    row_count = left_ref.shape[0]
    _, col_count, channels = o_ref.shape
    lanes = slab.shape[1] // 3
    span = band * col_count
    padded_rows = slab.shape[0]
    slab[pl.ds(0, col_count)] = jnp.zeros((col_count, slab.shape[1]), jnp.bfloat16)
    slab[pl.ds(padded_rows - col_count, col_count)] = jnp.zeros((col_count, slab.shape[1]), jnp.bfloat16)
    column = lax.broadcasted_iota(jnp.int32, (band, col_count, channels), 1)
    addends = []
    at = 0
    for segments in layout:
        addends.append(list(zip(flat[at : at + len(segments)], segments)))
        at += len(segments)

    def rows_of(ref_list, r0):
        for ref, (first, last) in ref_list:
            if first <= r0 < last:
                return ref[pl.ds(r0 - first, band)]

    for r0 in range(max(lo - band, 0), min(hi + band, row_count), band):
        block = rows_of(addends[0], r0).astype(jnp.float32)
        for extra in addends[1:]:
            block = block + rows_of(extra, r0).astype(jnp.float32)
        block = block.astype(jnp.bfloat16)
        shift_s[pl.ds(8, span)] = block.astype(jnp.float32).reshape(span, channels)
        before = shift_s[pl.ds(7, span)].reshape(band, col_count, channels)
        after = shift_s[pl.ds(9, span)].reshape(band, col_count, channels)
        rim_l = left_ref[pl.ds(r0, band)].astype(jnp.float32)[:, None, :]
        rim_r = right_ref[pl.ds(r0, band)].astype(jnp.float32)[:, None, :]
        before = jnp.where(column == 0, rim_l, before)
        after = jnp.where(column == col_count - 1, rim_r, after)
        rows = pl.ds((r0 + 1) * col_count, span)
        slab[rows, pl.ds(0, channels)] = before.reshape(span, channels).astype(jnp.bfloat16)
        slab[rows, pl.ds(lanes, channels)] = block.reshape(span, channels)
        slab[rows, pl.ds(2 * lanes, channels)] = after.reshape(span, channels).astype(jnp.bfloat16)

    for r0 in range(lo, hi, band):
        acc = None
        for a in range(3):
            rows = pl.ds((r0 + a) * col_count, span)
            term = jnp.dot(slab[rows, :], w_ref[a], preferred_element_type=jnp.float32)
            acc = term if acc is None else acc + term
        o_ref[pl.ds(r0 - lo, band)] = finish(acc).reshape(band, col_count, channels)


def norm_gelu(first):
    normed = first * lax.rsqrt(jnp.mean(first * first, axis=-1, keepdims=True) + 1e-06)
    return jax.nn.gelu(normed, approximate=True).astype(jnp.bfloat16)


def to_bf16(acc):
    return acc.astype(jnp.bfloat16)


def halo(edge_of):
    return shifted(edge_of(-1), "quarter", 1), shifted(edge_of(0), "quarter", -1)


def convolve(groups, rims, weight, finish, lo, hi, band):
    row_count, channels = rims[0].shape
    col_count = groups[0][0].shape[1]
    layout = []
    for segments in groups:
        spans = []
        first = 0
        for piece in segments:
            spans.append((first, first + piece.shape[0]))
            first += piece.shape[0]
        layout.append(tuple(spans))
    flat = [piece for segments in groups for piece in segments]
    vmem = pl.BlockSpec(memory_space=pltpu.VMEM)
    padded = (row_count + 2) * col_count
    stacked = weight.reshape(3, 3 * channels, channels)
    return pl.pallas_call(
        functools.partial(conv_kernel, layout=tuple(layout), lo=lo, hi=hi, band=band, finish=finish),
        out_shape=jax.ShapeDtypeStruct((hi - lo, col_count, channels), jnp.bfloat16),
        in_specs=[vmem] * (len(flat) + 3),
        out_specs=vmem,
        scratch_shapes=[
            pltpu.VMEM((padded, 3 * channels), jnp.bfloat16),
            pltpu.VMEM((band * col_count + 16, channels), jnp.float32),
        ],
    )(*flat, *rims, stacked)


def attend_kernel(x_ref, wqkv_ref, bias_ref, wout_ref, o_ref, qkv_s, blend_s):
    frames_all, count, channels = x_ref.shape
    head_dim = channels // HEADS
    scale = head_dim ** (-0.5)
    block = min(frames_all, 4)

    def project(f, carry):
        qkv_s[f] = lax.dot_general(
            wqkv_ref[...], x_ref[f], (((1,), (1,)), ((), ())), preferred_element_type=jnp.float32
        ).astype(jnp.bfloat16)
        return carry

    lax.fori_loop(0, frames_all, project, 0, unroll=frames_all <= 4)

    def head_block(h, first):
        frames = pl.ds(first, block)
        queries = qkv_s[frames, pl.ds(h * head_dim, head_dim), :].astype(jnp.float32)
        scores = []
        for g in range(frames_all):
            key_part = qkv_s[g, pl.ds(channels + h * head_dim, head_dim), :].astype(jnp.float32)
            bias = bias_ref[h, g, frames]
            scores.append(jnp.sum(queries * key_part[None], axis=1) * scale + bias)
        top = scores[0]
        for g in range(1, frames_all):
            top = jnp.maximum(top, scores[g])
        weights = [jnp.exp(s - top) for s in scores]
        total = weights[0]
        for g in range(1, frames_all):
            total = total + weights[g]
        blended = None
        for g in range(frames_all):
            value_part = qkv_s[g, pl.ds(2 * channels + h * head_dim, head_dim), :].astype(jnp.float32)
            prob = (weights[g] / total).astype(jnp.bfloat16).astype(jnp.float32)
            term = prob[:, None, :] * value_part[None]
            blended = term if blended is None else blended + term
        blend_s[frames, pl.ds(h * head_dim, head_dim), :] = blended.astype(jnp.bfloat16)

    def frame_block(i, carry):
        for h in range(HEADS):
            head_block(h, i * block)
        return carry

    lax.fori_loop(0, frames_all // block, frame_block, 0, unroll=frames_all <= 4)

    def out_project(f, carry):
        o_ref[f] = lax.dot_general(
            blend_s[f], wout_ref[...], (((0,), (0,)), ((), ())), preferred_element_type=jnp.float32
        ).astype(jnp.bfloat16)
        return carry

    lax.fori_loop(0, frames_all, out_project, 0, unroll=frames_all <= 4)


def attend(grid, qkv_weight, pos_bias, out_weight):
    frames_all, count, channels = grid.shape
    vmem = pl.BlockSpec(memory_space=pltpu.VMEM)
    return pl.pallas_call(
        attend_kernel,
        out_shape=jax.ShapeDtypeStruct((frames_all, count, channels), jnp.bfloat16),
        in_specs=[vmem] * 4,
        out_specs=vmem,
        scratch_shapes=[
            pltpu.VMEM((frames_all, 3 * channels, count), jnp.bfloat16),
            pltpu.VMEM((frames_all, channels, count), jnp.bfloat16),
        ],
    )(grid, qkv_weight.T, pos_bias.transpose(0, 2, 1)[..., None], out_weight)


def body(latents, conv1_weight, qkv_weight, out_weight, pos_bias, conv2_weight):
    frames_dev, row_count, col_count, channels = latents.shape
    frames_all = lax.axis_size("frame")
    tile = latents.reshape(row_count, col_count, channels)
    flat_tile = tile.reshape(row_count * col_count, channels)
    rims = halo(lambda c: flat_tile[c % col_count :: col_count])
    half = row_count // 2
    hidden = []
    returned = []
    for lo in (0, half):
        hidden.append(convolve([[tile]], rims, conv1_weight, norm_gelu, lo, lo + half, 12))
    pix_piece = half * col_count // frames_all
    if half % frames_all == 0:
        piece_shape = (frames_all, half // frames_all, col_count, channels)
    else:
        piece_shape = (frames_all, pix_piece, channels)
    for part in hidden:
        pieces = lax.all_to_all(part.reshape(piece_shape), "frame", split_axis=0, concat_axis=0, tiled=True)
        attended = attend(pieces.reshape(frames_all, pix_piece, channels), qkv_weight, pos_bias, out_weight)
        back = lax.all_to_all(attended.reshape(piece_shape), "frame", split_axis=0, concat_axis=0, tiled=True)
        returned.append(back.reshape(half, col_count, channels))

    def joined_edge(c):
        summed = [h[:, c, :].astype(jnp.float32) + r[:, c, :].astype(jnp.float32) for h, r in zip(hidden, returned)]
        return jnp.concatenate(summed, axis=0).astype(jnp.bfloat16)

    second = convolve([hidden, returned], halo(joined_edge), conv2_weight, to_bf16, 0, row_count, 12)
    return second.reshape(frames_dev, row_count, col_count, channels)


def solution(mesh):
    groups = mesh.shape["groups"]
    frames_all = mesh.shape["frame"] // 4
    split_mesh = Mesh(
        mesh.devices.reshape(groups, 4, frames_all), ("groups", "quarter", "frame")
    )
    tiles = P(("groups", "quarter", "frame"), None, None, None)
    placed = (tiles, P(), P(), P(), P(), P())
    return jax.shard_map(
        body,
        mesh=split_mesh,
        in_specs=placed,
        out_specs=tiles,
        check_vma=False,
    )
```

```python
import functools

import jax
import jax.numpy as jnp
from jax import lax
from jax.experimental import pallas as pl
from jax.experimental.pallas import tpu as pltpu
from jax.sharding import Mesh, PartitionSpec as P

HEADS = 5


def shifted(block, axis, distance):
    size = lax.axis_size(axis)
    route = [((i - distance) % size, i) for i in range(size)]
    moved = lax.ppermute(block, axis, route)
    source = lax.axis_index(axis) - distance
    inside = (source >= 0) & (source < size)
    return jnp.where(inside, moved, jnp.zeros_like(moved))


def conv_kernel(*refs, layout, lo, hi, finish):
    count = sum(len(segments) for segments in layout)
    flat = refs[:count]
    left_ref, right_ref, w_ref, o_ref, slab, shift_s = refs[count:]
    row_count = left_ref.shape[0]
    _, col_count, channels = o_ref.shape
    lanes = slab.shape[1] // 3
    band = 12
    span = band * col_count
    padded_rows = slab.shape[0]
    slab[pl.ds(0, col_count)] = jnp.zeros((col_count, slab.shape[1]), jnp.bfloat16)
    slab[pl.ds(padded_rows - col_count, col_count)] = jnp.zeros((col_count, slab.shape[1]), jnp.bfloat16)
    column = lax.broadcasted_iota(jnp.int32, (band, col_count, channels), 1)
    addends = []
    at = 0
    for segments in layout:
        addends.append(list(zip(flat[at : at + len(segments)], segments)))
        at += len(segments)

    def rows_of(ref_list, r0):
        for ref, (first, last) in ref_list:
            if first <= r0 < last:
                return ref[pl.ds(r0 - first, band)]

    for r0 in range(max(lo - band, 0), min(hi + band, row_count), band):
        block = rows_of(addends[0], r0).astype(jnp.float32)
        for extra in addends[1:]:
            block = block + rows_of(extra, r0).astype(jnp.float32)
        block = block.astype(jnp.bfloat16)
        shift_s[pl.ds(8, span)] = block.astype(jnp.float32).reshape(span, channels)
        before = shift_s[pl.ds(7, span)].reshape(band, col_count, channels)
        after = shift_s[pl.ds(9, span)].reshape(band, col_count, channels)
        rim_l = left_ref[pl.ds(r0, band)].astype(jnp.float32)[:, None, :]
        rim_r = right_ref[pl.ds(r0, band)].astype(jnp.float32)[:, None, :]
        before = jnp.where(column == 0, rim_l, before)
        after = jnp.where(column == col_count - 1, rim_r, after)
        rows = pl.ds((r0 + 1) * col_count, span)
        slab[rows, pl.ds(0, channels)] = before.reshape(span, channels).astype(jnp.bfloat16)
        slab[rows, pl.ds(lanes, channels)] = block.reshape(span, channels)
        slab[rows, pl.ds(2 * lanes, channels)] = after.reshape(span, channels).astype(jnp.bfloat16)

    for r0 in range(lo, hi, band):
        acc = None
        for a in range(3):
            rows = pl.ds((r0 + a) * col_count, span)
            term = jnp.dot(slab[rows, :], w_ref[a], preferred_element_type=jnp.float32)
            acc = term if acc is None else acc + term
        o_ref[pl.ds(r0 - lo, band)] = finish(acc).reshape(band, col_count, channels)


def norm_gelu(first):
    normed = first * lax.rsqrt(jnp.mean(first * first, axis=-1, keepdims=True) + 1e-06)
    return jax.nn.gelu(normed, approximate=True).astype(jnp.bfloat16)


def to_bf16(acc):
    return acc.astype(jnp.bfloat16)


def halo(edge_of):
    return shifted(edge_of(-1), "quarter", 1), shifted(edge_of(0), "quarter", -1)


def convolve(groups, rims, weight, finish, lo, hi):
    row_count, channels = rims[0].shape
    col_count = groups[0][0].shape[1]
    layout = []
    for segments in groups:
        spans = []
        first = 0
        for piece in segments:
            spans.append((first, first + piece.shape[0]))
            first += piece.shape[0]
        layout.append(tuple(spans))
    flat = [piece for segments in groups for piece in segments]
    vmem = pl.BlockSpec(memory_space=pltpu.VMEM)
    padded = (row_count + 2) * col_count
    stacked = weight.reshape(3, 3 * channels, channels)
    return pl.pallas_call(
        functools.partial(conv_kernel, layout=tuple(layout), lo=lo, hi=hi, finish=finish),
        out_shape=jax.ShapeDtypeStruct((hi - lo, col_count, channels), jnp.bfloat16),
        in_specs=[vmem] * (len(flat) + 3),
        out_specs=vmem,
        scratch_shapes=[
            pltpu.VMEM((padded, 3 * channels), jnp.bfloat16),
            pltpu.VMEM((12 * col_count + 16, channels), jnp.float32),
        ],
    )(*flat, *rims, stacked)


def attend_kernel(x_ref, wqkv_ref, bias_ref, wout_ref, o_ref, qkv_s, blend_s):
    frames_all, count, channels = x_ref.shape
    head_dim = channels // HEADS
    scale = head_dim ** (-0.5)
    block = min(frames_all, 4)

    def project(f, carry):
        qkv_s[f] = lax.dot_general(
            wqkv_ref[...], x_ref[f], (((1,), (1,)), ((), ())), preferred_element_type=jnp.float32
        ).astype(jnp.bfloat16)
        return carry

    lax.fori_loop(0, frames_all, project, 0, unroll=frames_all <= 4)

    def head_block(h, first):
        frames = pl.ds(first, block)
        queries = qkv_s[frames, pl.ds(h * head_dim, head_dim), :].astype(jnp.float32)
        scores = []
        for g in range(frames_all):
            key_part = qkv_s[g, pl.ds(channels + h * head_dim, head_dim), :].astype(jnp.float32)
            bias = bias_ref[h, g, frames]
            scores.append(jnp.sum(queries * key_part[None], axis=1) * scale + bias)
        top = scores[0]
        for g in range(1, frames_all):
            top = jnp.maximum(top, scores[g])
        weights = [jnp.exp(s - top) for s in scores]
        total = weights[0]
        for g in range(1, frames_all):
            total = total + weights[g]
        blended = None
        for g in range(frames_all):
            value_part = qkv_s[g, pl.ds(2 * channels + h * head_dim, head_dim), :].astype(jnp.float32)
            prob = (weights[g] / total).astype(jnp.bfloat16).astype(jnp.float32)
            term = prob[:, None, :] * value_part[None]
            blended = term if blended is None else blended + term
        blend_s[frames, pl.ds(h * head_dim, head_dim), :] = blended.astype(jnp.bfloat16)

    def frame_block(i, carry):
        for h in range(HEADS):
            head_block(h, i * block)
        return carry

    lax.fori_loop(0, frames_all // block, frame_block, 0, unroll=frames_all <= 4)

    def out_project(f, carry):
        o_ref[f] = lax.dot_general(
            blend_s[f], wout_ref[...], (((0,), (0,)), ((), ())), preferred_element_type=jnp.float32
        ).astype(jnp.bfloat16)
        return carry

    lax.fori_loop(0, frames_all, out_project, 0, unroll=frames_all <= 4)


def attend(grid, qkv_weight, pos_bias, out_weight):
    frames_all, count, channels = grid.shape
    vmem = pl.BlockSpec(memory_space=pltpu.VMEM)
    return pl.pallas_call(
        attend_kernel,
        out_shape=jax.ShapeDtypeStruct((frames_all, count, channels), jnp.bfloat16),
        in_specs=[vmem] * 4,
        out_specs=vmem,
        scratch_shapes=[
            pltpu.VMEM((frames_all, 3 * channels, count), jnp.bfloat16),
            pltpu.VMEM((frames_all, channels, count), jnp.bfloat16),
        ],
    )(grid, qkv_weight.T, pos_bias.transpose(0, 2, 1)[..., None], out_weight)


def rotated_attention(part, qkv_weight, pos_bias, out_weight):
    frames_all = lax.axis_size("frame")
    me = lax.axis_index("frame")
    rows, col_count, channels = part.shape
    band = rows // frames_all
    got = []
    for s in range(frames_all):
        piece = lax.dynamic_slice_in_dim(part, ((me + s) % frames_all) * band, band, axis=0)
        if s:
            piece = lax.ppermute(piece, "frame", [(i, (i + s) % frames_all) for i in range(frames_all)])
        got.append(piece)
    grid = jnp.stack(got).reshape(frames_all, band * col_count, channels)
    source = (me - jnp.arange(frames_all)) % frames_all
    bias = jnp.take(jnp.take(pos_bias, source, axis=1), source, axis=2)
    attended = attend(grid, qkv_weight, bias, out_weight).reshape(frames_all, band, col_count, channels)
    back = []
    for s in range(frames_all):
        piece = attended[s]
        if s:
            piece = lax.ppermute(piece, "frame", [(i, (i - s) % frames_all) for i in range(frames_all)])
        back.append(piece)
    order = (jnp.arange(frames_all) - me) % frames_all
    return jnp.take(jnp.stack(back), order, axis=0).reshape(rows, col_count, channels)


def body(latents, conv1_weight, qkv_weight, out_weight, pos_bias, conv2_weight):
    frames_dev, row_count, col_count, channels = latents.shape
    frames_all = lax.axis_size("frame")
    tile = latents.reshape(row_count, col_count, channels)
    rims = halo(lambda c: tile[:, c, :])
    half = row_count // 2
    hidden = []
    returned = []
    for lo in (0, half):
        hidden.append(convolve([[tile]], rims, conv1_weight, norm_gelu, lo, lo + half))
    pix_piece = half * col_count // frames_all
    if half % frames_all == 0:
        piece_shape = (frames_all, half // frames_all, col_count, channels)
    else:
        piece_shape = (frames_all, pix_piece, channels)
    rotate = frames_all <= 4 and half % frames_all == 0
    for part in hidden:
        if rotate:
            returned.append(rotated_attention(part, qkv_weight, pos_bias, out_weight))
            continue
        pieces = lax.all_to_all(part.reshape(piece_shape), "frame", split_axis=0, concat_axis=0, tiled=True)
        attended = attend(pieces.reshape(frames_all, pix_piece, channels), qkv_weight, pos_bias, out_weight)
        back = lax.all_to_all(attended.reshape(piece_shape), "frame", split_axis=0, concat_axis=0, tiled=True)
        returned.append(back.reshape(half, col_count, channels))

    def joined_edge(c):
        summed = [h[:, c, :].astype(jnp.float32) + r[:, c, :].astype(jnp.float32) for h, r in zip(hidden, returned)]
        return jnp.concatenate(summed, axis=0).astype(jnp.bfloat16)

    second = convolve([hidden, returned], halo(joined_edge), conv2_weight, to_bf16, 0, row_count)
    return second.reshape(frames_dev, row_count, col_count, channels)


def solution(mesh):
    groups = mesh.shape["groups"]
    frames_all = mesh.shape["frame"] // 4
    split_mesh = Mesh(
        mesh.devices.reshape(groups, 4, frames_all), ("groups", "quarter", "frame")
    )
    tiles = P(("groups", "quarter", "frame"), None, None, None)
    placed = (tiles, P(), P(), P(), P(), P())
    return jax.shard_map(
        body,
        mesh=split_mesh,
        in_specs=placed,
        out_specs=tiles,
        check_vma=False,
    )
```

```python
import functools

import jax
import jax.numpy as jnp
from jax import lax
from jax.experimental import pallas as pl
from jax.experimental.pallas import tpu as pltpu
from jax.sharding import Mesh, PartitionSpec as P

HEADS = 5


def shifted(block, axis, distance):
    size = lax.axis_size(axis)
    route = [((i - distance) % size, i) for i in range(size)]
    moved = lax.ppermute(block, axis, route)
    source = lax.axis_index(axis) - distance
    inside = (source >= 0) & (source < size)
    return jnp.where(inside, moved, jnp.zeros_like(moved))


def conv_kernel(*refs, layout, lo, hi, finish):
    count = sum(len(segments) for segments in layout)
    flat = refs[:count]
    left_ref, right_ref, w_ref, o_ref, slab, shift_s = refs[count:]
    row_count = left_ref.shape[0]
    _, col_count, channels = o_ref.shape
    lanes = slab.shape[1] // 3
    band = 12
    span = band * col_count
    padded_rows = slab.shape[0]
    slab[pl.ds(0, col_count)] = jnp.zeros((col_count, slab.shape[1]), jnp.bfloat16)
    slab[pl.ds(padded_rows - col_count, col_count)] = jnp.zeros((col_count, slab.shape[1]), jnp.bfloat16)
    column = lax.broadcasted_iota(jnp.int32, (band, col_count, channels), 1)
    addends = []
    at = 0
    for segments in layout:
        addends.append(list(zip(flat[at : at + len(segments)], segments)))
        at += len(segments)

    def rows_of(ref_list, r0):
        for ref, (first, last) in ref_list:
            if first <= r0 < last:
                return ref[pl.ds(r0 - first, band)]

    for r0 in range(max(lo - band, 0), min(hi + band, row_count), band):
        block = rows_of(addends[0], r0).astype(jnp.float32)
        for extra in addends[1:]:
            block = block + rows_of(extra, r0).astype(jnp.float32)
        block = block.astype(jnp.bfloat16)
        shift_s[pl.ds(8, span)] = block.astype(jnp.float32).reshape(span, channels)
        before = shift_s[pl.ds(7, span)].reshape(band, col_count, channels)
        after = shift_s[pl.ds(9, span)].reshape(band, col_count, channels)
        rim_l = left_ref[pl.ds(r0, band)].astype(jnp.float32)[:, None, :]
        rim_r = right_ref[pl.ds(r0, band)].astype(jnp.float32)[:, None, :]
        before = jnp.where(column == 0, rim_l, before)
        after = jnp.where(column == col_count - 1, rim_r, after)
        rows = pl.ds((r0 + 1) * col_count, span)
        slab[rows, pl.ds(0, channels)] = before.reshape(span, channels).astype(jnp.bfloat16)
        slab[rows, pl.ds(lanes, channels)] = block.reshape(span, channels)
        slab[rows, pl.ds(2 * lanes, channels)] = after.reshape(span, channels).astype(jnp.bfloat16)

    for r0 in range(lo, hi, band):
        acc = None
        for a in range(3):
            rows = pl.ds((r0 + a) * col_count, span)
            term = jnp.dot(slab[rows, :], w_ref[a], preferred_element_type=jnp.float32)
            acc = term if acc is None else acc + term
        o_ref[pl.ds(r0 - lo, band)] = finish(acc).reshape(band, col_count, channels)


def norm_gelu(first):
    normed = first * lax.rsqrt(jnp.mean(first * first, axis=-1, keepdims=True) + 1e-06)
    return jax.nn.gelu(normed, approximate=True).astype(jnp.bfloat16)


def to_bf16(acc):
    return acc.astype(jnp.bfloat16)


def halo(edge_of):
    return shifted(edge_of(-1), "quarter", 1), shifted(edge_of(0), "quarter", -1)


def convolve(groups, rims, weight, finish, lo, hi):
    row_count, channels = rims[0].shape
    col_count = groups[0][0].shape[1]
    layout = []
    for segments in groups:
        spans = []
        first = 0
        for piece in segments:
            spans.append((first, first + piece.shape[0]))
            first += piece.shape[0]
        layout.append(tuple(spans))
    flat = [piece for segments in groups for piece in segments]
    vmem = pl.BlockSpec(memory_space=pltpu.VMEM)
    padded = (row_count + 2) * col_count
    stacked = weight.reshape(3, 3 * channels, channels)
    return pl.pallas_call(
        functools.partial(conv_kernel, layout=tuple(layout), lo=lo, hi=hi, finish=finish),
        out_shape=jax.ShapeDtypeStruct((hi - lo, col_count, channels), jnp.bfloat16),
        in_specs=[vmem] * (len(flat) + 3),
        out_specs=vmem,
        scratch_shapes=[
            pltpu.VMEM((padded, 3 * channels), jnp.bfloat16),
            pltpu.VMEM((12 * col_count + 16, channels), jnp.float32),
        ],
    )(*flat, *rims, stacked)


def attend_kernel(x_ref, wqkv_ref, bias_ref, wout_ref, o_ref, qkv_s, blend_s):
    frames_all, count, channels = x_ref.shape
    head_dim = channels // HEADS
    scale = head_dim ** (-0.5)
    block = min(frames_all, 4)

    def project(f, carry):
        qkv_s[f] = lax.dot_general(
            wqkv_ref[...], x_ref[f], (((1,), (1,)), ((), ())), preferred_element_type=jnp.float32
        ).astype(jnp.bfloat16)
        return carry

    lax.fori_loop(0, frames_all, project, 0, unroll=frames_all <= 4)

    def head_block(h, first):
        frames = pl.ds(first, block)
        queries = qkv_s[frames, pl.ds(h * head_dim, head_dim), :].astype(jnp.float32)
        scores = []
        for g in range(frames_all):
            key_part = qkv_s[g, pl.ds(channels + h * head_dim, head_dim), :].astype(jnp.float32)
            bias = bias_ref[h, g, frames]
            scores.append(jnp.sum(queries * key_part[None], axis=1) * scale + bias)
        top = scores[0]
        for g in range(1, frames_all):
            top = jnp.maximum(top, scores[g])
        weights = [jnp.exp(s - top) for s in scores]
        total = weights[0]
        for g in range(1, frames_all):
            total = total + weights[g]
        blended = None
        for g in range(frames_all):
            value_part = qkv_s[g, pl.ds(2 * channels + h * head_dim, head_dim), :].astype(jnp.float32)
            prob = (weights[g] / total).astype(jnp.bfloat16).astype(jnp.float32)
            term = prob[:, None, :] * value_part[None]
            blended = term if blended is None else blended + term
        blend_s[frames, pl.ds(h * head_dim, head_dim), :] = blended.astype(jnp.bfloat16)

    def frame_block(i, carry):
        for h in range(HEADS):
            head_block(h, i * block)
        return carry

    lax.fori_loop(0, frames_all // block, frame_block, 0, unroll=frames_all <= 4)

    def out_project(f, carry):
        o_ref[f] = lax.dot_general(
            blend_s[f], wout_ref[...], (((0,), (0,)), ((), ())), preferred_element_type=jnp.float32
        ).astype(jnp.bfloat16)
        return carry

    lax.fori_loop(0, frames_all, out_project, 0, unroll=frames_all <= 4)


def attend(grid, qkv_weight, pos_bias, out_weight):
    frames_all, count, channels = grid.shape
    vmem = pl.BlockSpec(memory_space=pltpu.VMEM)
    return pl.pallas_call(
        attend_kernel,
        out_shape=jax.ShapeDtypeStruct((frames_all, count, channels), jnp.bfloat16),
        in_specs=[vmem] * 4,
        out_specs=vmem,
        scratch_shapes=[
            pltpu.VMEM((frames_all, 3 * channels, count), jnp.bfloat16),
            pltpu.VMEM((frames_all, channels, count), jnp.bfloat16),
        ],
    )(grid, qkv_weight.T, pos_bias.transpose(0, 2, 1)[..., None], out_weight)


def rotated_attention(source, lo, rows, qkv_weight, pos_bias, out_weight):
    frames_all = lax.axis_size("frame")
    me = lax.axis_index("frame")
    _, col_count, channels = source.shape
    band = rows // frames_all
    got = []
    for s in range(frames_all):
        piece = lax.dynamic_slice_in_dim(source, lo + ((me + s) % frames_all) * band, band, axis=0)
        if s:
            piece = lax.ppermute(piece, "frame", [(i, (i + s) % frames_all) for i in range(frames_all)])
        got.append(piece)
    grid = jnp.stack(got).reshape(frames_all, band * col_count, channels)
    source = (me - jnp.arange(frames_all)) % frames_all
    bias = jnp.take(jnp.take(pos_bias, source, axis=1), source, axis=2)
    attended = attend(grid, qkv_weight, bias, out_weight).reshape(frames_all, band, col_count, channels)
    back = []
    for s in range(frames_all):
        piece = attended[s]
        if s:
            piece = lax.ppermute(piece, "frame", [(i, (i - s) % frames_all) for i in range(frames_all)])
        back.append(piece)
    order = (jnp.arange(frames_all) - me) % frames_all
    return jnp.take(jnp.stack(back), order, axis=0).reshape(rows, col_count, channels)


def body(latents, conv1_weight, qkv_weight, out_weight, pos_bias, conv2_weight):
    frames_dev, row_count, col_count, channels = latents.shape
    frames_all = lax.axis_size("frame")
    tile = latents.reshape(row_count, col_count, channels)
    rims = halo(lambda c: tile[:, c, :])
    half = row_count // 2
    returned = []
    rotate = frames_all <= 4 and half % frames_all == 0
    if rotate:
        whole = convolve([[tile]], rims, conv1_weight, norm_gelu, 0, row_count)
        for lo in (0, half):
            returned.append(rotated_attention(whole, lo, half, qkv_weight, pos_bias, out_weight))
        hidden_rows = [whole]
        hidden = [whole[:half], whole[half:]]
    else:
        hidden = [convolve([[tile]], rims, conv1_weight, norm_gelu, lo, lo + half) for lo in (0, half)]
        hidden_rows = hidden
    pix_piece = half * col_count // frames_all
    if half % frames_all == 0:
        piece_shape = (frames_all, half // frames_all, col_count, channels)
    else:
        piece_shape = (frames_all, pix_piece, channels)
    for part in hidden:
        if rotate:
            break
        pieces = lax.all_to_all(part.reshape(piece_shape), "frame", split_axis=0, concat_axis=0, tiled=True)
        attended = attend(pieces.reshape(frames_all, pix_piece, channels), qkv_weight, pos_bias, out_weight)
        back = lax.all_to_all(attended.reshape(piece_shape), "frame", split_axis=0, concat_axis=0, tiled=True)
        returned.append(back.reshape(half, col_count, channels))

    def joined_edge(c):
        summed = [h[:, c, :].astype(jnp.float32) + r[:, c, :].astype(jnp.float32) for h, r in zip(hidden, returned)]
        return jnp.concatenate(summed, axis=0).astype(jnp.bfloat16)

    second = convolve([hidden_rows, returned], halo(joined_edge), conv2_weight, to_bf16, 0, row_count)
    return second.reshape(frames_dev, row_count, col_count, channels)


def solution(mesh):
    groups = mesh.shape["groups"]
    frames_all = mesh.shape["frame"] // 4
    split_mesh = Mesh(
        mesh.devices.reshape(groups, 4, frames_all), ("groups", "quarter", "frame")
    )
    tiles = P(("groups", "quarter", "frame"), None, None, None)
    placed = (tiles, P(), P(), P(), P(), P())
    return jax.shard_map(
        body,
        mesh=split_mesh,
        in_specs=placed,
        out_specs=tiles,
        check_vma=False,
    )
```

```python
import functools

import jax
import jax.numpy as jnp
from jax import lax
from jax.experimental import pallas as pl
from jax.experimental.pallas import tpu as pltpu
from jax.sharding import Mesh, PartitionSpec as P

HEADS = 5


def shifted(block, axis, distance):
    size = lax.axis_size(axis)
    route = [((i - distance) % size, i) for i in range(size)]
    moved = lax.ppermute(block, axis, route)
    source = lax.axis_index(axis) - distance
    inside = (source >= 0) & (source < size)
    return jnp.where(inside, moved, jnp.zeros_like(moved))


def conv_kernel(*refs, layout, lo, hi, finish):
    count = sum(len(segments) for segments in layout)
    flat = refs[:count]
    left_ref, right_ref, w_ref, o_ref, slab, shift_s = refs[count:]
    row_count = left_ref.shape[0]
    _, col_count, channels = o_ref.shape
    lanes = slab.shape[1] // 3
    band = 12
    span = band * col_count
    padded_rows = slab.shape[0]
    slab[pl.ds(0, col_count)] = jnp.zeros((col_count, slab.shape[1]), jnp.bfloat16)
    slab[pl.ds(padded_rows - col_count, col_count)] = jnp.zeros((col_count, slab.shape[1]), jnp.bfloat16)
    column = lax.broadcasted_iota(jnp.int32, (band, col_count, channels), 1)
    addends = []
    at = 0
    for segments in layout:
        addends.append(list(zip(flat[at : at + len(segments)], segments)))
        at += len(segments)

    def rows_of(ref_list, r0):
        for ref, (first, last) in ref_list:
            if first <= r0 < last:
                return ref[pl.ds(r0 - first, band)]

    for r0 in range(max(lo - band, 0), min(hi + band, row_count), band):
        block = rows_of(addends[0], r0).astype(jnp.float32)
        for extra in addends[1:]:
            block = block + rows_of(extra, r0).astype(jnp.float32)
        block = block.astype(jnp.bfloat16)
        shift_s[pl.ds(8, span)] = block.astype(jnp.float32).reshape(span, channels)
        before = shift_s[pl.ds(7, span)].reshape(band, col_count, channels)
        after = shift_s[pl.ds(9, span)].reshape(band, col_count, channels)
        rim_l = left_ref[pl.ds(r0, band)].astype(jnp.float32)[:, None, :]
        rim_r = right_ref[pl.ds(r0, band)].astype(jnp.float32)[:, None, :]
        before = jnp.where(column == 0, rim_l, before)
        after = jnp.where(column == col_count - 1, rim_r, after)
        rows = pl.ds((r0 + 1) * col_count, span)
        slab[rows, pl.ds(0, channels)] = before.reshape(span, channels).astype(jnp.bfloat16)
        slab[rows, pl.ds(lanes, channels)] = block.reshape(span, channels)
        slab[rows, pl.ds(2 * lanes, channels)] = after.reshape(span, channels).astype(jnp.bfloat16)

    for r0 in range(lo, hi, band):
        acc = None
        for a in range(3):
            rows = pl.ds((r0 + a) * col_count, span)
            term = jnp.dot(slab[rows, :], w_ref[a], preferred_element_type=jnp.float32)
            acc = term if acc is None else acc + term
        o_ref[pl.ds(r0 - lo, band)] = finish(acc).reshape(band, col_count, channels)


def norm_gelu(first):
    normed = first * lax.rsqrt(jnp.mean(first * first, axis=-1, keepdims=True) + 1e-06)
    return jax.nn.gelu(normed, approximate=True).astype(jnp.bfloat16)


def to_bf16(acc):
    return acc.astype(jnp.bfloat16)


def halo(edge_of):
    return shifted(edge_of(-1), "quarter", 1), shifted(edge_of(0), "quarter", -1)


def convolve(groups, rims, weight, finish, lo, hi):
    row_count, channels = rims[0].shape
    col_count = groups[0][0].shape[1]
    layout = []
    for segments in groups:
        spans = []
        first = 0
        for piece in segments:
            spans.append((first, first + piece.shape[0]))
            first += piece.shape[0]
        layout.append(tuple(spans))
    flat = [piece for segments in groups for piece in segments]
    vmem = pl.BlockSpec(memory_space=pltpu.VMEM)
    padded = (row_count + 2) * col_count
    stacked = weight.reshape(3, 3 * channels, channels)
    return pl.pallas_call(
        functools.partial(conv_kernel, layout=tuple(layout), lo=lo, hi=hi, finish=finish),
        out_shape=jax.ShapeDtypeStruct((hi - lo, col_count, channels), jnp.bfloat16),
        in_specs=[vmem] * (len(flat) + 3),
        out_specs=vmem,
        scratch_shapes=[
            pltpu.VMEM((padded, 3 * channels), jnp.bfloat16),
            pltpu.VMEM((12 * col_count + 16, channels), jnp.float32),
        ],
    )(*flat, *rims, stacked)


def attend_kernel(*refs, parts):
    if parts:
        x_refs = refs[:parts]
        wqkv_ref, bias_ref, wout_ref = refs[parts : parts + 3]
        o_refs = refs[parts + 3 : 2 * parts + 3]
        qkv_s, blend_s = refs[2 * parts + 3 :]
        frames_all, _, count = qkv_s.shape
        channels = wout_ref.shape[0]
        for f in range(parts):
            qkv_s[f] = lax.dot_general(
                wqkv_ref[...],
                x_refs[f][...].reshape(count, channels),
                (((1,), (1,)), ((), ())),
                preferred_element_type=jnp.float32,
            ).astype(jnp.bfloat16)
    else:
        x_ref, wqkv_ref, bias_ref, wout_ref, o_ref, qkv_s, blend_s = refs
        frames_all, count, channels = x_ref.shape

        def project(f, carry):
            qkv_s[f] = lax.dot_general(
                wqkv_ref[...], x_ref[f], (((1,), (1,)), ((), ())), preferred_element_type=jnp.float32
            ).astype(jnp.bfloat16)
            return carry

        lax.fori_loop(0, frames_all, project, 0, unroll=frames_all <= 4)
    head_dim = channels // HEADS
    scale = head_dim ** (-0.5)
    block = min(frames_all, 4)

    def head_block(h, first):
        frames = pl.ds(first, block)
        queries = qkv_s[frames, pl.ds(h * head_dim, head_dim), :].astype(jnp.float32)
        scores = []
        for g in range(frames_all):
            key_part = qkv_s[g, pl.ds(channels + h * head_dim, head_dim), :].astype(jnp.float32)
            bias = bias_ref[h, g, frames]
            scores.append(jnp.sum(queries * key_part[None], axis=1) * scale + bias)
        top = scores[0]
        for g in range(1, frames_all):
            top = jnp.maximum(top, scores[g])
        weights = [jnp.exp(s - top) for s in scores]
        total = weights[0]
        for g in range(1, frames_all):
            total = total + weights[g]
        blended = None
        for g in range(frames_all):
            value_part = qkv_s[g, pl.ds(2 * channels + h * head_dim, head_dim), :].astype(jnp.float32)
            prob = (weights[g] / total).astype(jnp.bfloat16).astype(jnp.float32)
            term = prob[:, None, :] * value_part[None]
            blended = term if blended is None else blended + term
        blend_s[frames, pl.ds(h * head_dim, head_dim), :] = blended.astype(jnp.bfloat16)

    def frame_block(i, carry):
        for h in range(HEADS):
            head_block(h, i * block)
        return carry

    lax.fori_loop(0, frames_all // block, frame_block, 0, unroll=frames_all <= 4)

    def out_product(f):
        return lax.dot_general(
            blend_s[f], wout_ref[...], (((0,), (0,)), ((), ())), preferred_element_type=jnp.float32
        ).astype(jnp.bfloat16)

    if parts:
        for f in range(parts):
            o_refs[f][...] = out_product(f).reshape(o_refs[f].shape)
        return

    def out_project(f, carry):
        o_ref[f] = out_product(f)
        return carry

    lax.fori_loop(0, frames_all, out_project, 0, unroll=frames_all <= 4)


def attend_pieces(pieces, qkv_weight, pos_bias, out_weight):
    frames_all = len(pieces)
    band, col_count, channels = pieces[0].shape
    count = band * col_count
    vmem = pl.BlockSpec(memory_space=pltpu.VMEM)
    return pl.pallas_call(
        functools.partial(attend_kernel, parts=frames_all),
        out_shape=tuple(jax.ShapeDtypeStruct(pieces[0].shape, jnp.bfloat16) for _ in pieces),
        in_specs=[vmem] * (frames_all + 3),
        out_specs=tuple(vmem for _ in pieces),
        scratch_shapes=[
            pltpu.VMEM((frames_all, 3 * channels, count), jnp.bfloat16),
            pltpu.VMEM((frames_all, channels, count), jnp.bfloat16),
        ],
    )(*pieces, qkv_weight.T, pos_bias.transpose(0, 2, 1)[..., None], out_weight)


def attend(grid, qkv_weight, pos_bias, out_weight):
    frames_all, count, channels = grid.shape
    vmem = pl.BlockSpec(memory_space=pltpu.VMEM)
    return pl.pallas_call(
        functools.partial(attend_kernel, parts=0),
        out_shape=jax.ShapeDtypeStruct((frames_all, count, channels), jnp.bfloat16),
        in_specs=[vmem] * 4,
        out_specs=vmem,
        scratch_shapes=[
            pltpu.VMEM((frames_all, 3 * channels, count), jnp.bfloat16),
            pltpu.VMEM((frames_all, channels, count), jnp.bfloat16),
        ],
    )(grid, qkv_weight.T, pos_bias.transpose(0, 2, 1)[..., None], out_weight)


def rotated_attention(source, lo, rows, qkv_weight, pos_bias, out_weight):
    frames_all = lax.axis_size("frame")
    me = lax.axis_index("frame")
    _, col_count, channels = source.shape
    band = rows // frames_all
    got = []
    for s in range(frames_all):
        piece = lax.dynamic_slice_in_dim(source, lo + ((me + s) % frames_all) * band, band, axis=0)
        if s:
            piece = lax.ppermute(piece, "frame", [(i, (i + s) % frames_all) for i in range(frames_all)])
        got.append(piece)
    source = (me - jnp.arange(frames_all)) % frames_all
    bias = jnp.take(jnp.take(pos_bias, source, axis=1), source, axis=2)
    attended = attend_pieces(got, qkv_weight, bias, out_weight)
    back = []
    for s in range(frames_all):
        piece = attended[s]
        if s:
            piece = lax.ppermute(piece, "frame", [(i, (i - s) % frames_all) for i in range(frames_all)])
        back.append(piece)
    order = (jnp.arange(frames_all) - me) % frames_all
    return jnp.take(jnp.stack(back), order, axis=0).reshape(rows, col_count, channels)


def body(latents, conv1_weight, qkv_weight, out_weight, pos_bias, conv2_weight):
    frames_dev, row_count, col_count, channels = latents.shape
    frames_all = lax.axis_size("frame")
    tile = latents.reshape(row_count, col_count, channels)
    rims = halo(lambda c: tile[:, c, :])
    half = row_count // 2
    returned = []
    rotate = frames_all <= 4 and half % frames_all == 0
    if rotate:
        whole = convolve([[tile]], rims, conv1_weight, norm_gelu, 0, row_count)
        for lo in (0, half):
            returned.append(rotated_attention(whole, lo, half, qkv_weight, pos_bias, out_weight))
        hidden_rows = [whole]
        hidden = [whole[:half], whole[half:]]
    else:
        hidden = [convolve([[tile]], rims, conv1_weight, norm_gelu, lo, lo + half) for lo in (0, half)]
        hidden_rows = hidden
    pix_piece = half * col_count // frames_all
    if half % frames_all == 0:
        piece_shape = (frames_all, half // frames_all, col_count, channels)
    else:
        piece_shape = (frames_all, pix_piece, channels)
    for part in hidden:
        if rotate:
            break
        pieces = lax.all_to_all(part.reshape(piece_shape), "frame", split_axis=0, concat_axis=0, tiled=True)
        attended = attend(pieces.reshape(frames_all, pix_piece, channels), qkv_weight, pos_bias, out_weight)
        back = lax.all_to_all(attended.reshape(piece_shape), "frame", split_axis=0, concat_axis=0, tiled=True)
        returned.append(back.reshape(half, col_count, channels))

    def joined_edge(c):
        summed = [h[:, c, :].astype(jnp.float32) + r[:, c, :].astype(jnp.float32) for h, r in zip(hidden, returned)]
        return jnp.concatenate(summed, axis=0).astype(jnp.bfloat16)

    second = convolve([hidden_rows, returned], halo(joined_edge), conv2_weight, to_bf16, 0, row_count)
    return second.reshape(frames_dev, row_count, col_count, channels)


def solution(mesh):
    groups = mesh.shape["groups"]
    frames_all = mesh.shape["frame"] // 4
    split_mesh = Mesh(
        mesh.devices.reshape(groups, 4, frames_all), ("groups", "quarter", "frame")
    )
    tiles = P(("groups", "quarter", "frame"), None, None, None)
    placed = (tiles, P(), P(), P(), P(), P())
    return jax.shard_map(
        body,
        mesh=split_mesh,
        in_specs=placed,
        out_specs=tiles,
        check_vma=False,
    )
```

```python
import functools

import jax
import jax.numpy as jnp
from jax import lax
from jax.experimental import pallas as pl
from jax.experimental.pallas import tpu as pltpu
from jax.sharding import Mesh, PartitionSpec as P

HEADS = 5


def shifted(block, axis, distance):
    size = lax.axis_size(axis)
    route = [((i - distance) % size, i) for i in range(size)]
    moved = lax.ppermute(block, axis, route)
    source = lax.axis_index(axis) - distance
    inside = (source >= 0) & (source < size)
    return jnp.where(inside, moved, jnp.zeros_like(moved))


def conv_kernel(*refs, layout, lo, hi, finish):
    count = sum(len(segments) for segments in layout)
    flat = refs[:count]
    left_ref, right_ref, w_ref, o_ref, slab, shift_s = refs[count:]
    row_count = left_ref.shape[0]
    _, col_count, channels = o_ref.shape
    lanes = slab.shape[1] // 3
    band = 12
    span = band * col_count
    padded_rows = slab.shape[0]
    slab[pl.ds(0, col_count)] = jnp.zeros((col_count, slab.shape[1]), jnp.bfloat16)
    slab[pl.ds(padded_rows - col_count, col_count)] = jnp.zeros((col_count, slab.shape[1]), jnp.bfloat16)
    column = lax.broadcasted_iota(jnp.int32, (band, col_count, channels), 1)
    addends = []
    at = 0
    for segments in layout:
        addends.append(list(zip(flat[at : at + len(segments)], segments)))
        at += len(segments)

    def rows_of(ref_list, r0):
        for ref, (first, last) in ref_list:
            if first <= r0 < last:
                return ref[pl.ds(r0 - first, band)]

    for r0 in range(max(lo - band, 0), min(hi + band, row_count), band):
        block = rows_of(addends[0], r0).astype(jnp.float32)
        for extra in addends[1:]:
            block = block + rows_of(extra, r0).astype(jnp.float32)
        block = block.astype(jnp.bfloat16)
        shift_s[pl.ds(8, span)] = block.astype(jnp.float32).reshape(span, channels)
        before = shift_s[pl.ds(7, span)].reshape(band, col_count, channels)
        after = shift_s[pl.ds(9, span)].reshape(band, col_count, channels)
        rim_l = left_ref[pl.ds(r0, band)].astype(jnp.float32)[:, None, :]
        rim_r = right_ref[pl.ds(r0, band)].astype(jnp.float32)[:, None, :]
        before = jnp.where(column == 0, rim_l, before)
        after = jnp.where(column == col_count - 1, rim_r, after)
        rows = pl.ds((r0 + 1) * col_count, span)
        slab[rows, pl.ds(0, channels)] = before.reshape(span, channels).astype(jnp.bfloat16)
        slab[rows, pl.ds(lanes, channels)] = block.reshape(span, channels)
        slab[rows, pl.ds(2 * lanes, channels)] = after.reshape(span, channels).astype(jnp.bfloat16)

    for r0 in range(lo, hi, band):
        acc = None
        for a in range(3):
            rows = pl.ds((r0 + a) * col_count, span)
            term = jnp.dot(slab[rows, :], w_ref[a], preferred_element_type=jnp.float32)
            acc = term if acc is None else acc + term
        o_ref[pl.ds(r0 - lo, band)] = finish(acc).reshape(band, col_count, channels)


def norm_gelu(first):
    normed = first * lax.rsqrt(jnp.mean(first * first, axis=-1, keepdims=True) + 1e-06)
    return jax.nn.gelu(normed, approximate=True).astype(jnp.bfloat16)


def to_bf16(acc):
    return acc.astype(jnp.bfloat16)


def halo(edge_of):
    return shifted(edge_of(-1), "quarter", 1), shifted(edge_of(0), "quarter", -1)


def convolve(groups, rims, weight, finish, lo, hi):
    row_count, channels = rims[0].shape
    col_count = groups[0][0].shape[1]
    layout = []
    for segments in groups:
        spans = []
        first = 0
        for piece in segments:
            spans.append((first, first + piece.shape[0]))
            first += piece.shape[0]
        layout.append(tuple(spans))
    flat = [piece for segments in groups for piece in segments]
    vmem = pl.BlockSpec(memory_space=pltpu.VMEM)
    padded = (row_count + 2) * col_count
    stacked = weight.reshape(3, 3 * channels, channels)
    return pl.pallas_call(
        functools.partial(conv_kernel, layout=tuple(layout), lo=lo, hi=hi, finish=finish),
        out_shape=jax.ShapeDtypeStruct((hi - lo, col_count, channels), jnp.bfloat16),
        in_specs=[vmem] * (len(flat) + 3),
        out_specs=vmem,
        scratch_shapes=[
            pltpu.VMEM((padded, 3 * channels), jnp.bfloat16),
            pltpu.VMEM((12 * col_count + 16, channels), jnp.float32),
        ],
    )(*flat, *rims, stacked)


def attend_kernel(*refs, parts):
    if parts:
        x_refs = refs[:parts]
        wqkv_ref, bias_ref, wout_ref = refs[parts : parts + 3]
        o_refs = refs[parts + 3 : 2 * parts + 3]
        qkv_s, blend_s = refs[2 * parts + 3 :]
        frames_all, _, count = qkv_s.shape
        channels = wout_ref.shape[0]
        for f in range(parts):
            qkv_s[f] = lax.dot_general(
                wqkv_ref[...],
                x_refs[f][...].reshape(count, channels),
                (((1,), (1,)), ((), ())),
                preferred_element_type=jnp.float32,
            ).astype(jnp.bfloat16)
    else:
        x_ref, wqkv_ref, bias_ref, wout_ref, o_ref, qkv_s, blend_s = refs
        frames_all, count, channels = x_ref.shape

        def project(f, carry):
            qkv_s[f] = lax.dot_general(
                wqkv_ref[...], x_ref[f], (((1,), (1,)), ((), ())), preferred_element_type=jnp.float32
            ).astype(jnp.bfloat16)
            return carry

        lax.fori_loop(0, frames_all, project, 0, unroll=frames_all <= 4)
    head_dim = channels // HEADS
    scale = head_dim ** (-0.5)
    block = min(frames_all, 4)

    def head_block(h, first):
        frames = pl.ds(first, block)
        queries = qkv_s[frames, pl.ds(h * head_dim, head_dim), :].astype(jnp.float32)
        scores = []
        for g in range(frames_all):
            key_part = qkv_s[g, pl.ds(channels + h * head_dim, head_dim), :].astype(jnp.float32)
            bias = bias_ref[h, g, frames]
            scores.append(jnp.sum(queries * key_part[None], axis=1) * scale + bias)
        top = scores[0]
        for g in range(1, frames_all):
            top = jnp.maximum(top, scores[g])
        weights = [jnp.exp(s - top) for s in scores]
        total = weights[0]
        for g in range(1, frames_all):
            total = total + weights[g]
        blended = None
        for g in range(frames_all):
            value_part = qkv_s[g, pl.ds(2 * channels + h * head_dim, head_dim), :].astype(jnp.float32)
            prob = (weights[g] / total).astype(jnp.bfloat16).astype(jnp.float32)
            term = prob[:, None, :] * value_part[None]
            blended = term if blended is None else blended + term
        blend_s[frames, pl.ds(h * head_dim, head_dim), :] = blended.astype(jnp.bfloat16)

    def frame_block(i, carry):
        for h in range(HEADS):
            head_block(h, i * block)
        return carry

    lax.fori_loop(0, frames_all // block, frame_block, 0, unroll=frames_all <= 4)

    def out_product(f):
        return lax.dot_general(
            blend_s[f], wout_ref[...], (((0,), (0,)), ((), ())), preferred_element_type=jnp.float32
        ).astype(jnp.bfloat16)

    if parts:
        for f in range(parts):
            o_refs[f][...] = out_product(f).reshape(o_refs[f].shape)
        return

    def out_project(f, carry):
        o_ref[f] = out_product(f)
        return carry

    lax.fori_loop(0, frames_all, out_project, 0, unroll=frames_all <= 4)


def attend_pieces(pieces, qkv_weight, pos_bias, out_weight):
    frames_all = len(pieces)
    band, col_count, channels = pieces[0].shape
    count = band * col_count
    vmem = pl.BlockSpec(memory_space=pltpu.VMEM)
    return pl.pallas_call(
        functools.partial(attend_kernel, parts=frames_all),
        out_shape=tuple(jax.ShapeDtypeStruct(pieces[0].shape, jnp.bfloat16) for _ in pieces),
        in_specs=[vmem] * (frames_all + 3),
        out_specs=tuple(vmem for _ in pieces),
        scratch_shapes=[
            pltpu.VMEM((frames_all, 3 * channels, count), jnp.bfloat16),
            pltpu.VMEM((frames_all, channels, count), jnp.bfloat16),
        ],
    )(*pieces, qkv_weight.T, pos_bias.transpose(0, 2, 1)[..., None], out_weight)


def attend(grid, qkv_weight, pos_bias, out_weight):
    frames_all, count, channels = grid.shape
    vmem = pl.BlockSpec(memory_space=pltpu.VMEM)
    return pl.pallas_call(
        functools.partial(attend_kernel, parts=0),
        out_shape=jax.ShapeDtypeStruct((frames_all, count, channels), jnp.bfloat16),
        in_specs=[vmem] * 4,
        out_specs=vmem,
        scratch_shapes=[
            pltpu.VMEM((frames_all, 3 * channels, count), jnp.bfloat16),
            pltpu.VMEM((frames_all, channels, count), jnp.bfloat16),
        ],
    )(grid, qkv_weight.T, pos_bias.transpose(0, 2, 1)[..., None], out_weight)


def rotated_attention(source, lo, rows, qkv_weight, pos_bias, out_weight):
    frames_all = lax.axis_size("frame")
    me = lax.axis_index("frame")
    _, col_count, channels = source.shape
    band = rows // frames_all
    got = []
    for s in range(frames_all):
        piece = lax.dynamic_slice_in_dim(source, lo + ((me + s) % frames_all) * band, band, axis=0)
        if s:
            piece = lax.ppermute(piece, "frame", [(i, (i + s) % frames_all) for i in range(frames_all)])
        got.append(piece)
    source = (me - jnp.arange(frames_all)) % frames_all
    bias = jnp.take(jnp.take(pos_bias, source, axis=1), source, axis=2)
    attended = attend_pieces(got, qkv_weight, bias, out_weight)
    back = []
    for s in range(frames_all):
        piece = attended[s]
        if s:
            piece = lax.ppermute(piece, "frame", [(i, (i - s) % frames_all) for i in range(frames_all)])
        back.append(piece)
    order = (jnp.arange(frames_all) - me) % frames_all
    return jnp.take(jnp.stack(back), order, axis=0).reshape(rows, col_count, channels)


def body(latents, conv1_weight, qkv_weight, out_weight, pos_bias, conv2_weight):
    frames_dev, row_count, col_count, channels = latents.shape
    frames_all = lax.axis_size("frame")
    tile = latents.reshape(row_count, col_count, channels)
    def tile_edge(c):
        pick = (jnp.arange(col_count) == c % col_count).astype(tile.dtype)
        return jnp.einsum("rwc,w->rc", tile, pick, preferred_element_type=jnp.float32).astype(tile.dtype)

    rims = halo(tile_edge)
    half = row_count // 2
    returned = []
    rotate = frames_all <= 4 and half % frames_all == 0
    if rotate:
        whole = convolve([[tile]], rims, conv1_weight, norm_gelu, 0, row_count)
        for lo in (0, half):
            returned.append(rotated_attention(whole, lo, half, qkv_weight, pos_bias, out_weight))
        hidden_rows = [whole]
        hidden = [whole[:half], whole[half:]]
    else:
        hidden = [convolve([[tile]], rims, conv1_weight, norm_gelu, lo, lo + half) for lo in (0, half)]
        hidden_rows = hidden
    pix_piece = half * col_count // frames_all
    if half % frames_all == 0:
        piece_shape = (frames_all, half // frames_all, col_count, channels)
    else:
        piece_shape = (frames_all, pix_piece, channels)
    for part in hidden:
        if rotate:
            break
        pieces = lax.all_to_all(part.reshape(piece_shape), "frame", split_axis=0, concat_axis=0, tiled=True)
        attended = attend(pieces.reshape(frames_all, pix_piece, channels), qkv_weight, pos_bias, out_weight)
        back = lax.all_to_all(attended.reshape(piece_shape), "frame", split_axis=0, concat_axis=0, tiled=True)
        returned.append(back.reshape(half, col_count, channels))

    def joined_edge(c):
        summed = [h[:, c, :].astype(jnp.float32) + r[:, c, :].astype(jnp.float32) for h, r in zip(hidden, returned)]
        return jnp.concatenate(summed, axis=0).astype(jnp.bfloat16)

    second = convolve([hidden_rows, returned], halo(joined_edge), conv2_weight, to_bf16, 0, row_count)
    return second.reshape(frames_dev, row_count, col_count, channels)


def solution(mesh):
    groups = mesh.shape["groups"]
    frames_all = mesh.shape["frame"] // 4
    split_mesh = Mesh(
        mesh.devices.reshape(groups, 4, frames_all), ("groups", "quarter", "frame")
    )
    tiles = P(("groups", "quarter", "frame"), None, None, None)
    placed = (tiles, P(), P(), P(), P(), P())
    return jax.shard_map(
        body,
        mesh=split_mesh,
        in_specs=placed,
        out_specs=tiles,
        check_vma=False,
    )
```

```python
import functools

import jax
import jax.numpy as jnp
from jax import lax
from jax.experimental import pallas as pl
from jax.experimental.pallas import tpu as pltpu
from jax.sharding import Mesh, PartitionSpec as P

HEADS = 5


def shifted(block, axis, distance):
    size = lax.axis_size(axis)
    route = [((i - distance) % size, i) for i in range(size)]
    moved = lax.ppermute(block, axis, route)
    source = lax.axis_index(axis) - distance
    inside = (source >= 0) & (source < size)
    return jnp.where(inside, moved, jnp.zeros_like(moved))


def conv_kernel(*refs, layout, lo, hi, finish):
    count = sum(len(segments) for segments in layout)
    flat = refs[:count]
    left_ref, right_ref, w_ref, o_ref, slab, shift_s = refs[count:]
    row_count = left_ref.shape[0]
    _, col_count, channels = o_ref.shape
    lanes = slab.shape[1] // 3
    band = 12
    span = band * col_count
    padded_rows = slab.shape[0]
    slab[pl.ds(0, col_count)] = jnp.zeros((col_count, slab.shape[1]), jnp.bfloat16)
    slab[pl.ds(padded_rows - col_count, col_count)] = jnp.zeros((col_count, slab.shape[1]), jnp.bfloat16)
    column = lax.broadcasted_iota(jnp.int32, (band, col_count, channels), 1)
    addends = []
    at = 0
    for segments in layout:
        addends.append(list(zip(flat[at : at + len(segments)], segments)))
        at += len(segments)

    def rows_of(ref_list, r0):
        for ref, (first, last) in ref_list:
            if first <= r0 < last:
                return ref[pl.ds(r0 - first, band)]

    for r0 in range(max(lo - band, 0), min(hi + band, row_count), band):
        block = rows_of(addends[0], r0).astype(jnp.float32)
        for extra in addends[1:]:
            block = block + rows_of(extra, r0).astype(jnp.float32)
        block = block.astype(jnp.bfloat16)
        shift_s[pl.ds(8, span)] = block.astype(jnp.float32).reshape(span, channels)
        before = shift_s[pl.ds(7, span)].reshape(band, col_count, channels)
        after = shift_s[pl.ds(9, span)].reshape(band, col_count, channels)
        rim_l = left_ref[pl.ds(r0, band)].astype(jnp.float32)[:, None, :]
        rim_r = right_ref[pl.ds(r0, band)].astype(jnp.float32)[:, None, :]
        before = jnp.where(column == 0, rim_l, before)
        after = jnp.where(column == col_count - 1, rim_r, after)
        rows = pl.ds((r0 + 1) * col_count, span)
        slab[rows, pl.ds(0, channels)] = before.reshape(span, channels).astype(jnp.bfloat16)
        slab[rows, pl.ds(lanes, channels)] = block.reshape(span, channels)
        slab[rows, pl.ds(2 * lanes, channels)] = after.reshape(span, channels).astype(jnp.bfloat16)

    for r0 in range(lo, hi, band):
        acc = None
        for a in range(3):
            rows = pl.ds((r0 + a) * col_count, span)
            term = jnp.dot(slab[rows, :], w_ref[a], preferred_element_type=jnp.float32)
            acc = term if acc is None else acc + term
        o_ref[pl.ds(r0 - lo, band)] = finish(acc).reshape(band, col_count, channels)


def norm_gelu(first):
    normed = first * lax.rsqrt(jnp.mean(first * first, axis=-1, keepdims=True) + 1e-06)
    return jax.nn.gelu(normed, approximate=True).astype(jnp.bfloat16)


def to_bf16(acc):
    return acc.astype(jnp.bfloat16)


def halo(edge_of):
    return shifted(edge_of(-1), "quarter", 1), shifted(edge_of(0), "quarter", -1)


def convolve(groups, rims, weight, finish, lo, hi):
    row_count, channels = rims[0].shape
    col_count = groups[0][0].shape[1]
    layout = []
    for segments in groups:
        spans = []
        first = 0
        for piece in segments:
            spans.append((first, first + piece.shape[0]))
            first += piece.shape[0]
        layout.append(tuple(spans))
    flat = [piece for segments in groups for piece in segments]
    vmem = pl.BlockSpec(memory_space=pltpu.VMEM)
    padded = (row_count + 2) * col_count
    stacked = weight.reshape(3, 3 * channels, channels)
    return pl.pallas_call(
        functools.partial(conv_kernel, layout=tuple(layout), lo=lo, hi=hi, finish=finish),
        out_shape=jax.ShapeDtypeStruct((hi - lo, col_count, channels), jnp.bfloat16),
        in_specs=[vmem] * (len(flat) + 3),
        out_specs=vmem,
        scratch_shapes=[
            pltpu.VMEM((padded, 3 * channels), jnp.bfloat16),
            pltpu.VMEM((12 * col_count + 16, channels), jnp.float32),
        ],
    )(*flat, *rims, stacked)


def attend_kernel(*refs, parts):
    if parts:
        x_refs = refs[:parts]
        wqkv_ref, bias_ref, wout_ref = refs[parts : parts + 3]
        o_refs = refs[parts + 3 : 2 * parts + 3]
        qkv_s, blend_s = refs[2 * parts + 3 :]
        frames_all, _, count = qkv_s.shape
        channels = wout_ref.shape[0]
        for f in range(parts):
            qkv_s[f] = lax.dot_general(
                wqkv_ref[...],
                x_refs[f][...].reshape(count, channels),
                (((1,), (1,)), ((), ())),
                preferred_element_type=jnp.float32,
            ).astype(jnp.bfloat16)
    else:
        x_ref, wqkv_ref, bias_ref, wout_ref, o_ref, qkv_s, blend_s = refs
        frames_all, count, channels = x_ref.shape

        def project(f, carry):
            qkv_s[f] = lax.dot_general(
                wqkv_ref[...], x_ref[f], (((1,), (1,)), ((), ())), preferred_element_type=jnp.float32
            ).astype(jnp.bfloat16)
            return carry

        lax.fori_loop(0, frames_all, project, 0, unroll=frames_all <= 4)
    head_dim = channels // HEADS
    scale = head_dim ** (-0.5)
    block = min(frames_all, 4)

    def head_block(h, first):
        frames = pl.ds(first, block)
        queries = qkv_s[frames, pl.ds(h * head_dim, head_dim), :].astype(jnp.float32)
        scores = []
        for g in range(frames_all):
            key_part = qkv_s[g, pl.ds(channels + h * head_dim, head_dim), :].astype(jnp.float32)
            bias = bias_ref[h, g, frames]
            scores.append(jnp.sum(queries * key_part[None], axis=1) * scale + bias)
        top = scores[0]
        for g in range(1, frames_all):
            top = jnp.maximum(top, scores[g])
        weights = [jnp.exp(s - top) for s in scores]
        total = weights[0]
        for g in range(1, frames_all):
            total = total + weights[g]
        blended = None
        for g in range(frames_all):
            value_part = qkv_s[g, pl.ds(2 * channels + h * head_dim, head_dim), :].astype(jnp.float32)
            prob = (weights[g] / total).astype(jnp.bfloat16).astype(jnp.float32)
            term = prob[:, None, :] * value_part[None]
            blended = term if blended is None else blended + term
        blend_s[frames, pl.ds(h * head_dim, head_dim), :] = blended.astype(jnp.bfloat16)

    def frame_block(i, carry):
        for h in range(HEADS):
            head_block(h, i * block)
        return carry

    lax.fori_loop(0, frames_all // block, frame_block, 0, unroll=frames_all <= 4)

    def out_product(f):
        return lax.dot_general(
            blend_s[f], wout_ref[...], (((0,), (0,)), ((), ())), preferred_element_type=jnp.float32
        ).astype(jnp.bfloat16)

    if parts:
        for f in range(parts):
            o_refs[f][...] = out_product(f).reshape(o_refs[f].shape)
        return

    def out_project(f, carry):
        o_ref[f] = out_product(f)
        return carry

    lax.fori_loop(0, frames_all, out_project, 0, unroll=frames_all <= 4)


def attend_pieces(pieces, qkv_weight, pos_bias, out_weight):
    frames_all = len(pieces)
    band, col_count, channels = pieces[0].shape
    count = band * col_count
    vmem = pl.BlockSpec(memory_space=pltpu.VMEM)
    return pl.pallas_call(
        functools.partial(attend_kernel, parts=frames_all),
        out_shape=tuple(jax.ShapeDtypeStruct(pieces[0].shape, jnp.bfloat16) for _ in pieces),
        in_specs=[vmem] * (frames_all + 3),
        out_specs=tuple(vmem for _ in pieces),
        scratch_shapes=[
            pltpu.VMEM((frames_all, 3 * channels, count), jnp.bfloat16),
            pltpu.VMEM((frames_all, channels, count), jnp.bfloat16),
        ],
    )(*pieces, qkv_weight.T, pos_bias.transpose(0, 2, 1)[..., None], out_weight)


def attend(grid, qkv_weight, pos_bias, out_weight):
    frames_all, count, channels = grid.shape
    vmem = pl.BlockSpec(memory_space=pltpu.VMEM)
    return pl.pallas_call(
        functools.partial(attend_kernel, parts=0),
        out_shape=jax.ShapeDtypeStruct((frames_all, count, channels), jnp.bfloat16),
        in_specs=[vmem] * 4,
        out_specs=vmem,
        scratch_shapes=[
            pltpu.VMEM((frames_all, 3 * channels, count), jnp.bfloat16),
            pltpu.VMEM((frames_all, channels, count), jnp.bfloat16),
        ],
    )(grid, qkv_weight.T, pos_bias.transpose(0, 2, 1)[..., None], out_weight)


def rotated_attention(source, lo, rows, qkv_weight, pos_bias, out_weight):
    frames_all = lax.axis_size("frame")
    me = lax.axis_index("frame")
    _, col_count, channels = source.shape
    band = rows // frames_all
    got = []
    for s in range(frames_all):
        piece = lax.dynamic_slice_in_dim(source, lo + ((me + s) % frames_all) * band, band, axis=0)
        if s:
            piece = lax.ppermute(piece, "frame", [(i, (i + s) % frames_all) for i in range(frames_all)])
        got.append(piece)
    source = (me - jnp.arange(frames_all)) % frames_all
    bias = jnp.take(jnp.take(pos_bias, source, axis=1), source, axis=2)
    attended = attend_pieces(got, qkv_weight, bias, out_weight)
    back = []
    for s in range(frames_all):
        piece = attended[s]
        if s:
            piece = lax.ppermute(piece, "frame", [(i, (i - s) % frames_all) for i in range(frames_all)])
        back.append(piece)
    order = (jnp.arange(frames_all) - me) % frames_all
    return jnp.take(jnp.stack(back), order, axis=0).reshape(rows, col_count, channels)


def body(latents, conv1_weight, qkv_weight, out_weight, pos_bias, conv2_weight):
    frames_dev, row_count, col_count, channels = latents.shape
    frames_all = lax.axis_size("frame")
    tile = latents.reshape(row_count, col_count, channels)
    def tile_edge(c):
        pick = (jnp.arange(col_count) == c % col_count).astype(tile.dtype)
        return jnp.einsum("rwc,w->rc", tile, pick, preferred_element_type=jnp.float32).astype(tile.dtype)

    rims = halo(tile_edge)
    half = row_count // 2
    returned = []
    rotate = frames_all <= 4 and half % frames_all == 0
    if rotate:
        whole = convolve([[tile]], rims, conv1_weight, norm_gelu, 0, row_count)
        returned.append(rotated_attention(whole, 0, row_count, qkv_weight, pos_bias, out_weight))
        hidden_rows = [whole]
        hidden = [whole]
    else:
        hidden = [convolve([[tile]], rims, conv1_weight, norm_gelu, lo, lo + half) for lo in (0, half)]
        hidden_rows = hidden
    pix_piece = half * col_count // frames_all
    if half % frames_all == 0:
        piece_shape = (frames_all, half // frames_all, col_count, channels)
    else:
        piece_shape = (frames_all, pix_piece, channels)
    for part in hidden:
        if rotate:
            break
        pieces = lax.all_to_all(part.reshape(piece_shape), "frame", split_axis=0, concat_axis=0, tiled=True)
        attended = attend(pieces.reshape(frames_all, pix_piece, channels), qkv_weight, pos_bias, out_weight)
        back = lax.all_to_all(attended.reshape(piece_shape), "frame", split_axis=0, concat_axis=0, tiled=True)
        returned.append(back.reshape(half, col_count, channels))

    def joined_edge(c):
        summed = [h[:, c, :].astype(jnp.float32) + r[:, c, :].astype(jnp.float32) for h, r in zip(hidden, returned)]
        return jnp.concatenate(summed, axis=0).astype(jnp.bfloat16)

    second = convolve([hidden_rows, returned], halo(joined_edge), conv2_weight, to_bf16, 0, row_count)
    return second.reshape(frames_dev, row_count, col_count, channels)


def solution(mesh):
    groups = mesh.shape["groups"]
    frames_all = mesh.shape["frame"] // 4
    split_mesh = Mesh(
        mesh.devices.reshape(groups, 4, frames_all), ("groups", "quarter", "frame")
    )
    tiles = P(("groups", "quarter", "frame"), None, None, None)
    placed = (tiles, P(), P(), P(), P(), P())
    return jax.shard_map(
        body,
        mesh=split_mesh,
        in_specs=placed,
        out_specs=tiles,
        check_vma=False,
    )
```

```python
import functools

import jax
import jax.numpy as jnp
from jax import lax
from jax.experimental import pallas as pl
from jax.experimental.pallas import tpu as pltpu
from jax.sharding import Mesh, PartitionSpec as P

HEADS = 5


def shifted(block, axis, distance):
    size = lax.axis_size(axis)
    route = [((i - distance) % size, i) for i in range(size)]
    moved = lax.ppermute(block, axis, route)
    source = lax.axis_index(axis) - distance
    inside = (source >= 0) & (source < size)
    return jnp.where(inside, moved, jnp.zeros_like(moved))


def conv_kernel(*refs, layout, lo, hi, finish):
    count = sum(len(segments) for segments in layout)
    flat = refs[:count]
    left_ref, right_ref, w_ref, o_ref, slab, shift_s = refs[count:]
    row_count = left_ref.shape[0]
    _, col_count, channels = o_ref.shape
    lanes = slab.shape[1] // 3
    band = 12
    span = band * col_count
    padded_rows = slab.shape[0]
    slab[pl.ds(0, col_count)] = jnp.zeros((col_count, slab.shape[1]), jnp.bfloat16)
    slab[pl.ds(padded_rows - col_count, col_count)] = jnp.zeros((col_count, slab.shape[1]), jnp.bfloat16)
    column = lax.broadcasted_iota(jnp.int32, (band, col_count, channels), 1)
    addends = []
    at = 0
    for segments in layout:
        addends.append(list(zip(flat[at : at + len(segments)], segments)))
        at += len(segments)

    def rows_of(ref_list, r0):
        for ref, (first, last) in ref_list:
            if first <= r0 < last:
                return ref[pl.ds(r0 - first, band)]

    for r0 in range(max(lo - band, 0), min(hi + band, row_count), band):
        block = rows_of(addends[0], r0).astype(jnp.float32)
        for extra in addends[1:]:
            block = block + rows_of(extra, r0).astype(jnp.float32)
        block = block.astype(jnp.bfloat16)
        shift_s[pl.ds(8, span)] = block.astype(jnp.float32).reshape(span, channels)
        before = shift_s[pl.ds(7, span)].reshape(band, col_count, channels)
        after = shift_s[pl.ds(9, span)].reshape(band, col_count, channels)
        rim_l = left_ref[pl.ds(r0, band)].astype(jnp.float32)[:, None, :]
        rim_r = right_ref[pl.ds(r0, band)].astype(jnp.float32)[:, None, :]
        before = jnp.where(column == 0, rim_l, before)
        after = jnp.where(column == col_count - 1, rim_r, after)
        rows = pl.ds((r0 + 1) * col_count, span)
        slab[rows, pl.ds(0, channels)] = before.reshape(span, channels).astype(jnp.bfloat16)
        slab[rows, pl.ds(lanes, channels)] = block.reshape(span, channels)
        slab[rows, pl.ds(2 * lanes, channels)] = after.reshape(span, channels).astype(jnp.bfloat16)

    for r0 in range(lo, hi, band):
        acc = None
        for a in range(3):
            rows = pl.ds((r0 + a) * col_count, span)
            term = jnp.dot(slab[rows, :], w_ref[a], preferred_element_type=jnp.float32)
            acc = term if acc is None else acc + term
        o_ref[pl.ds(r0 - lo, band)] = finish(acc).reshape(band, col_count, channels)


def norm_gelu(first):
    normed = first * lax.rsqrt(jnp.mean(first * first, axis=-1, keepdims=True) + 1e-06)
    return jax.nn.gelu(normed, approximate=True).astype(jnp.bfloat16)


def to_bf16(acc):
    return acc.astype(jnp.bfloat16)


def halo(edge_of):
    return shifted(edge_of(-1), "quarter", 1), shifted(edge_of(0), "quarter", -1)


def convolve(groups, rims, weight, finish, lo, hi):
    row_count, channels = rims[0].shape
    col_count = groups[0][0].shape[1]
    layout = []
    for segments in groups:
        spans = []
        first = 0
        for piece in segments:
            spans.append((first, first + piece.shape[0]))
            first += piece.shape[0]
        layout.append(tuple(spans))
    flat = [piece for segments in groups for piece in segments]
    vmem = pl.BlockSpec(memory_space=pltpu.VMEM)
    padded = (row_count + 2) * col_count
    stacked = weight.reshape(3, 3 * channels, channels)
    return pl.pallas_call(
        functools.partial(conv_kernel, layout=tuple(layout), lo=lo, hi=hi, finish=finish),
        out_shape=jax.ShapeDtypeStruct((hi - lo, col_count, channels), jnp.bfloat16),
        in_specs=[vmem] * (len(flat) + 3),
        out_specs=vmem,
        scratch_shapes=[
            pltpu.VMEM((padded, 3 * channels), jnp.bfloat16),
            pltpu.VMEM((12 * col_count + 16, channels), jnp.float32),
        ],
    )(*flat, *rims, stacked)


def attend_kernel(*refs, parts):
    if parts:
        x_refs = refs[:parts]
        wqkv_ref, bias_ref, wout_ref = refs[parts : parts + 3]
        o_refs = refs[parts + 3 : 2 * parts + 3]
        qkv_s, blend_s = refs[2 * parts + 3 :]
        frames_all, _, count = qkv_s.shape
        channels = wout_ref.shape[0]
        for f in range(parts):
            qkv_s[f] = lax.dot_general(
                wqkv_ref[...],
                x_refs[f][...].reshape(count, channels),
                (((1,), (1,)), ((), ())),
                preferred_element_type=jnp.float32,
            ).astype(jnp.bfloat16)
    else:
        x_ref, wqkv_ref, bias_ref, wout_ref, o_ref, qkv_s, blend_s = refs
        frames_all, count, channels = x_ref.shape

        def project(f, carry):
            qkv_s[f] = lax.dot_general(
                wqkv_ref[...], x_ref[f], (((1,), (1,)), ((), ())), preferred_element_type=jnp.float32
            ).astype(jnp.bfloat16)
            return carry

        lax.fori_loop(0, frames_all, project, 0, unroll=frames_all <= 4)
    head_dim = channels // HEADS
    scale = head_dim ** (-0.5)
    block = min(frames_all, 4)

    def head_block(h, first):
        frames = pl.ds(first, block)
        queries = qkv_s[frames, pl.ds(h * head_dim, head_dim), :].astype(jnp.float32)
        scores = []
        for g in range(frames_all):
            key_part = qkv_s[g, pl.ds(channels + h * head_dim, head_dim), :].astype(jnp.float32)
            bias = bias_ref[h, g, frames]
            scores.append(jnp.sum(queries * key_part[None], axis=1) * scale + bias)
        top = scores[0]
        for g in range(1, frames_all):
            top = jnp.maximum(top, scores[g])
        weights = [jnp.exp(s - top) for s in scores]
        total = weights[0]
        for g in range(1, frames_all):
            total = total + weights[g]
        blended = None
        for g in range(frames_all):
            value_part = qkv_s[g, pl.ds(2 * channels + h * head_dim, head_dim), :].astype(jnp.float32)
            prob = (weights[g] / total).astype(jnp.bfloat16).astype(jnp.float32)
            term = prob[:, None, :] * value_part[None]
            blended = term if blended is None else blended + term
        blend_s[frames, pl.ds(h * head_dim, head_dim), :] = blended.astype(jnp.bfloat16)

    def frame_block(i, carry):
        for h in range(HEADS):
            head_block(h, i * block)
        return carry

    lax.fori_loop(0, frames_all // block, frame_block, 0, unroll=frames_all <= 4)

    def out_product(f):
        return lax.dot_general(
            blend_s[f], wout_ref[...], (((0,), (0,)), ((), ())), preferred_element_type=jnp.float32
        ).astype(jnp.bfloat16)

    if parts:
        for f in range(parts):
            o_refs[f][...] = out_product(f).reshape(o_refs[f].shape)
        return

    def out_project(f, carry):
        o_ref[f] = out_product(f)
        return carry

    lax.fori_loop(0, frames_all, out_project, 0, unroll=frames_all <= 4)


def attend_pieces(pieces, qkv_weight, pos_bias, out_weight):
    frames_all = len(pieces)
    band, col_count, channels = pieces[0].shape
    count = band * col_count
    vmem = pl.BlockSpec(memory_space=pltpu.VMEM)
    return pl.pallas_call(
        functools.partial(attend_kernel, parts=frames_all),
        out_shape=tuple(jax.ShapeDtypeStruct(pieces[0].shape, jnp.bfloat16) for _ in pieces),
        in_specs=[vmem] * (frames_all + 3),
        out_specs=tuple(vmem for _ in pieces),
        scratch_shapes=[
            pltpu.VMEM((frames_all, 3 * channels, count), jnp.bfloat16),
            pltpu.VMEM((frames_all, channels, count), jnp.bfloat16),
        ],
    )(*pieces, qkv_weight.T, pos_bias.transpose(0, 2, 1)[..., None], out_weight)


def attend(grid, qkv_weight, pos_bias, out_weight):
    frames_all, count, channels = grid.shape
    vmem = pl.BlockSpec(memory_space=pltpu.VMEM)
    return pl.pallas_call(
        functools.partial(attend_kernel, parts=0),
        out_shape=jax.ShapeDtypeStruct((frames_all, count, channels), jnp.bfloat16),
        in_specs=[vmem] * 4,
        out_specs=vmem,
        scratch_shapes=[
            pltpu.VMEM((frames_all, 3 * channels, count), jnp.bfloat16),
            pltpu.VMEM((frames_all, channels, count), jnp.bfloat16),
        ],
    )(grid, qkv_weight.T, pos_bias.transpose(0, 2, 1)[..., None], out_weight)


def rotated_attention(source, lo, rows, qkv_weight, pos_bias, out_weight):
    frames_all = lax.axis_size("frame")
    me = lax.axis_index("frame")
    _, col_count, channels = source.shape
    band = rows // frames_all
    got = []
    for s in range(frames_all):
        piece = lax.dynamic_slice_in_dim(source, lo + ((me + s) % frames_all) * band, band, axis=0)
        if s:
            piece = lax.ppermute(piece, "frame", [(i, (i + s) % frames_all) for i in range(frames_all)])
        got.append(piece)
    source = (me - jnp.arange(frames_all)) % frames_all
    bias = jnp.take(jnp.take(pos_bias, source, axis=1), source, axis=2)
    attended = attend_pieces(got, qkv_weight, bias, out_weight)
    back = []
    for s in range(frames_all):
        piece = attended[s]
        if s:
            piece = lax.ppermute(piece, "frame", [(i, (i - s) % frames_all) for i in range(frames_all)])
        back.append(piece)
    order = (jnp.arange(frames_all) - me) % frames_all
    return jnp.take(jnp.stack(back), order, axis=0).reshape(rows, col_count, channels)


def body(latents, conv1_weight, qkv_weight, out_weight, pos_bias, conv2_weight):
    frames_dev, row_count, col_count, channels = latents.shape
    frames_all = lax.axis_size("frame")
    tile = latents.reshape(row_count, col_count, channels)
    def tile_edge(c):
        pick = (jnp.arange(col_count) == c % col_count).astype(tile.dtype)
        return jnp.einsum("rwc,w->rc", tile, pick, preferred_element_type=jnp.float32).astype(tile.dtype)

    rims = halo(tile_edge)
    half = row_count // 2
    returned = []
    rotate = frames_all <= 4 and half % frames_all == 0
    if rotate:
        whole = convolve([[tile]], rims, conv1_weight, norm_gelu, 0, row_count)
        chunks = 3 if row_count % 3 == 0 and (row_count // 3) % (12 * frames_all // 4) == 0 else 2
        rows = row_count // chunks
        for lo in range(0, row_count, rows):
            returned.append(rotated_attention(whole, lo, rows, qkv_weight, pos_bias, out_weight))
        hidden_rows = [whole]
        hidden = [whole[lo : lo + rows] for lo in range(0, row_count, rows)]
    else:
        hidden = [convolve([[tile]], rims, conv1_weight, norm_gelu, lo, lo + half) for lo in (0, half)]
        hidden_rows = hidden
    pix_piece = half * col_count // frames_all
    if half % frames_all == 0:
        piece_shape = (frames_all, half // frames_all, col_count, channels)
    else:
        piece_shape = (frames_all, pix_piece, channels)
    for part in hidden:
        if rotate:
            break
        pieces = lax.all_to_all(part.reshape(piece_shape), "frame", split_axis=0, concat_axis=0, tiled=True)
        attended = attend(pieces.reshape(frames_all, pix_piece, channels), qkv_weight, pos_bias, out_weight)
        back = lax.all_to_all(attended.reshape(piece_shape), "frame", split_axis=0, concat_axis=0, tiled=True)
        returned.append(back.reshape(half, col_count, channels))

    def joined_edge(c):
        summed = [h[:, c, :].astype(jnp.float32) + r[:, c, :].astype(jnp.float32) for h, r in zip(hidden, returned)]
        return jnp.concatenate(summed, axis=0).astype(jnp.bfloat16)

    second = convolve([hidden_rows, returned], halo(joined_edge), conv2_weight, to_bf16, 0, row_count)
    return second.reshape(frames_dev, row_count, col_count, channels)


def solution(mesh):
    groups = mesh.shape["groups"]
    frames_all = mesh.shape["frame"] // 4
    split_mesh = Mesh(
        mesh.devices.reshape(groups, 4, frames_all), ("groups", "quarter", "frame")
    )
    tiles = P(("groups", "quarter", "frame"), None, None, None)
    placed = (tiles, P(), P(), P(), P(), P())
    return jax.shard_map(
        body,
        mesh=split_mesh,
        in_specs=placed,
        out_specs=tiles,
        check_vma=False,
    )
```

```python
import functools

import jax
import jax.numpy as jnp
from jax import lax
from jax.experimental import pallas as pl
from jax.experimental.pallas import tpu as pltpu
from jax.sharding import Mesh, PartitionSpec as P

HEADS = 5


def shifted(block, axis, distance):
    size = lax.axis_size(axis)
    route = [((i - distance) % size, i) for i in range(size)]
    moved = lax.ppermute(block, axis, route)
    source = lax.axis_index(axis) - distance
    inside = (source >= 0) & (source < size)
    return jnp.where(inside, moved, jnp.zeros_like(moved))


def conv_kernel(*refs, layout, lo, hi, band, finish):
    count = sum(len(segments) for segments in layout)
    flat = refs[:count]
    left_ref, right_ref, w_ref, o_ref, slab, shift_s = refs[count:]
    row_count = left_ref.shape[0]
    _, col_count, channels = o_ref.shape
    lanes = slab.shape[1] // 3
    span = band * col_count
    padded_rows = slab.shape[0]
    slab[pl.ds(0, col_count)] = jnp.zeros((col_count, slab.shape[1]), jnp.bfloat16)
    slab[pl.ds(padded_rows - col_count, col_count)] = jnp.zeros((col_count, slab.shape[1]), jnp.bfloat16)
    column = lax.broadcasted_iota(jnp.int32, (band, col_count, channels), 1)
    addends = []
    at = 0
    for segments in layout:
        addends.append(list(zip(flat[at : at + len(segments)], segments)))
        at += len(segments)

    def rows_of(ref_list, r0):
        for ref, (first, last) in ref_list:
            if first <= r0 < last:
                return ref[pl.ds(r0 - first, band)]

    for r0 in range(max(lo - band, 0), min(hi + band, row_count), band):
        block = rows_of(addends[0], r0).astype(jnp.float32)
        for extra in addends[1:]:
            block = block + rows_of(extra, r0).astype(jnp.float32)
        block = block.astype(jnp.bfloat16)
        shift_s[pl.ds(8, span)] = block.astype(jnp.float32).reshape(span, channels)
        before = shift_s[pl.ds(7, span)].reshape(band, col_count, channels)
        after = shift_s[pl.ds(9, span)].reshape(band, col_count, channels)
        rim_l = left_ref[pl.ds(r0, band)].astype(jnp.float32)[:, None, :]
        rim_r = right_ref[pl.ds(r0, band)].astype(jnp.float32)[:, None, :]
        before = jnp.where(column == 0, rim_l, before)
        after = jnp.where(column == col_count - 1, rim_r, after)
        rows = pl.ds((r0 + 1) * col_count, span)
        slab[rows, pl.ds(0, channels)] = before.reshape(span, channels).astype(jnp.bfloat16)
        slab[rows, pl.ds(lanes, channels)] = block.reshape(span, channels)
        slab[rows, pl.ds(2 * lanes, channels)] = after.reshape(span, channels).astype(jnp.bfloat16)

    for r0 in range(lo, hi, band):
        acc = None
        for a in range(3):
            rows = pl.ds((r0 + a) * col_count, span)
            term = jnp.dot(slab[rows, :], w_ref[a], preferred_element_type=jnp.float32)
            acc = term if acc is None else acc + term
        o_ref[pl.ds(r0 - lo, band)] = finish(acc).reshape(band, col_count, channels)


def norm_gelu(first):
    normed = first * lax.rsqrt(jnp.mean(first * first, axis=-1, keepdims=True) + 1e-06)
    return jax.nn.gelu(normed, approximate=True).astype(jnp.bfloat16)


def to_bf16(acc):
    return acc.astype(jnp.bfloat16)


def halo(edge_of):
    return shifted(edge_of(-1), "quarter", 1), shifted(edge_of(0), "quarter", -1)


def convolve(groups, rims, weight, finish, lo, hi, band=12):
    row_count, channels = rims[0].shape
    col_count = groups[0][0].shape[1]
    layout = []
    for segments in groups:
        spans = []
        first = 0
        for piece in segments:
            spans.append((first, first + piece.shape[0]))
            first += piece.shape[0]
        layout.append(tuple(spans))
    flat = [piece for segments in groups for piece in segments]
    vmem = pl.BlockSpec(memory_space=pltpu.VMEM)
    padded = (row_count + 2) * col_count
    stacked = weight.reshape(3, 3 * channels, channels)
    return pl.pallas_call(
        functools.partial(conv_kernel, layout=tuple(layout), lo=lo, hi=hi, band=band, finish=finish),
        out_shape=jax.ShapeDtypeStruct((hi - lo, col_count, channels), jnp.bfloat16),
        in_specs=[vmem] * (len(flat) + 3),
        out_specs=vmem,
        scratch_shapes=[
            pltpu.VMEM((padded, 3 * channels), jnp.bfloat16),
            pltpu.VMEM((band * col_count + 16, channels), jnp.float32),
        ],
    )(*flat, *rims, stacked)


def attend_kernel(*refs, parts):
    if parts:
        x_refs = refs[:parts]
        wqkv_ref, bias_ref, wout_ref = refs[parts : parts + 3]
        o_refs = refs[parts + 3 : 2 * parts + 3]
        qkv_s, blend_s = refs[2 * parts + 3 :]
        frames_all, _, count = qkv_s.shape
        channels = wout_ref.shape[0]
        for f in range(parts):
            qkv_s[f] = lax.dot_general(
                wqkv_ref[...],
                x_refs[f][...].reshape(count, channels),
                (((1,), (1,)), ((), ())),
                preferred_element_type=jnp.float32,
            ).astype(jnp.bfloat16)
    else:
        x_ref, wqkv_ref, bias_ref, wout_ref, o_ref, qkv_s, blend_s = refs
        frames_all, count, channels = x_ref.shape

        def project(f, carry):
            qkv_s[f] = lax.dot_general(
                wqkv_ref[...], x_ref[f], (((1,), (1,)), ((), ())), preferred_element_type=jnp.float32
            ).astype(jnp.bfloat16)
            return carry

        lax.fori_loop(0, frames_all, project, 0, unroll=frames_all <= 4)
    head_dim = channels // HEADS
    scale = head_dim ** (-0.5)
    block = min(frames_all, 4)

    def head_block(h, first):
        frames = pl.ds(first, block)
        queries = qkv_s[frames, pl.ds(h * head_dim, head_dim), :].astype(jnp.float32)
        scores = []
        for g in range(frames_all):
            key_part = qkv_s[g, pl.ds(channels + h * head_dim, head_dim), :].astype(jnp.float32)
            bias = bias_ref[h, g, frames]
            scores.append(jnp.sum(queries * key_part[None], axis=1) * scale + bias)
        top = scores[0]
        for g in range(1, frames_all):
            top = jnp.maximum(top, scores[g])
        weights = [jnp.exp(s - top) for s in scores]
        total = weights[0]
        for g in range(1, frames_all):
            total = total + weights[g]
        blended = None
        for g in range(frames_all):
            value_part = qkv_s[g, pl.ds(2 * channels + h * head_dim, head_dim), :].astype(jnp.float32)
            prob = (weights[g] / total).astype(jnp.bfloat16).astype(jnp.float32)
            term = prob[:, None, :] * value_part[None]
            blended = term if blended is None else blended + term
        blend_s[frames, pl.ds(h * head_dim, head_dim), :] = blended.astype(jnp.bfloat16)

    def frame_block(i, carry):
        for h in range(HEADS):
            head_block(h, i * block)
        return carry

    lax.fori_loop(0, frames_all // block, frame_block, 0, unroll=frames_all <= 4)

    def out_product(f):
        return lax.dot_general(
            blend_s[f], wout_ref[...], (((0,), (0,)), ((), ())), preferred_element_type=jnp.float32
        ).astype(jnp.bfloat16)

    if parts:
        for f in range(parts):
            o_refs[f][...] = out_product(f).reshape(o_refs[f].shape)
        return

    def out_project(f, carry):
        o_ref[f] = out_product(f)
        return carry

    lax.fori_loop(0, frames_all, out_project, 0, unroll=frames_all <= 4)


def attend_pieces(pieces, qkv_weight, pos_bias, out_weight):
    frames_all = len(pieces)
    band, col_count, channels = pieces[0].shape
    count = band * col_count
    vmem = pl.BlockSpec(memory_space=pltpu.VMEM)
    return pl.pallas_call(
        functools.partial(attend_kernel, parts=frames_all),
        out_shape=tuple(jax.ShapeDtypeStruct(pieces[0].shape, jnp.bfloat16) for _ in pieces),
        in_specs=[vmem] * (frames_all + 3),
        out_specs=tuple(vmem for _ in pieces),
        scratch_shapes=[
            pltpu.VMEM((frames_all, 3 * channels, count), jnp.bfloat16),
            pltpu.VMEM((frames_all, channels, count), jnp.bfloat16),
        ],
    )(*pieces, qkv_weight.T, pos_bias.transpose(0, 2, 1)[..., None], out_weight)


def attend(grid, qkv_weight, pos_bias, out_weight):
    frames_all, count, channels = grid.shape
    vmem = pl.BlockSpec(memory_space=pltpu.VMEM)
    return pl.pallas_call(
        functools.partial(attend_kernel, parts=0),
        out_shape=jax.ShapeDtypeStruct((frames_all, count, channels), jnp.bfloat16),
        in_specs=[vmem] * 4,
        out_specs=vmem,
        scratch_shapes=[
            pltpu.VMEM((frames_all, 3 * channels, count), jnp.bfloat16),
            pltpu.VMEM((frames_all, channels, count), jnp.bfloat16),
        ],
    )(grid, qkv_weight.T, pos_bias.transpose(0, 2, 1)[..., None], out_weight)


def rotated_attention(source, lo, rows, qkv_weight, pos_bias, out_weight):
    frames_all = lax.axis_size("frame")
    me = lax.axis_index("frame")
    _, col_count, channels = source.shape
    band = rows // frames_all
    got = []
    for s in range(frames_all):
        piece = lax.dynamic_slice_in_dim(source, lo + ((me + s) % frames_all) * band, band, axis=0)
        if s:
            piece = lax.ppermute(piece, "frame", [(i, (i + s) % frames_all) for i in range(frames_all)])
        got.append(piece)
    source = (me - jnp.arange(frames_all)) % frames_all
    bias = jnp.take(jnp.take(pos_bias, source, axis=1), source, axis=2)
    attended = attend_pieces(got, qkv_weight, bias, out_weight)
    back = []
    for s in range(frames_all):
        piece = attended[s]
        if s:
            piece = lax.ppermute(piece, "frame", [(i, (i - s) % frames_all) for i in range(frames_all)])
        back.append(piece)
    order = (jnp.arange(frames_all) - me) % frames_all
    return jnp.take(jnp.stack(back), order, axis=0).reshape(rows, col_count, channels)


def body(latents, conv1_weight, qkv_weight, out_weight, pos_bias, conv2_weight):
    frames_dev, row_count, col_count, channels = latents.shape
    frames_all = lax.axis_size("frame")
    tile = latents.reshape(row_count, col_count, channels)
    def tile_edge(c):
        pick = (jnp.arange(col_count) == c % col_count).astype(tile.dtype)
        return jnp.einsum("rwc,w->rc", tile, pick, preferred_element_type=jnp.float32).astype(tile.dtype)

    rims = halo(tile_edge)
    half = row_count // 2
    returned = []
    rotate = frames_all <= 4 and half % frames_all == 0
    if rotate:
        whole = convolve([[tile]], rims, conv1_weight, norm_gelu, 0, row_count)
        for lo in (0, half):
            returned.append(rotated_attention(whole, lo, half, qkv_weight, pos_bias, out_weight))
        hidden_rows = [whole]
        hidden = [whole[:half], whole[half:]]
    else:
        hidden = [convolve([[tile]], rims, conv1_weight, norm_gelu, lo, lo + half) for lo in (0, half)]
        hidden_rows = hidden
    pix_piece = half * col_count // frames_all
    if half % frames_all == 0:
        piece_shape = (frames_all, half // frames_all, col_count, channels)
    else:
        piece_shape = (frames_all, pix_piece, channels)
    for part in hidden:
        if rotate:
            break
        pieces = lax.all_to_all(part.reshape(piece_shape), "frame", split_axis=0, concat_axis=0, tiled=True)
        attended = attend(pieces.reshape(frames_all, pix_piece, channels), qkv_weight, pos_bias, out_weight)
        back = lax.all_to_all(attended.reshape(piece_shape), "frame", split_axis=0, concat_axis=0, tiled=True)
        returned.append(back.reshape(half, col_count, channels))

    def joined_edge(c):
        summed = [h[:, c, :].astype(jnp.float32) + r[:, c, :].astype(jnp.float32) for h, r in zip(hidden, returned)]
        return jnp.concatenate(summed, axis=0).astype(jnp.bfloat16)

    second = convolve([hidden_rows, returned], halo(joined_edge), conv2_weight, to_bf16, 0, row_count, 6)
    return second.reshape(frames_dev, row_count, col_count, channels)


def solution(mesh):
    groups = mesh.shape["groups"]
    frames_all = mesh.shape["frame"] // 4
    split_mesh = Mesh(
        mesh.devices.reshape(groups, 4, frames_all), ("groups", "quarter", "frame")
    )
    tiles = P(("groups", "quarter", "frame"), None, None, None)
    placed = (tiles, P(), P(), P(), P(), P())
    return jax.shard_map(
        body,
        mesh=split_mesh,
        in_specs=placed,
        out_specs=tiles,
        check_vma=False,
    )
```

```python
import functools

import jax
import jax.numpy as jnp
from jax import lax
from jax.experimental import pallas as pl
from jax.experimental.pallas import tpu as pltpu
from jax.sharding import Mesh, PartitionSpec as P

HEADS = 5


def shifted(block, axis, distance):
    size = lax.axis_size(axis)
    route = [((i - distance) % size, i) for i in range(size)]
    moved = lax.ppermute(block, axis, route)
    source = lax.axis_index(axis) - distance
    inside = (source >= 0) & (source < size)
    return jnp.where(inside, moved, jnp.zeros_like(moved))


def conv_kernel(*refs, layout, lo, hi, band, finish):
    count = sum(len(segments) for segments in layout)
    flat = refs[:count]
    left_ref, right_ref, w_ref, o_ref, slab, shift_s = refs[count:]
    row_count = left_ref.shape[0]
    _, col_count, channels = o_ref.shape
    lanes = slab.shape[1] // 3
    span = band * col_count
    padded_rows = slab.shape[0]
    slab[pl.ds(0, col_count)] = jnp.zeros((col_count, slab.shape[1]), jnp.bfloat16)
    slab[pl.ds(padded_rows - col_count, col_count)] = jnp.zeros((col_count, slab.shape[1]), jnp.bfloat16)
    column = lax.broadcasted_iota(jnp.int32, (band, col_count, channels), 1)
    addends = []
    at = 0
    for segments in layout:
        addends.append(list(zip(flat[at : at + len(segments)], segments)))
        at += len(segments)

    def rows_of(ref_list, r0):
        for ref, (first, last) in ref_list:
            if first <= r0 < last:
                return ref[pl.ds(r0 - first, band)]

    for r0 in range(max(lo - band, 0), min(hi + band, row_count), band):
        block = rows_of(addends[0], r0).astype(jnp.float32)
        for extra in addends[1:]:
            block = block + rows_of(extra, r0).astype(jnp.float32)
        block = block.astype(jnp.bfloat16)
        shift_s[pl.ds(8, span)] = block.astype(jnp.float32).reshape(span, channels)
        before = shift_s[pl.ds(7, span)].reshape(band, col_count, channels)
        after = shift_s[pl.ds(9, span)].reshape(band, col_count, channels)
        rim_l = left_ref[pl.ds(r0, band)].astype(jnp.float32)[:, None, :]
        rim_r = right_ref[pl.ds(r0, band)].astype(jnp.float32)[:, None, :]
        before = jnp.where(column == 0, rim_l, before)
        after = jnp.where(column == col_count - 1, rim_r, after)
        rows = pl.ds((r0 + 1) * col_count, span)
        slab[rows, pl.ds(0, channels)] = before.reshape(span, channels).astype(jnp.bfloat16)
        slab[rows, pl.ds(lanes, channels)] = block.reshape(span, channels)
        slab[rows, pl.ds(2 * lanes, channels)] = after.reshape(span, channels).astype(jnp.bfloat16)

    for r0 in range(lo, hi, band):
        acc = None
        for a in range(3):
            rows = pl.ds((r0 + a) * col_count, span)
            term = jnp.dot(slab[rows, :], w_ref[a], preferred_element_type=jnp.float32)
            acc = term if acc is None else acc + term
        o_ref[pl.ds(r0 - lo, band)] = finish(acc).reshape(band, col_count, channels)


def norm_gelu(first):
    normed = first * lax.rsqrt(jnp.mean(first * first, axis=-1, keepdims=True) + 1e-06)
    return jax.nn.gelu(normed, approximate=True).astype(jnp.bfloat16)


def to_bf16(acc):
    return acc.astype(jnp.bfloat16)


def halo(edge_of):
    return shifted(edge_of(-1), "quarter", 1), shifted(edge_of(0), "quarter", -1)


def convolve(groups, rims, weight, finish, lo, hi, band=12):
    row_count, channels = rims[0].shape
    col_count = groups[0][0].shape[1]
    layout = []
    for segments in groups:
        spans = []
        first = 0
        for piece in segments:
            spans.append((first, first + piece.shape[0]))
            first += piece.shape[0]
        layout.append(tuple(spans))
    flat = [piece for segments in groups for piece in segments]
    vmem = pl.BlockSpec(memory_space=pltpu.VMEM)
    padded = (row_count + 2) * col_count
    stacked = weight.reshape(3, 3 * channels, channels)
    return pl.pallas_call(
        functools.partial(conv_kernel, layout=tuple(layout), lo=lo, hi=hi, band=band, finish=finish),
        out_shape=jax.ShapeDtypeStruct((hi - lo, col_count, channels), jnp.bfloat16),
        in_specs=[vmem] * (len(flat) + 3),
        out_specs=vmem,
        scratch_shapes=[
            pltpu.VMEM((padded, 3 * channels), jnp.bfloat16),
            pltpu.VMEM((band * col_count + 16, channels), jnp.float32),
        ],
    )(*flat, *rims, stacked)


def attend_kernel(*refs, parts):
    if parts:
        x_refs = refs[:parts]
        wqkv_ref, bias_ref, wout_ref = refs[parts : parts + 3]
        o_refs = refs[parts + 3 : 2 * parts + 3]
        qkv_s, blend_s = refs[2 * parts + 3 :]
        frames_all, _, count = qkv_s.shape
        channels = wout_ref.shape[0]
        for f in range(parts):
            qkv_s[f] = lax.dot_general(
                wqkv_ref[...],
                x_refs[f][...].reshape(count, channels),
                (((1,), (1,)), ((), ())),
                preferred_element_type=jnp.float32,
            ).astype(jnp.bfloat16)
    else:
        x_ref, wqkv_ref, bias_ref, wout_ref, o_ref, qkv_s, blend_s = refs
        frames_all, count, channels = x_ref.shape

        def project(f, carry):
            qkv_s[f] = lax.dot_general(
                wqkv_ref[...], x_ref[f], (((1,), (1,)), ((), ())), preferred_element_type=jnp.float32
            ).astype(jnp.bfloat16)
            return carry

        lax.fori_loop(0, frames_all, project, 0, unroll=frames_all <= 4)
    head_dim = channels // HEADS
    scale = head_dim ** (-0.5)
    block = min(frames_all, 4)

    def head_block(h, first):
        frames = pl.ds(first, block)
        queries = qkv_s[frames, pl.ds(h * head_dim, head_dim), :].astype(jnp.float32)
        scores = []
        for g in range(frames_all):
            key_part = qkv_s[g, pl.ds(channels + h * head_dim, head_dim), :].astype(jnp.float32)
            bias = bias_ref[h, g, frames]
            scores.append(jnp.sum(queries * key_part[None], axis=1) * scale + bias)
        top = scores[0]
        for g in range(1, frames_all):
            top = jnp.maximum(top, scores[g])
        weights = [jnp.exp(s - top) for s in scores]
        total = weights[0]
        for g in range(1, frames_all):
            total = total + weights[g]
        blended = None
        for g in range(frames_all):
            value_part = qkv_s[g, pl.ds(2 * channels + h * head_dim, head_dim), :].astype(jnp.float32)
            prob = (weights[g] / total).astype(jnp.bfloat16).astype(jnp.float32)
            term = prob[:, None, :] * value_part[None]
            blended = term if blended is None else blended + term
        blend_s[frames, pl.ds(h * head_dim, head_dim), :] = blended.astype(jnp.bfloat16)

    def frame_block(i, carry):
        for h in range(HEADS):
            head_block(h, i * block)
        return carry

    lax.fori_loop(0, frames_all // block, frame_block, 0, unroll=frames_all <= 4)

    def out_product(f):
        return lax.dot_general(
            blend_s[f], wout_ref[...], (((0,), (0,)), ((), ())), preferred_element_type=jnp.float32
        ).astype(jnp.bfloat16)

    if parts:
        for f in range(parts):
            o_refs[f][...] = out_product(f).reshape(o_refs[f].shape)
        return

    def out_project(f, carry):
        o_ref[f] = out_product(f)
        return carry

    lax.fori_loop(0, frames_all, out_project, 0, unroll=frames_all <= 4)


def attend_pieces(pieces, qkv_weight, pos_bias, out_weight):
    frames_all = len(pieces)
    band, col_count, channels = pieces[0].shape
    count = band * col_count
    vmem = pl.BlockSpec(memory_space=pltpu.VMEM)
    return pl.pallas_call(
        functools.partial(attend_kernel, parts=frames_all),
        out_shape=tuple(jax.ShapeDtypeStruct(pieces[0].shape, jnp.bfloat16) for _ in pieces),
        in_specs=[vmem] * (frames_all + 3),
        out_specs=tuple(vmem for _ in pieces),
        scratch_shapes=[
            pltpu.VMEM((frames_all, 3 * channels, count), jnp.bfloat16),
            pltpu.VMEM((frames_all, channels, count), jnp.bfloat16),
        ],
    )(*pieces, qkv_weight.T, pos_bias.transpose(0, 2, 1)[..., None], out_weight)


def attend(grid, qkv_weight, pos_bias, out_weight):
    frames_all, count, channels = grid.shape
    vmem = pl.BlockSpec(memory_space=pltpu.VMEM)
    return pl.pallas_call(
        functools.partial(attend_kernel, parts=0),
        out_shape=jax.ShapeDtypeStruct((frames_all, count, channels), jnp.bfloat16),
        in_specs=[vmem] * 4,
        out_specs=vmem,
        scratch_shapes=[
            pltpu.VMEM((frames_all, 3 * channels, count), jnp.bfloat16),
            pltpu.VMEM((frames_all, channels, count), jnp.bfloat16),
        ],
    )(grid, qkv_weight.T, pos_bias.transpose(0, 2, 1)[..., None], out_weight)


def rotated_attention(source, lo, rows, qkv_weight, pos_bias, out_weight):
    frames_all = lax.axis_size("frame")
    me = lax.axis_index("frame")
    _, col_count, channels = source.shape
    band = rows // frames_all
    got = []
    for s in range(frames_all):
        piece = lax.dynamic_slice_in_dim(source, lo + ((me + s) % frames_all) * band, band, axis=0)
        if s:
            piece = lax.ppermute(piece, "frame", [(i, (i + s) % frames_all) for i in range(frames_all)])
        got.append(piece)
    source = (me - jnp.arange(frames_all)) % frames_all
    bias = jnp.take(jnp.take(pos_bias, source, axis=1), source, axis=2)
    attended = attend_pieces(got, qkv_weight, bias, out_weight)
    back = []
    for s in range(frames_all):
        piece = attended[s]
        if s:
            piece = lax.ppermute(piece, "frame", [(i, (i - s) % frames_all) for i in range(frames_all)])
        back.append(piece)
    order = (jnp.arange(frames_all) - me) % frames_all
    return jnp.take(jnp.stack(back), order, axis=0).reshape(rows, col_count, channels)


def body(latents, conv1_weight, qkv_weight, out_weight, pos_bias, conv2_weight):
    frames_dev, row_count, col_count, channels = latents.shape
    frames_all = lax.axis_size("frame")
    tile = latents.reshape(row_count, col_count, channels)
    def tile_edge(c):
        pick = (jnp.arange(col_count) == c % col_count).astype(tile.dtype)
        return jnp.einsum("rwc,w->rc", tile, pick, preferred_element_type=jnp.float32).astype(tile.dtype)

    rims = halo(tile_edge)
    half = row_count // 2
    returned = []
    rotate = frames_all <= 4 and half % frames_all == 0
    if rotate:
        whole = convolve([[tile]], rims, conv1_weight, norm_gelu, 0, row_count, 6)
        for lo in (0, half):
            returned.append(rotated_attention(whole, lo, half, qkv_weight, pos_bias, out_weight))
        hidden_rows = [whole]
        hidden = [whole[:half], whole[half:]]
    else:
        hidden = [convolve([[tile]], rims, conv1_weight, norm_gelu, lo, lo + half) for lo in (0, half)]
        hidden_rows = hidden
    pix_piece = half * col_count // frames_all
    if half % frames_all == 0:
        piece_shape = (frames_all, half // frames_all, col_count, channels)
    else:
        piece_shape = (frames_all, pix_piece, channels)
    for part in hidden:
        if rotate:
            break
        pieces = lax.all_to_all(part.reshape(piece_shape), "frame", split_axis=0, concat_axis=0, tiled=True)
        attended = attend(pieces.reshape(frames_all, pix_piece, channels), qkv_weight, pos_bias, out_weight)
        back = lax.all_to_all(attended.reshape(piece_shape), "frame", split_axis=0, concat_axis=0, tiled=True)
        returned.append(back.reshape(half, col_count, channels))

    def joined_edge(c):
        summed = [h[:, c, :].astype(jnp.float32) + r[:, c, :].astype(jnp.float32) for h, r in zip(hidden, returned)]
        return jnp.concatenate(summed, axis=0).astype(jnp.bfloat16)

    second = convolve([hidden_rows, returned], halo(joined_edge), conv2_weight, to_bf16, 0, row_count, 6)
    return second.reshape(frames_dev, row_count, col_count, channels)


def solution(mesh):
    groups = mesh.shape["groups"]
    frames_all = mesh.shape["frame"] // 4
    split_mesh = Mesh(
        mesh.devices.reshape(groups, 4, frames_all), ("groups", "quarter", "frame")
    )
    tiles = P(("groups", "quarter", "frame"), None, None, None)
    placed = (tiles, P(), P(), P(), P(), P())
    return jax.shard_map(
        body,
        mesh=split_mesh,
        in_specs=placed,
        out_specs=tiles,
        check_vma=False,
    )
```

```python
import functools

import jax
import jax.numpy as jnp
from jax import lax
from jax.experimental import pallas as pl
from jax.experimental.pallas import tpu as pltpu
from jax.sharding import Mesh, PartitionSpec as P

HEADS = 5


def shifted(block, axis, distance):
    size = lax.axis_size(axis)
    route = [((i - distance) % size, i) for i in range(size)]
    moved = lax.ppermute(block, axis, route)
    source = lax.axis_index(axis) - distance
    inside = (source >= 0) & (source < size)
    return jnp.where(inside, moved, jnp.zeros_like(moved))


def conv_kernel(*refs, layout, lo, hi, band, finish):
    count = sum(len(segments) for segments in layout)
    flat = refs[:count]
    left_ref, right_ref, w_ref, o_ref, slab, shift_s = refs[count:]
    row_count = left_ref.shape[0]
    _, col_count, channels = o_ref.shape
    lanes = slab.shape[1] // 3
    span = band * col_count
    padded_rows = slab.shape[0]
    slab[pl.ds(0, col_count)] = jnp.zeros((col_count, slab.shape[1]), jnp.bfloat16)
    slab[pl.ds(padded_rows - col_count, col_count)] = jnp.zeros((col_count, slab.shape[1]), jnp.bfloat16)
    column = lax.broadcasted_iota(jnp.int32, (band, col_count, channels), 1)
    addends = []
    at = 0
    for segments in layout:
        addends.append(list(zip(flat[at : at + len(segments)], segments)))
        at += len(segments)

    def rows_of(ref_list, r0):
        for ref, (first, last) in ref_list:
            if first <= r0 < last:
                return ref[pl.ds(r0 - first, band)]

    for r0 in range(max(lo - band, 0), min(hi + band, row_count), band):
        block = rows_of(addends[0], r0).astype(jnp.float32)
        for extra in addends[1:]:
            block = block + rows_of(extra, r0).astype(jnp.float32)
        block = block.astype(jnp.bfloat16)
        shift_s[pl.ds(8, span)] = block.astype(jnp.float32).reshape(span, channels)
        before = shift_s[pl.ds(7, span)].reshape(band, col_count, channels)
        after = shift_s[pl.ds(9, span)].reshape(band, col_count, channels)
        rim_l = left_ref[pl.ds(r0, band)].astype(jnp.float32)[:, None, :]
        rim_r = right_ref[pl.ds(r0, band)].astype(jnp.float32)[:, None, :]
        before = jnp.where(column == 0, rim_l, before)
        after = jnp.where(column == col_count - 1, rim_r, after)
        rows = pl.ds((r0 + 1) * col_count, span)
        slab[rows, pl.ds(0, channels)] = before.reshape(span, channels).astype(jnp.bfloat16)
        slab[rows, pl.ds(lanes, channels)] = block.reshape(span, channels)
        slab[rows, pl.ds(2 * lanes, channels)] = after.reshape(span, channels).astype(jnp.bfloat16)

    for r0 in range(lo, hi, band):
        acc = None
        for a in range(3):
            rows = pl.ds((r0 + a) * col_count, span)
            term = jnp.dot(slab[rows, :], w_ref[a], preferred_element_type=jnp.float32)
            acc = term if acc is None else acc + term
        o_ref[pl.ds(r0 - lo, band)] = finish(acc).reshape(band, col_count, channels)


def norm_gelu(first):
    normed = first * lax.rsqrt(jnp.mean(first * first, axis=-1, keepdims=True) + 1e-06)
    return jax.nn.gelu(normed, approximate=True).astype(jnp.bfloat16)


def to_bf16(acc):
    return acc.astype(jnp.bfloat16)


def halo(edge_of):
    return shifted(edge_of(-1), "quarter", 1), shifted(edge_of(0), "quarter", -1)


def convolve(groups, rims, weight, finish, lo, hi, band=12):
    row_count, channels = rims[0].shape
    col_count = groups[0][0].shape[1]
    layout = []
    for segments in groups:
        spans = []
        first = 0
        for piece in segments:
            spans.append((first, first + piece.shape[0]))
            first += piece.shape[0]
        layout.append(tuple(spans))
    flat = [piece for segments in groups for piece in segments]
    vmem = pl.BlockSpec(memory_space=pltpu.VMEM)
    padded = (row_count + 2) * col_count
    stacked = weight.reshape(3, 3 * channels, channels)
    return pl.pallas_call(
        functools.partial(conv_kernel, layout=tuple(layout), lo=lo, hi=hi, band=band, finish=finish),
        out_shape=jax.ShapeDtypeStruct((hi - lo, col_count, channels), jnp.bfloat16),
        in_specs=[vmem] * (len(flat) + 3),
        out_specs=vmem,
        scratch_shapes=[
            pltpu.VMEM((padded, 3 * channels), jnp.bfloat16),
            pltpu.VMEM((band * col_count + 16, channels), jnp.float32),
        ],
    )(*flat, *rims, stacked)


def attend_kernel(*refs, parts):
    if parts:
        x_refs = refs[:parts]
        wqkv_ref, bias_ref, wout_ref = refs[parts : parts + 3]
        o_refs = refs[parts + 3 : 2 * parts + 3]
        qkv_s, blend_s = refs[2 * parts + 3 :]
        frames_all, _, count = qkv_s.shape
        channels = wout_ref.shape[0]
        for f in range(parts):
            qkv_s[f] = lax.dot_general(
                wqkv_ref[...],
                x_refs[f][...].reshape(count, channels),
                (((1,), (1,)), ((), ())),
                preferred_element_type=jnp.float32,
            ).astype(jnp.bfloat16)
    else:
        x_ref, wqkv_ref, bias_ref, wout_ref, o_ref, qkv_s, blend_s = refs
        frames_all, count, channels = x_ref.shape

        def project(f, carry):
            qkv_s[f] = lax.dot_general(
                wqkv_ref[...], x_ref[f], (((1,), (1,)), ((), ())), preferred_element_type=jnp.float32
            ).astype(jnp.bfloat16)
            return carry

        lax.fori_loop(0, frames_all, project, 0, unroll=frames_all <= 4)
    head_dim = channels // HEADS
    scale = head_dim ** (-0.5)
    block = min(frames_all, 4)

    def head_block(h, first):
        frames = pl.ds(first, block)
        queries = qkv_s[frames, pl.ds(h * head_dim, head_dim), :].astype(jnp.float32)
        scores = []
        for g in range(frames_all):
            key_part = qkv_s[g, pl.ds(channels + h * head_dim, head_dim), :].astype(jnp.float32)
            bias = bias_ref[h, g, frames]
            scores.append(jnp.sum(queries * key_part[None], axis=1) * scale + bias)
        top = scores[0]
        for g in range(1, frames_all):
            top = jnp.maximum(top, scores[g])
        weights = [jnp.exp(s - top) for s in scores]
        total = weights[0]
        for g in range(1, frames_all):
            total = total + weights[g]
        blended = None
        for g in range(frames_all):
            value_part = qkv_s[g, pl.ds(2 * channels + h * head_dim, head_dim), :].astype(jnp.float32)
            prob = (weights[g] / total).astype(jnp.bfloat16).astype(jnp.float32)
            term = prob[:, None, :] * value_part[None]
            blended = term if blended is None else blended + term
        blend_s[frames, pl.ds(h * head_dim, head_dim), :] = blended.astype(jnp.bfloat16)

    def frame_block(i, carry):
        for h in range(HEADS):
            head_block(h, i * block)
        return carry

    lax.fori_loop(0, frames_all // block, frame_block, 0, unroll=frames_all <= 4)

    def out_product(f):
        return lax.dot_general(
            blend_s[f], wout_ref[...], (((0,), (0,)), ((), ())), preferred_element_type=jnp.float32
        ).astype(jnp.bfloat16)

    if parts:
        for f in range(parts):
            o_refs[f][...] = out_product(f).reshape(o_refs[f].shape)
        return

    def out_project(f, carry):
        o_ref[f] = out_product(f)
        return carry

    lax.fori_loop(0, frames_all, out_project, 0, unroll=frames_all <= 4)


def attend_pieces(pieces, qkv_weight, pos_bias, out_weight):
    frames_all = len(pieces)
    band, col_count, channels = pieces[0].shape
    count = band * col_count
    vmem = pl.BlockSpec(memory_space=pltpu.VMEM)
    return pl.pallas_call(
        functools.partial(attend_kernel, parts=frames_all),
        out_shape=tuple(jax.ShapeDtypeStruct(pieces[0].shape, jnp.bfloat16) for _ in pieces),
        in_specs=[vmem] * (frames_all + 3),
        out_specs=tuple(vmem for _ in pieces),
        scratch_shapes=[
            pltpu.VMEM((frames_all, 3 * channels, count), jnp.bfloat16),
            pltpu.VMEM((frames_all, channels, count), jnp.bfloat16),
        ],
    )(*pieces, qkv_weight.T, pos_bias.transpose(0, 2, 1)[..., None], out_weight)


def attend(grid, qkv_weight, pos_bias, out_weight):
    frames_all, count, channels = grid.shape
    vmem = pl.BlockSpec(memory_space=pltpu.VMEM)
    return pl.pallas_call(
        functools.partial(attend_kernel, parts=0),
        out_shape=jax.ShapeDtypeStruct((frames_all, count, channels), jnp.bfloat16),
        in_specs=[vmem] * 4,
        out_specs=vmem,
        scratch_shapes=[
            pltpu.VMEM((frames_all, 3 * channels, count), jnp.bfloat16),
            pltpu.VMEM((frames_all, channels, count), jnp.bfloat16),
        ],
    )(grid, qkv_weight.T, pos_bias.transpose(0, 2, 1)[..., None], out_weight)


def rotated_attention(source, lo, rows, qkv_weight, pos_bias, out_weight):
    frames_all = lax.axis_size("frame")
    me = lax.axis_index("frame")
    _, col_count, channels = source.shape
    band = rows // frames_all
    got = []
    for s in range(frames_all):
        piece = lax.dynamic_slice_in_dim(source, lo + ((me + s) % frames_all) * band, band, axis=0)
        if s:
            piece = lax.ppermute(piece, "frame", [(i, (i + s) % frames_all) for i in range(frames_all)])
        got.append(piece)
    source = (me - jnp.arange(frames_all)) % frames_all
    bias = jnp.take(jnp.take(pos_bias, source, axis=1), source, axis=2)
    attended = attend_pieces(got, qkv_weight, bias, out_weight)
    back = []
    for s in range(frames_all):
        piece = attended[s]
        if s:
            piece = lax.ppermute(piece, "frame", [(i, (i - s) % frames_all) for i in range(frames_all)])
        back.append(piece)
    order = (jnp.arange(frames_all) - me) % frames_all
    return jnp.take(jnp.stack(back), order, axis=0).reshape(rows, col_count, channels)


def body(latents, conv1_weight, qkv_weight, out_weight, pos_bias, conv2_weight):
    frames_dev, row_count, col_count, channels = latents.shape
    frames_all = lax.axis_size("frame")
    tile = latents.reshape(row_count, col_count, channels)
    def tile_edge(c):
        pick = (jnp.arange(col_count) == c % col_count).astype(tile.dtype)
        return jnp.einsum("rwc,w->rc", tile, pick, preferred_element_type=jnp.float32).astype(tile.dtype)

    rims = halo(tile_edge)
    half = row_count // 2
    returned = []
    rotate = frames_all <= 4 and half % frames_all == 0
    if rotate:
        whole = convolve([[tile]], rims, conv1_weight, norm_gelu, 0, row_count)
        for lo in (0, half):
            returned.append(rotated_attention(whole, lo, half, qkv_weight, pos_bias, out_weight))
        hidden_rows = [whole]
        hidden = [whole[:half], whole[half:]]
    else:
        hidden = [convolve([[tile]], rims, conv1_weight, norm_gelu, lo, lo + half) for lo in (0, half)]
        hidden_rows = hidden
    pix_piece = half * col_count // frames_all
    if half % frames_all == 0:
        piece_shape = (frames_all, half // frames_all, col_count, channels)
    else:
        piece_shape = (frames_all, pix_piece, channels)
    for part in hidden:
        if rotate:
            break
        pieces = lax.all_to_all(part.reshape(piece_shape), "frame", split_axis=0, concat_axis=0, tiled=True)
        attended = attend(pieces.reshape(frames_all, pix_piece, channels), qkv_weight, pos_bias, out_weight)
        back = lax.all_to_all(attended.reshape(piece_shape), "frame", split_axis=0, concat_axis=0, tiled=True)
        returned.append(back.reshape(half, col_count, channels))

    def joined_edge(c):
        summed = [h[:, c, :].astype(jnp.float32) + r[:, c, :].astype(jnp.float32) for h, r in zip(hidden, returned)]
        return jnp.concatenate(summed, axis=0).astype(jnp.bfloat16)

    second = convolve([hidden_rows, returned], halo(joined_edge), conv2_weight, to_bf16, 0, row_count, 4)
    return second.reshape(frames_dev, row_count, col_count, channels)


def solution(mesh):
    groups = mesh.shape["groups"]
    frames_all = mesh.shape["frame"] // 4
    split_mesh = Mesh(
        mesh.devices.reshape(groups, 4, frames_all), ("groups", "quarter", "frame")
    )
    tiles = P(("groups", "quarter", "frame"), None, None, None)
    placed = (tiles, P(), P(), P(), P(), P())
    return jax.shard_map(
        body,
        mesh=split_mesh,
        in_specs=placed,
        out_specs=tiles,
        check_vma=False,
    )
```

```python
import functools

import jax
import jax.numpy as jnp
from jax import lax
from jax.experimental import pallas as pl
from jax.experimental.pallas import tpu as pltpu
from jax.sharding import Mesh, PartitionSpec as P

HEADS = 5


def shifted(block, axis, distance):
    size = lax.axis_size(axis)
    route = [((i - distance) % size, i) for i in range(size)]
    moved = lax.ppermute(block, axis, route)
    source = lax.axis_index(axis) - distance
    inside = (source >= 0) & (source < size)
    return jnp.where(inside, moved, jnp.zeros_like(moved))


def conv_kernel(*refs, layout, lo, hi, band, finish):
    count = sum(len(segments) for segments in layout)
    flat = refs[:count]
    left_ref, right_ref, w_ref, o_ref, slab, shift_s = refs[count:]
    row_count = left_ref.shape[0]
    _, col_count, channels = o_ref.shape
    lanes = slab.shape[1] // 3
    span = band * col_count
    padded_rows = slab.shape[0]
    slab[pl.ds(0, col_count)] = jnp.zeros((col_count, slab.shape[1]), jnp.bfloat16)
    slab[pl.ds(padded_rows - col_count, col_count)] = jnp.zeros((col_count, slab.shape[1]), jnp.bfloat16)
    column = lax.broadcasted_iota(jnp.int32, (band, col_count, channels), 1)
    addends = []
    at = 0
    for segments in layout:
        addends.append(list(zip(flat[at : at + len(segments)], segments)))
        at += len(segments)

    def rows_of(ref_list, r0):
        for ref, (first, last) in ref_list:
            if first <= r0 < last:
                return ref[pl.ds(r0 - first, band)]

    for r0 in range(max(lo - band, 0), min(hi + band, row_count), band):
        block = rows_of(addends[0], r0).astype(jnp.float32)
        for extra in addends[1:]:
            block = block + rows_of(extra, r0).astype(jnp.float32)
        block = block.astype(jnp.bfloat16)
        shift_s[pl.ds(8, span)] = block.astype(jnp.float32).reshape(span, channels)
        before = shift_s[pl.ds(7, span)].reshape(band, col_count, channels)
        after = shift_s[pl.ds(9, span)].reshape(band, col_count, channels)
        rim_l = left_ref[pl.ds(r0, band)].astype(jnp.float32)[:, None, :]
        rim_r = right_ref[pl.ds(r0, band)].astype(jnp.float32)[:, None, :]
        before = jnp.where(column == 0, rim_l, before)
        after = jnp.where(column == col_count - 1, rim_r, after)
        rows = pl.ds((r0 + 1) * col_count, span)
        slab[rows, pl.ds(0, channels)] = before.reshape(span, channels).astype(jnp.bfloat16)
        slab[rows, pl.ds(lanes, channels)] = block.reshape(span, channels)
        slab[rows, pl.ds(2 * lanes, channels)] = after.reshape(span, channels).astype(jnp.bfloat16)

    for r0 in range(lo, hi, band):
        acc = None
        for a in range(3):
            rows = pl.ds((r0 + a) * col_count, span)
            term = jnp.dot(slab[rows, :], w_ref[a], preferred_element_type=jnp.float32)
            acc = term if acc is None else acc + term
        o_ref[pl.ds(r0 - lo, band)] = finish(acc).reshape(band, col_count, channels)


def norm_gelu(first):
    normed = first * lax.rsqrt(jnp.mean(first * first, axis=-1, keepdims=True) + 1e-06)
    return jax.nn.gelu(normed, approximate=True).astype(jnp.bfloat16)


def to_bf16(acc):
    return acc.astype(jnp.bfloat16)


def halo(edge_of):
    return shifted(edge_of(-1), "quarter", 1), shifted(edge_of(0), "quarter", -1)


def convolve(groups, rims, weight, finish, lo, hi, band=12):
    row_count, channels = rims[0].shape
    col_count = groups[0][0].shape[1]
    layout = []
    for segments in groups:
        spans = []
        first = 0
        for piece in segments:
            spans.append((first, first + piece.shape[0]))
            first += piece.shape[0]
        layout.append(tuple(spans))
    flat = [piece for segments in groups for piece in segments]
    vmem = pl.BlockSpec(memory_space=pltpu.VMEM)
    padded = (row_count + 2) * col_count
    stacked = weight.reshape(3, 3 * channels, channels)
    return pl.pallas_call(
        functools.partial(conv_kernel, layout=tuple(layout), lo=lo, hi=hi, band=band, finish=finish),
        out_shape=jax.ShapeDtypeStruct((hi - lo, col_count, channels), jnp.bfloat16),
        in_specs=[vmem] * (len(flat) + 3),
        out_specs=vmem,
        scratch_shapes=[
            pltpu.VMEM((padded, 3 * channels), jnp.bfloat16),
            pltpu.VMEM((band * col_count + 16, channels), jnp.float32),
        ],
    )(*flat, *rims, stacked)


def attend_kernel(*refs, parts):
    if parts:
        x_refs = refs[:parts]
        wqkv_ref, bias_ref, wout_ref = refs[parts : parts + 3]
        o_refs = refs[parts + 3 : 2 * parts + 3]
        qkv_s, blend_s = refs[2 * parts + 3 :]
        frames_all, _, count = qkv_s.shape
        channels = wout_ref.shape[0]
        for f in range(parts):
            qkv_s[f] = lax.dot_general(
                wqkv_ref[...],
                x_refs[f][...].reshape(count, channels),
                (((1,), (1,)), ((), ())),
                preferred_element_type=jnp.float32,
            ).astype(jnp.bfloat16)
    else:
        x_ref, wqkv_ref, bias_ref, wout_ref, o_ref, qkv_s, blend_s = refs
        frames_all, count, channels = x_ref.shape

        def project(f, carry):
            qkv_s[f] = lax.dot_general(
                wqkv_ref[...], x_ref[f], (((1,), (1,)), ((), ())), preferred_element_type=jnp.float32
            ).astype(jnp.bfloat16)
            return carry

        lax.fori_loop(0, frames_all, project, 0, unroll=frames_all <= 4)
    head_dim = channels // HEADS
    scale = head_dim ** (-0.5)
    block = min(frames_all, 4)

    def head_block(h, first):
        frames = pl.ds(first, block)
        queries = qkv_s[frames, pl.ds(h * head_dim, head_dim), :].astype(jnp.float32)
        scores = []
        for g in range(frames_all):
            key_part = qkv_s[g, pl.ds(channels + h * head_dim, head_dim), :].astype(jnp.float32)
            bias = bias_ref[h, g, frames]
            scores.append(jnp.sum(queries * key_part[None], axis=1) * scale + bias)
        top = scores[0]
        for g in range(1, frames_all):
            top = jnp.maximum(top, scores[g])
        weights = [jnp.exp(s - top) for s in scores]
        total = weights[0]
        for g in range(1, frames_all):
            total = total + weights[g]
        blended = None
        for g in range(frames_all):
            value_part = qkv_s[g, pl.ds(2 * channels + h * head_dim, head_dim), :].astype(jnp.float32)
            prob = (weights[g] / total).astype(jnp.bfloat16).astype(jnp.float32)
            term = prob[:, None, :] * value_part[None]
            blended = term if blended is None else blended + term
        blend_s[frames, pl.ds(h * head_dim, head_dim), :] = blended.astype(jnp.bfloat16)

    def frame_block(i, carry):
        for h in range(HEADS):
            head_block(h, i * block)
        return carry

    lax.fori_loop(0, frames_all // block, frame_block, 0, unroll=frames_all <= 4)

    def out_product(f):
        return lax.dot_general(
            blend_s[f], wout_ref[...], (((0,), (0,)), ((), ())), preferred_element_type=jnp.float32
        ).astype(jnp.bfloat16)

    if parts:
        for f in range(parts):
            o_refs[f][...] = out_product(f).reshape(o_refs[f].shape)
        return

    def out_project(f, carry):
        o_ref[f] = out_product(f)
        return carry

    lax.fori_loop(0, frames_all, out_project, 0, unroll=frames_all <= 4)


def attend_pieces(pieces, qkv_weight, pos_bias, out_weight):
    frames_all = len(pieces)
    band, col_count, channels = pieces[0].shape
    count = band * col_count
    vmem = pl.BlockSpec(memory_space=pltpu.VMEM)
    return pl.pallas_call(
        functools.partial(attend_kernel, parts=frames_all),
        out_shape=tuple(jax.ShapeDtypeStruct(pieces[0].shape, jnp.bfloat16) for _ in pieces),
        in_specs=[vmem] * (frames_all + 3),
        out_specs=tuple(vmem for _ in pieces),
        scratch_shapes=[
            pltpu.VMEM((frames_all, 3 * channels, count), jnp.bfloat16),
            pltpu.VMEM((frames_all, channels, count), jnp.bfloat16),
        ],
    )(*pieces, qkv_weight.T, pos_bias.transpose(0, 2, 1)[..., None], out_weight)


def attend(grid, qkv_weight, pos_bias, out_weight):
    frames_all, count, channels = grid.shape
    vmem = pl.BlockSpec(memory_space=pltpu.VMEM)
    return pl.pallas_call(
        functools.partial(attend_kernel, parts=0),
        out_shape=jax.ShapeDtypeStruct((frames_all, count, channels), jnp.bfloat16),
        in_specs=[vmem] * 4,
        out_specs=vmem,
        scratch_shapes=[
            pltpu.VMEM((frames_all, 3 * channels, count), jnp.bfloat16),
            pltpu.VMEM((frames_all, channels, count), jnp.bfloat16),
        ],
    )(grid, qkv_weight.T, pos_bias.transpose(0, 2, 1)[..., None], out_weight)


def rotated_attention(source, lo, rows, qkv_weight, pos_bias, out_weight):
    frames_all = lax.axis_size("frame")
    me = lax.axis_index("frame")
    _, col_count, channels = source.shape
    band = rows // frames_all
    got = []
    for s in range(frames_all):
        piece = lax.dynamic_slice_in_dim(source, lo + ((me + s) % frames_all) * band, band, axis=0)
        if s:
            piece = lax.ppermute(piece, "frame", [(i, (i + s) % frames_all) for i in range(frames_all)])
        got.append(piece)
    source = (me - jnp.arange(frames_all)) % frames_all
    bias = jnp.take(jnp.take(pos_bias, source, axis=1), source, axis=2)
    attended = attend_pieces(got, qkv_weight, bias, out_weight)
    back = []
    for s in range(frames_all):
        piece = attended[s]
        if s:
            piece = lax.ppermute(piece, "frame", [(i, (i - s) % frames_all) for i in range(frames_all)])
        back.append(piece)
    order = (jnp.arange(frames_all) - me) % frames_all
    return jnp.take(jnp.stack(back), order, axis=0).reshape(rows, col_count, channels)


def body(latents, conv1_weight, qkv_weight, out_weight, pos_bias, conv2_weight):
    frames_dev, row_count, col_count, channels = latents.shape
    frames_all = lax.axis_size("frame")
    tile = latents.reshape(row_count, col_count, channels)
    def tile_edge(c):
        pick = (jnp.arange(col_count) == c % col_count).astype(tile.dtype)
        return jnp.einsum("rwc,w->rc", tile, pick, preferred_element_type=jnp.float32).astype(tile.dtype)

    rims = halo(tile_edge)
    half = row_count // 2
    returned = []
    rotate = frames_all <= 4 and half % frames_all == 0
    if rotate:
        whole = convolve([[tile]], rims, conv1_weight, norm_gelu, 0, row_count, 18)
        for lo in (0, half):
            returned.append(rotated_attention(whole, lo, half, qkv_weight, pos_bias, out_weight))
        hidden_rows = [whole]
        hidden = [whole[:half], whole[half:]]
    else:
        hidden = [convolve([[tile]], rims, conv1_weight, norm_gelu, lo, lo + half) for lo in (0, half)]
        hidden_rows = hidden
    pix_piece = half * col_count // frames_all
    if half % frames_all == 0:
        piece_shape = (frames_all, half // frames_all, col_count, channels)
    else:
        piece_shape = (frames_all, pix_piece, channels)
    for part in hidden:
        if rotate:
            break
        pieces = lax.all_to_all(part.reshape(piece_shape), "frame", split_axis=0, concat_axis=0, tiled=True)
        attended = attend(pieces.reshape(frames_all, pix_piece, channels), qkv_weight, pos_bias, out_weight)
        back = lax.all_to_all(attended.reshape(piece_shape), "frame", split_axis=0, concat_axis=0, tiled=True)
        returned.append(back.reshape(half, col_count, channels))

    def joined_edge(c):
        summed = [h[:, c, :].astype(jnp.float32) + r[:, c, :].astype(jnp.float32) for h, r in zip(hidden, returned)]
        return jnp.concatenate(summed, axis=0).astype(jnp.bfloat16)

    second = convolve([hidden_rows, returned], halo(joined_edge), conv2_weight, to_bf16, 0, row_count, 6)
    return second.reshape(frames_dev, row_count, col_count, channels)


def solution(mesh):
    groups = mesh.shape["groups"]
    frames_all = mesh.shape["frame"] // 4
    split_mesh = Mesh(
        mesh.devices.reshape(groups, 4, frames_all), ("groups", "quarter", "frame")
    )
    tiles = P(("groups", "quarter", "frame"), None, None, None)
    placed = (tiles, P(), P(), P(), P(), P())
    return jax.shard_map(
        body,
        mesh=split_mesh,
        in_specs=placed,
        out_specs=tiles,
        check_vma=False,
    )
```
